32 devices in a mesh: rows: 8 (over z, x), cols: 4 (over y, core).
Axes of the slice: x: 2, y: 2, z: 4, core: 2. Of those that a mesh axis runs over, the one named last changes fastest.
Arguments:
- probes: float32 [64, 128, 512], P(None, 'rows', 'cols'), may hold values from -6 to 6
- observed: float32 [128, 512], P('rows', 'cols'), may hold values from -1.8 to 1.8
- kappa_sq: float32 [128, 512], P('rows', 'cols'), may hold values from 0.01 to 1
- variance_weight: float32 [128, 512], P('rows', 'cols'), may hold values from 0.25 to 10
Outputs:
- grad_kappa: float32 [128, 512], P('rows', 'cols')
- grad_weight: float32 [128, 512], P('rows', 'cols')
The draws below stay inside these ranges and needn't reach their ends.
All inputs are finite; a program needn't handle non-finite values.
Results may differ from the reference program's by a relative error of at most 0.0001.
Values sent between devices are 32-bit elements; how exact they have to be, the bound alone decides.
No kernel may reach another device: no remote copies, remote signals or barrier semaphores. Data moves between devices by JAX's collectives and lax.ppermute only.
A program may use at most 64 MiB of HBM per device.

```python
import math
import jax
import jax.numpy as jnp
from jax import lax

PROBES = 64
ITERS = 3
NR = 128
NC = 512


def draw_variance_weight(key, part):
    row_frac = jnp.arange(NR, dtype=jnp.float32)[:, None] / (NR - 1)
    row_trend = jnp.exp(math.log(3.0) * row_frac)
    jitter = jax.random.uniform(key, (NR, NC), jnp.float32, math.log(0.5), math.log(2.0))
    return (row_trend * jnp.exp(jitter)).astype(jnp.float32)


def steps_of(key, dims, cuts, least, high):
    def one(position, parts):
        steps = jax.random.uniform(jax.random.fold_in(jax.random.fold_in(key, 6), position), (parts,), jnp.float32, least / len(cuts), high / len(cuts))
        return jnp.repeat(jnp.exp(steps), dims[position] // parts).reshape((-1,) + (1,) * (len(dims) - position - 1))

    gain = one(*cuts[0])
    for cut in cuts[1:]:
        gain = gain * one(*cut)
    return gain


def bell_draw(own_key, extent, deviation, limit, cuts=(), kind=jnp.bfloat16):
    loudness = steps_of(own_key, extent, cuts, -0.22, 0.18) if cuts else 1.0
    drawn = jax.random.normal(own_key, extent, jnp.float32) * deviation * loudness
    return jnp.minimum(jnp.maximum(drawn, -limit), limit).astype(kind)


def setup_inputs(seed: int = 0) -> dict:
    key_list = jax.random.split(jax.random.key(seed), 5)
    probes = bell_draw(key_list[0], (PROBES, NR, NC), 1.0, 6.0, ((1, 8), (2, 4)), jnp.float32)
    observed = bell_draw(key_list[1], (NR, NC), 0.3, 1.8, ((0, 8), (1, 4)), jnp.float32)
    kappa_sq = jnp.clip(jnp.exp(math.log(1.0) - 4.6051702 * jax.random.uniform(key_list[2], (NR, NC), jnp.float32) ** steps_of(key_list[2], (NR, NC), ((0, 8), (1, 4)), -0.2, 0.2)), 0.01, 1.0)
    variance_weight = draw_variance_weight(jax.random.fold_in(key_list[4], 71), 0)
    return dict(probes=probes, observed=observed, kappa_sq=kappa_sq, variance_weight=variance_weight)


def stencil(padded, kappa_sq):
    centre = padded[..., 1:-1, 1:-1]
    edge_sum = padded[..., :-2, 1:-1] + padded[..., 2:, 1:-1] + padded[..., 1:-1, :-2] + padded[..., 1:-1, 2:]
    corners = padded[..., :-2, :-2] + padded[..., :-2, 2:] + padded[..., 2:, :-2] + padded[..., 2:, 2:]
    return (kappa_sq + 20.0 / 6.0) * centre - (4.0 * edge_sum + corners) / 6.0


def stiffen(field, kappa_sq):
    return stencil(jnp.pad(field, ((1, 1), (1, 1))), kappa_sq)


def solve_one(one_probe, kappa_sq, variance_weight):
    residual = one_probe
    direction = one_probe
    solution = jnp.zeros_like(one_probe)
    norm_now = jnp.sum(residual * residual)
    stiff_probe = None
    for iteration in range(ITERS):
        stiffness = stiffen(direction, kappa_sq)
        if iteration == 0:
            stiff_probe = stiffness
        applied = stiffen(variance_weight * stiffness, kappa_sq)
        step_len = norm_now / jnp.sum(direction * applied)
        solution = solution + step_len * direction
        residual = residual - step_len * applied
        norm_next = jnp.sum(residual * residual)
        direction = residual + (norm_next / norm_now) * direction
        norm_now = norm_next
    return solution, stiff_probe


def reference(probes, observed, kappa_sq, variance_weight):
    def accumulate(totals, one_probe):
        solution, stiff_probe = solve_one(one_probe, kappa_sq, variance_weight)
        stiff_solution = stiffen(solution, kappa_sq)
        weight_total = totals[0] + stiff_solution * stiff_probe
        kappa_total = totals[1] + (solution * stiff_probe + stiff_solution * one_probe)
        return (weight_total, kappa_total), None

    zeros_field = jnp.zeros(observed.shape, jnp.float32)
    (weight_total, kappa_total), _ = lax.scan(accumulate, (zeros_field, zeros_field), probes)
    stiff_obs = stiffen(observed, kappa_sq)
    grad_weight = 0.5 * weight_total / PROBES - 0.5 * stiff_obs * stiff_obs
    grad_kappa = 0.5 * variance_weight * (kappa_total / PROBES) - observed * variance_weight * stiff_obs
    return grad_kappa, grad_weight
```

```python
import jax
import jax.numpy as jnp
from jax import lax
from jax.sharding import PartitionSpec as P

ITERS = 3
HALO = 2 * ITERS


def extended(cells, sides, width):
    for axis, dim in sides:
        count = lax.axis_size(axis)
        ends = count - 1
        head = lax.slice_in_dim(cells, 0, width, axis=dim)
        tail = lax.slice_in_dim(cells, cells.shape[dim] - width, cells.shape[dim], axis=dim)
        cells = jnp.concatenate(
            [
                lax.ppermute(tail, axis, [(i, (i + 1) % count) for i in range(ends)]),
                cells,
                lax.ppermute(head, axis, [((i + 1) % count, i) for i in range(ends)]),
            ],
            axis=dim,
        )
    return cells


def stencil(padded, kappa_sq):
    centre = padded[..., 1:-1, 1:-1]
    edge_sum = (
        padded[..., :-2, 1:-1]
        + padded[..., 2:, 1:-1]
        + padded[..., 1:-1, :-2]
        + padded[..., 1:-1, 2:]
    )
    corners = (
        padded[..., :-2, :-2] + padded[..., :-2, 2:] + padded[..., 2:, :-2] + padded[..., 2:, 2:]
    )
    return (kappa_sq + 20.0 / 6.0) * centre - (4.0 * edge_sum + corners) / 6.0


def stiffen(field, kappa_sq):
    pads = ((0, 0),) * (field.ndim - 2) + ((1, 1), (1, 1))
    return stencil(jnp.pad(field, pads), kappa_sq)


def all_sum(terms):
    for axis in ("cols", "rows"):
        count = lax.axis_size(axis)
        if count & (count - 1):
            terms = lax.psum(terms, axis)
            continue
        hop = 1
        while hop < count:
            terms = terms + lax.ppermute(terms, axis, [(i, i ^ hop) for i in range(count)])
            hop *= 2
    return terms


def inside_mask(rows, cols):
    row_at = lax.axis_index("rows") * rows - HALO + lax.iota(jnp.int32, rows + 2 * HALO)
    col_at = lax.axis_index("cols") * cols - HALO + lax.iota(jnp.int32, cols + 2 * HALO)
    row_in = (row_at >= 0) & (row_at < rows * lax.axis_size("rows"))
    col_in = (col_at >= 0) & (col_at < cols * lax.axis_size("cols"))
    return (row_in[:, None] & col_in[None, :]).astype(jnp.float32)


def on_device(probes, observed, kappa_sq, variance_weight):
    probe_count, rows, cols = probes.shape
    stacked = jnp.concatenate(
        [probes, observed[None], kappa_sq[None], variance_weight[None]], axis=0
    )
    ext = extended(stacked, (("rows", 1), ("cols", 2)), HALO)
    probe_ext = ext[:probe_count]
    observed_ext = ext[probe_count]
    kappa_ext = ext[probe_count + 1]
    weight_ext = ext[probe_count + 2]
    mask = inside_mask(rows, cols)

    def inner(field):
        return field[..., HALO : HALO + rows, HALO : HALO + cols]

    def dot(first, second):
        return jnp.sum(inner(first) * inner(second), axis=(-2, -1))

    def apply_q(direction):
        stiffness = stiffen(direction, kappa_ext)
        applied = mask * stiffen(weight_ext * stiffness, kappa_ext)
        return stiffness, applied

    residual = probe_ext
    direction = probe_ext
    solution = None
    stiff_probe, applied = apply_q(direction)
    first = all_sum(jnp.stack([dot(residual, residual), dot(direction, applied)]))
    norm_now = first[0]
    curvature = first[1]
    for iteration in range(ITERS):
        if iteration > 0:
            _, applied = apply_q(direction)
            curvature = all_sum(dot(direction, applied))
        step_len = (norm_now / curvature)[:, None, None]
        solution = step_len * direction if solution is None else solution + step_len * direction
        if iteration + 1 < ITERS:
            residual = residual - step_len * applied
            norm_next = all_sum(dot(residual, residual))
            direction = residual + (norm_next / norm_now)[:, None, None] * direction
            norm_now = norm_next

    stiff_solution = inner(stiffen(solution, kappa_ext))
    stiff_obs = inner(stiffen(observed_ext, kappa_ext))
    stiff_probe = inner(stiff_probe)
    solution = inner(solution)
    weight_total = jnp.sum(stiff_solution * stiff_probe, axis=0)
    kappa_total = jnp.sum(solution * stiff_probe + stiff_solution * probes, axis=0)
    grad_weight = 0.5 * weight_total / probe_count - 0.5 * stiff_obs * stiff_obs
    grad_kappa = (
        0.5 * variance_weight * (kappa_total / probe_count) - observed * variance_weight * stiff_obs
    )
    return (grad_kappa, grad_weight)


def solution(mesh):
    placed = (P(None, "rows", "cols"), P("rows", "cols"), P("rows", "cols"), P("rows", "cols"))
    return jax.shard_map(
        on_device,
        mesh=mesh,
        in_specs=placed,
        out_specs=(P("rows", "cols"), P("rows", "cols")),
        check_vma=False,
    )
```

```python
import functools

import jax
import jax.numpy as jnp
from jax import lax
from jax.experimental import pallas as pl
from jax.experimental.pallas import tpu as pltpu
from jax.sharding import PartitionSpec as P

ITERS = 3
HALO = 2 * ITERS
BLOCK = 8


def extended(cells, sides, width):
    for axis, dim in sides:
        count = lax.axis_size(axis)
        ends = count - 1
        head = lax.slice_in_dim(cells, 0, width, axis=dim)
        tail = lax.slice_in_dim(cells, cells.shape[dim] - width, cells.shape[dim], axis=dim)
        cells = jnp.concatenate(
            [
                lax.ppermute(tail, axis, [(i, (i + 1) % count) for i in range(ends)]),
                cells,
                lax.ppermute(head, axis, [((i + 1) % count, i) for i in range(ends)]),
            ],
            axis=dim,
        )
    return cells


def stencil(padded, kappa_sq):
    centre = padded[..., 1:-1, 1:-1]
    edge_sum = (
        padded[..., :-2, 1:-1]
        + padded[..., 2:, 1:-1]
        + padded[..., 1:-1, :-2]
        + padded[..., 1:-1, 2:]
    )
    corners = (
        padded[..., :-2, :-2] + padded[..., :-2, 2:] + padded[..., 2:, :-2] + padded[..., 2:, 2:]
    )
    return (kappa_sq + 20.0 / 6.0) * centre - (4.0 * edge_sum + corners) / 6.0


def stiffen(field, kappa_sq):
    pads = ((0, 0),) * (field.ndim - 2) + ((1, 1), (1, 1))
    return stencil(jnp.pad(field, pads), kappa_sq)


def all_sum(terms):
    for axis in ("cols", "rows"):
        count = lax.axis_size(axis)
        if count & (count - 1):
            terms = lax.psum(terms, axis)
            continue
        hop = 1
        while hop < count:
            terms = terms + lax.ppermute(terms, axis, [(i, i ^ hop) for i in range(count)])
            hop *= 2
    return terms


def _roll(value, shift, axis):
    return pltpu.roll(value, shift % value.shape[axis], axis)


def _stiffen_slab(value, centre_gain):
    vertical = _roll(value, 1, 0) + _roll(value, -1, 0)
    edge_sum = vertical + _roll(value, 1, 1) + _roll(value, -1, 1)
    corners = _roll(vertical, 1, 1) + _roll(vertical, -1, 1)
    return centre_gain * value - (4.0 * edge_sum + corners) / 6.0


def _lane_sum(value, keep):
    rows = jnp.sum(jnp.where(keep, value, 0.0), axis=0, keepdims=True)
    lanes = value.shape[1]
    total = rows[:, :128]
    for start in range(128, lanes, 128):
        total = total + rows[:, start : start + 128]
    return total


def _first_kernel(z_ref, gain_ref, weight_ref, inside_ref, inner_ref,
                  stiff_ref, applied_ref, zz_ref, za_ref):
    def body(i, carry):
        gain = gain_ref[...]
        z = z_ref[i]
        stiffness = _stiffen_slab(z, gain)
        applied = _stiffen_slab(weight_ref[...] * stiffness, gain)
        applied = jnp.where(inside_ref[...] > 0.5, applied, 0.0)
        stiff_ref[i] = stiffness
        applied_ref[i] = applied
        keep = inner_ref[...] > 0.5
        zz_ref[pl.ds(i, 1), :] = _lane_sum(z * z, keep)
        za_ref[pl.ds(i, 1), :] = _lane_sum(z * applied, keep)
        return carry

    lax.fori_loop(0, BLOCK, body, 0)


def _start_kernel(step_ref, z_ref, applied_ref, inner_ref, solution_ref, residual_ref, rr_ref):
    base = pl.program_id(0) * BLOCK

    def body(i, carry):
        step = step_ref[base + i]
        z = z_ref[i]
        residual = z - step * applied_ref[i]
        solution_ref[i] = step * z
        residual_ref[i] = residual
        rr_ref[pl.ds(i, 1), :] = _lane_sum(residual * residual, inner_ref[...] > 0.5)
        return carry

    lax.fori_loop(0, BLOCK, body, 0)


def _update_kernel(step_ref, solution_ref, direction_ref, residual_ref, applied_ref, inner_ref,
                   solution_out, residual_out, rr_ref):
    base = pl.program_id(0) * BLOCK

    def body(i, carry):
        step = step_ref[base + i]
        residual = residual_ref[i] - step * applied_ref[i]
        solution_out[i] = solution_ref[i] + step * direction_ref[i]
        residual_out[i] = residual
        rr_ref[pl.ds(i, 1), :] = _lane_sum(residual * residual, inner_ref[...] > 0.5)
        return carry

    lax.fori_loop(0, BLOCK, body, 0)


def _direction_kernel(beta_ref, residual_ref, direction_ref, gain_ref, weight_ref, inside_ref,
                      inner_ref, direction_out, applied_out, pa_ref):
    base = pl.program_id(0) * BLOCK

    def body(i, carry):
        beta = beta_ref[base + i]
        direction = residual_ref[i] + beta * direction_ref[i]
        gain = gain_ref[...]
        stiffness = _stiffen_slab(direction, gain)
        applied = _stiffen_slab(weight_ref[...] * stiffness, gain)
        applied = jnp.where(inside_ref[...] > 0.5, applied, 0.0)
        direction_out[i] = direction
        applied_out[i] = applied
        pa_ref[pl.ds(i, 1), :] = _lane_sum(direction * applied, inner_ref[...] > 0.5)
        return carry

    lax.fori_loop(0, BLOCK, body, 0)


def _final_kernel(step_ref, solution_ref, direction_ref, z_ref, stiff_ref, gain_ref,
                  weight_total, kappa_total):
    base = pl.program_id(0) * BLOCK

    @pl.when(pl.program_id(0) == 0)
    def _():
        weight_total[...] = jnp.zeros_like(weight_total)
        kappa_total[...] = jnp.zeros_like(kappa_total)

    def body(i, carry):
        step = step_ref[base + i]
        solution = solution_ref[i] + step * direction_ref[i]
        stiff_solution = _stiffen_slab(solution, gain_ref[...])
        stiff_probe = stiff_ref[i]
        weight_total[...] = weight_total[...] + stiff_solution * stiff_probe
        kappa_total[...] = kappa_total[...] + (solution * stiff_probe + stiff_solution * z_ref[i])
        return carry

    lax.fori_loop(0, BLOCK, body, 0)


def _field_spec(shape, offset=0):
    return pl.BlockSpec((BLOCK,) + shape, lambda g, *_: (g + offset, 0, 0))


def _plane_spec(shape, index=None):
    if index is None:
        return pl.BlockSpec(shape, lambda g, *_: (0, 0))
    return pl.BlockSpec((None,) + shape, lambda g, *_: (index, 0, 0))


def _call(kernel, scalars, inputs, in_specs, out_shapes, out_specs, probes, passes, sequential=False):
    field_bytes = 4 * probes * out_shapes[0].shape[-1] * out_shapes[0].shape[-2]
    grid_spec = pltpu.PrefetchScalarGridSpec(
        num_scalar_prefetch=len(scalars),
        grid=(probes // BLOCK,),
        in_specs=in_specs,
        out_specs=out_specs,
    )
    return pl.pallas_call(
        kernel,
        grid_spec=grid_spec,
        out_shape=out_shapes,
        compiler_params=pltpu.CompilerParams(
            dimension_semantics=("arbitrary" if sequential else "parallel",)
        ),
        cost_estimate=pl.CostEstimate(
            flops=30 * field_bytes // 4, transcendentals=0, bytes_accessed=passes * field_bytes
        ),
    )(*scalars, *inputs)


def on_device(probes, observed, kappa_sq, variance_weight):
    probe_count, rows, cols = probes.shape
    assert probe_count % BLOCK == 0 and rows >= HALO and cols >= HALO
    stacked = jnp.concatenate(
        [probes, observed[None], kappa_sq[None], variance_weight[None]], axis=0
    )
    ext = extended(stacked, (("rows", 1), ("cols", 2)), HALO)
    slab_rows = -(-(rows + 2 * HALO) // 8) * 8
    slab_cols = -(-(cols + 2 * HALO) // 128) * 128
    ext = jnp.pad(
        ext, ((0, 0), (0, slab_rows - ext.shape[1]), (0, slab_cols - ext.shape[2]))
    )
    slab = (slab_rows, slab_cols)
    observed_ext = ext[probe_count]
    gain = ext[probe_count + 1] + 20.0 / 6.0
    weight_ext = ext[probe_count + 2]

    row_at = lax.axis_index("rows") * rows - HALO + lax.iota(jnp.int32, slab_rows)
    col_at = lax.axis_index("cols") * cols - HALO + lax.iota(jnp.int32, slab_cols)
    row_in = (row_at >= 0) & (row_at < rows * lax.axis_size("rows"))
    col_in = (col_at >= 0) & (col_at < cols * lax.axis_size("cols"))
    inside = (row_in[:, None] & col_in[None, :]).astype(jnp.float32)
    row_inner = (lax.iota(jnp.int32, slab_rows) >= HALO) & (lax.iota(jnp.int32, slab_rows) < HALO + rows)
    col_inner = (lax.iota(jnp.int32, slab_cols) >= HALO) & (lax.iota(jnp.int32, slab_cols) < HALO + cols)
    inner = (row_inner[:, None] & col_inner[None, :]).astype(jnp.float32)

    field = jax.ShapeDtypeStruct((probe_count,) + slab, jnp.float32)
    dots = jax.ShapeDtypeStruct((probe_count, 128), jnp.float32)
    dot_spec = pl.BlockSpec((BLOCK, 128), lambda g, *_: (g, 0))
    fspec = _field_spec(slab)
    pspec = _plane_spec(slab)

    def lane_total(partial):
        return jnp.sum(partial, axis=1)

    stiff_probe, applied, zz, za = _call(
        _first_kernel, (), (ext, gain, weight_ext, inside, inner),
        [fspec, pspec, pspec, pspec, pspec],
        (field, field, dots, dots), (fspec, fspec, dot_spec, dot_spec), probe_count, 3,
    )
    first = all_sum(jnp.stack([lane_total(zz), lane_total(za)]))
    norm_now = first[0]
    step_len = norm_now / first[1]
    solution, residual, rr = _call(
        _start_kernel, (step_len,), (ext, applied, inner),
        [fspec, fspec, pspec], (field, field, dots), (fspec, fspec, dot_spec), probe_count, 4,
    )
    direction = ext
    for iteration in range(1, ITERS):
        norm_next = all_sum(lane_total(rr))
        beta = norm_next / norm_now
        norm_now = norm_next
        direction, applied, pa = _call(
            _direction_kernel, (beta,),
            (residual, direction, gain, weight_ext, inside, inner),
            [fspec, fspec, pspec, pspec, pspec, pspec],
            (field, field, dots), (fspec, fspec, dot_spec), probe_count, 4,
        )
        step_len = norm_now / all_sum(lane_total(pa))
        if iteration + 1 < ITERS:
            solution, residual, rr = _call(
                _update_kernel, (step_len,), (solution, direction, residual, applied, inner),
                [fspec, fspec, fspec, fspec, pspec],
                (field, field, dots), (fspec, fspec, dot_spec), probe_count, 6,
            )

    plane = jax.ShapeDtypeStruct(slab, jnp.float32)
    weight_total, kappa_total = _call(
        _final_kernel, (step_len,), (solution, direction, ext, stiff_probe, gain),
        [fspec, fspec, fspec, fspec, pspec],
        (plane, plane), (pspec, pspec), probe_count, 4, sequential=True,
    )

    def inner_of(plane_value):
        return plane_value[HALO : HALO + rows, HALO : HALO + cols]

    weight_total = inner_of(weight_total)
    kappa_total = inner_of(kappa_total)
    stiff_obs = inner_of(stiffen(observed_ext, ext[probe_count + 1]))
    grad_weight = 0.5 * weight_total / probe_count - 0.5 * stiff_obs * stiff_obs
    grad_kappa = (
        0.5 * variance_weight * (kappa_total / probe_count) - observed * variance_weight * stiff_obs
    )
    return (grad_kappa, grad_weight)


def solution(mesh):
    placed = (P(None, "rows", "cols"), P("rows", "cols"), P("rows", "cols"), P("rows", "cols"))
    return jax.shard_map(
        on_device,
        mesh=mesh,
        in_specs=placed,
        out_specs=(P("rows", "cols"), P("rows", "cols")),
        check_vma=False,
    )
```

```python
import jax
import jax.numpy as jnp
from jax import lax
from jax.sharding import PartitionSpec as P

ITERS = 3
HALO = 2 * ITERS


def extended(cells, sides, width):
    for axis, dim in sides:
        count = lax.axis_size(axis)
        ends = count - 1
        head = lax.slice_in_dim(cells, 0, width, axis=dim)
        tail = lax.slice_in_dim(cells, cells.shape[dim] - width, cells.shape[dim], axis=dim)
        cells = jnp.concatenate(
            [
                lax.ppermute(tail, axis, [(i, (i + 1) % count) for i in range(ends)]),
                cells,
                lax.ppermute(head, axis, [((i + 1) % count, i) for i in range(ends)]),
            ],
            axis=dim,
        )
    return cells


def stencil(padded, kappa_sq):
    centre = padded[..., 1:-1, 1:-1]
    edge_sum = (
        padded[..., :-2, 1:-1]
        + padded[..., 2:, 1:-1]
        + padded[..., 1:-1, :-2]
        + padded[..., 1:-1, 2:]
    )
    corners = (
        padded[..., :-2, :-2] + padded[..., :-2, 2:] + padded[..., 2:, :-2] + padded[..., 2:, 2:]
    )
    return (kappa_sq + 20.0 / 6.0) * centre - (4.0 * edge_sum + corners) / 6.0


def stiffen(field, kappa_sq):
    pads = ((0, 0),) * (field.ndim - 2) + ((1, 1), (1, 1))
    return stencil(jnp.pad(field, pads), kappa_sq)


def all_sum(terms):
    for axis in ("cols", "rows"):
        count = lax.axis_size(axis)
        if count & (count - 1):
            terms = lax.psum(terms, axis)
            continue
        hop = 1
        while hop < count:
            terms = terms + lax.ppermute(terms, axis, [(i, i ^ hop) for i in range(count)])
            hop *= 2
    return terms


def stiffen_lanes(field, kappa_sq):
    padded = jnp.pad(field, ((1, 1), (1, 1), (0, 0)))
    centre = padded[1:-1, 1:-1]
    edge_sum = padded[:-2, 1:-1] + padded[2:, 1:-1] + padded[1:-1, :-2] + padded[1:-1, 2:]
    corners = padded[:-2, :-2] + padded[:-2, 2:] + padded[2:, :-2] + padded[2:, 2:]
    return (kappa_sq + 20.0 / 6.0) * centre - (4.0 * edge_sum + corners) / 6.0


def on_device(probes, observed, kappa_sq, variance_weight):
    probe_count, rows, cols = probes.shape
    assert rows >= HALO and cols % 2 == 0 and cols // 2 >= HALO
    half = cols // 2
    width = half + 2 * HALO
    stacked = jnp.concatenate(
        [probes, observed[None], kappa_sq[None], variance_weight[None]], axis=0
    )
    ext = extended(stacked, (("rows", 1), ("cols", 2)), HALO)
    halves = [ext[:, :, h * half : h * half + width] for h in range(2)]

    def on_lanes(index):
        if index is None:
            return jnp.concatenate([jnp.transpose(h[:probe_count], (1, 2, 0)) for h in halves], axis=2)
        return jnp.concatenate(
            [jnp.broadcast_to(h[index][:, :, None], h.shape[1:] + (probe_count,)) for h in halves],
            axis=2,
        )

    probe_ext = on_lanes(None)
    kappa_ext = on_lanes(probe_count + 1)
    weight_ext = on_lanes(probe_count + 2)

    row_at = lax.axis_index("rows") * rows - HALO + lax.iota(jnp.int32, rows + 2 * HALO)
    row_in = (row_at >= 0) & (row_at < rows * lax.axis_size("rows"))
    col_in = []
    for h in range(2):
        col_at = lax.axis_index("cols") * cols - HALO + h * half + lax.iota(jnp.int32, width)
        col_in.append((col_at >= 0) & (col_at < cols * lax.axis_size("cols")))
    col_in = jnp.concatenate(
        [jnp.broadcast_to(c[:, None], (width, probe_count)) for c in col_in], axis=1
    )
    mask = (row_in[:, None, None] & col_in[None, :, :]).astype(jnp.float32)

    def inner(field):
        return field[HALO : HALO + rows, HALO : HALO + half]

    def dot(first, second):
        lanes = jnp.sum(inner(first) * inner(second), axis=(0, 1))
        return jnp.sum(lanes.reshape(2, probe_count), axis=0)

    def on_lane(scalars):
        return jnp.tile(scalars, 2)[None, None, :]

    def apply_q(direction):
        stiffness = stiffen_lanes(direction, kappa_ext)
        applied = mask * stiffen_lanes(weight_ext * stiffness, kappa_ext)
        return stiffness, applied

    residual = probe_ext
    direction = probe_ext
    solution = None
    stiff_probe, applied = apply_q(direction)
    first = all_sum(jnp.stack([dot(residual, residual), dot(direction, applied)]))
    norm_now = first[0]
    curvature = first[1]
    for iteration in range(ITERS):
        if iteration > 0:
            _, applied = apply_q(direction)
            curvature = all_sum(dot(direction, applied))
        step_len = on_lane(norm_now / curvature)
        solution = step_len * direction if solution is None else solution + step_len * direction
        if iteration + 1 < ITERS:
            residual = residual - step_len * applied
            norm_next = all_sum(dot(residual, residual))
            direction = residual + on_lane(norm_next / norm_now) * direction
            norm_now = norm_next

    stiff_solution = inner(stiffen_lanes(solution, kappa_ext))
    stiff_probe = inner(stiff_probe)
    solution = inner(solution)
    probe_in = inner(probe_ext)

    def probe_total(terms):
        per_half = jnp.sum(terms.reshape(rows, half, 2, probe_count), axis=3)
        return jnp.transpose(per_half, (0, 2, 1)).reshape(rows, cols)

    weight_total = probe_total(stiff_solution * stiff_probe)
    kappa_total = probe_total(solution * stiff_probe + stiff_solution * probe_in)
    stiff_obs = stiffen(ext[probe_count], ext[probe_count + 1])[HALO : HALO + rows, HALO : HALO + cols]
    grad_weight = 0.5 * weight_total / probe_count - 0.5 * stiff_obs * stiff_obs
    grad_kappa = (
        0.5 * variance_weight * (kappa_total / probe_count) - observed * variance_weight * stiff_obs
    )
    return (grad_kappa, grad_weight)


def solution(mesh):
    placed = (P(None, "rows", "cols"), P("rows", "cols"), P("rows", "cols"), P("rows", "cols"))
    return jax.shard_map(
        on_device,
        mesh=mesh,
        in_specs=placed,
        out_specs=(P("rows", "cols"), P("rows", "cols")),
        check_vma=False,
    )
```

```python
import jax
import jax.numpy as jnp
from jax import lax
from jax.experimental import pallas as pl
from jax.experimental.pallas import tpu as pltpu
from jax.sharding import PartitionSpec as P

ITERS = 3
HALO = 2 * ITERS


def extended(cells, sides, width):
    for axis, dim in sides:
        count = lax.axis_size(axis)
        ends = count - 1
        head = lax.slice_in_dim(cells, 0, width, axis=dim)
        tail = lax.slice_in_dim(cells, cells.shape[dim] - width, cells.shape[dim], axis=dim)
        cells = jnp.concatenate(
            [
                lax.ppermute(tail, axis, [(i, (i + 1) % count) for i in range(ends)]),
                cells,
                lax.ppermute(head, axis, [((i + 1) % count, i) for i in range(ends)]),
            ],
            axis=dim,
        )
    return cells


def stencil(padded, kappa_sq):
    centre = padded[..., 1:-1, 1:-1]
    edge_sum = (
        padded[..., :-2, 1:-1]
        + padded[..., 2:, 1:-1]
        + padded[..., 1:-1, :-2]
        + padded[..., 1:-1, 2:]
    )
    corners = (
        padded[..., :-2, :-2] + padded[..., :-2, 2:] + padded[..., 2:, :-2] + padded[..., 2:, 2:]
    )
    return (kappa_sq + 20.0 / 6.0) * centre - (4.0 * edge_sum + corners) / 6.0


def stiffen(field, kappa_sq):
    pads = ((0, 0),) * (field.ndim - 2) + ((1, 1), (1, 1))
    return stencil(jnp.pad(field, pads), kappa_sq)


def all_sum(terms):
    for axis in ("cols", "rows"):
        count = lax.axis_size(axis)
        if count & (count - 1):
            terms = lax.psum(terms, axis)
            continue
        hop = 1
        while hop < count:
            terms = terms + lax.ppermute(terms, axis, [(i, i ^ hop) for i in range(count)])
            hop *= 2
    return terms


def _stiffen_row(ref, r, gain):
    mid = ref[r]
    vertical = ref[r - 1] + ref[r + 1]
    n = mid.shape[0]
    edge_sum = vertical + pltpu.roll(mid, 1, 0) + pltpu.roll(mid, n - 1, 0)
    corners = pltpu.roll(vertical, 1, 0) + pltpu.roll(vertical, n - 1, 0)
    return gain * mid - (4.0 * edge_sum + corners) * (1.0 / 6.0)


def _row_sum(value, keep):
    return jnp.sum(jnp.where(keep, value, 0.0), axis=0, keepdims=True)


class _Plan:
    def __init__(self, slab_rows, first_inner, inner_rows):
        self.slab_rows = slab_rows
        self.first_inner = first_inner
        self.inner_rows = inner_rows

    def inner_row(self, r):
        return (r >= self.first_inner) & (r < self.first_inner + self.inner_rows)


def _zero_edges(ref):
    ref[0] = jnp.zeros(ref.shape[1:], ref.dtype)
    ref[ref.shape[0] - 1] = jnp.zeros(ref.shape[1:], ref.dtype)


def _apply_q(plan, source, gain_ref, weight_ref, inside_ref, row_ref, inner_ref, stiff_ref,
             applied_ref, dot_source):
    last = plan.slab_rows - 1
    _zero_edges(stiff_ref)
    _zero_edges(applied_ref)

    def first_pass(r, carry):
        stiff_ref[r] = weight_ref[r] * _stiffen_row(source, r, gain_ref[r])
        return carry

    lax.fori_loop(1, last, first_pass, 0)

    def second_pass(r, totals):
        applied = _stiffen_row(stiff_ref, r, gain_ref[r])
        keep = (inside_ref[...] > 0.5) & (row_ref[r] > 0.5)
        applied = jnp.where(keep, applied, 0.0)
        applied_ref[r] = applied
        inner = (inner_ref[...] > 0.5) & plan.inner_row(r)
        return totals + _row_sum(dot_source[r] * applied, inner)

    return lax.fori_loop(1, last, second_pass, jnp.zeros((1, source.shape[2]), jnp.float32))


def _first_kernel(plan, z_ref, gain_ref, weight_ref, inside_ref, row_ref, inner_ref,
                  stiff_out, applied_out, dots_out, scratch):
    last = plan.slab_rows - 1
    _zero_edges(stiff_out)

    def probe_pass(r, totals):
        stiff_out[r] = _stiffen_row(z_ref, r, gain_ref[r])
        z = z_ref[r]
        inner = (inner_ref[...] > 0.5) & plan.inner_row(r)
        return totals + _row_sum(z * z, inner)

    zz = lax.fori_loop(1, last, probe_pass, jnp.zeros((1, z_ref.shape[2]), jnp.float32))
    _zero_edges(scratch)

    def weigh(r, carry):
        scratch[r] = weight_ref[r] * stiff_out[r]
        return carry

    lax.fori_loop(1, last, weigh, 0)

    def second_pass(r, totals):
        applied = _stiffen_row(scratch, r, gain_ref[r])
        keep = (inside_ref[...] > 0.5) & (row_ref[r] > 0.5)
        applied = jnp.where(keep, applied, 0.0)
        applied_out[r] = applied
        inner = (inner_ref[...] > 0.5) & plan.inner_row(r)
        return totals + _row_sum(z_ref[r] * applied, inner)

    _zero_edges(applied_out)
    za = lax.fori_loop(1, last, second_pass, jnp.zeros((1, z_ref.shape[2]), jnp.float32))
    dots_out[0:1, :] = zz
    dots_out[1:2, :] = za


def _start_kernel(plan, step_ref, z_ref, applied_ref, inner_ref, solution_out, residual_out, rr_out):
    step = step_ref[...]

    def body(r, totals):
        z = z_ref[r]
        residual = z - step * applied_ref[r]
        solution_out[r] = step * z
        residual_out[r] = residual
        inner = (inner_ref[...] > 0.5) & plan.inner_row(r)
        return totals + _row_sum(residual * residual, inner)

    rr_out[...] = lax.fori_loop(0, plan.slab_rows, body, jnp.zeros((1, z_ref.shape[2]), jnp.float32))


def _update_kernel(plan, step_ref, solution_ref, direction_ref, residual_ref, applied_ref, inner_ref,
                   solution_out, residual_out, rr_out):
    step = step_ref[...]

    def body(r, totals):
        residual = residual_ref[r] - step * applied_ref[r]
        solution_out[r] = solution_ref[r] + step * direction_ref[r]
        residual_out[r] = residual
        inner = (inner_ref[...] > 0.5) & plan.inner_row(r)
        return totals + _row_sum(residual * residual, inner)

    rr_out[...] = lax.fori_loop(
        0, plan.slab_rows, body, jnp.zeros((1, residual_ref.shape[2]), jnp.float32)
    )


def _direction_kernel(plan, beta_ref, residual_ref, direction_ref, gain_ref, weight_ref, inside_ref,
                      row_ref, inner_ref, direction_out, applied_out, pa_out, scratch):
    beta = beta_ref[...]

    def new_direction(r, carry):
        direction_out[r] = residual_ref[r] + beta * direction_ref[r]
        return carry

    lax.fori_loop(0, plan.slab_rows, new_direction, 0)
    pa_out[...] = _apply_q(plan, direction_out, gain_ref, weight_ref, inside_ref, row_ref, inner_ref,
                           scratch, applied_out, direction_out)


def _final_kernel(plan, step_ref, solution_ref, direction_ref, z_ref, stiff_ref, gain_ref,
                  weight_out, kappa_out, scratch):
    step = step_ref[...]
    last = plan.slab_rows - 1

    def new_solution(r, carry):
        scratch[r] = solution_ref[r] + step * direction_ref[r]
        return carry

    lax.fori_loop(0, plan.slab_rows, new_solution, 0)
    _zero_edges(weight_out)
    _zero_edges(kappa_out)

    def body(r, carry):
        stiff_solution = _stiffen_row(scratch, r, gain_ref[r])
        stiff_probe = stiff_ref[r]
        weight_out[r] = stiff_solution * stiff_probe
        kappa_out[r] = scratch[r] * stiff_probe + stiff_solution * z_ref[r]
        return carry

    lax.fori_loop(1, last, body, 0)


def _vmem():
    return pl.BlockSpec(memory_space=pltpu.VMEM)


def _call(kernel, plan, inputs, out_shapes, scratch=0, smem=()):
    field = out_shapes[0]
    nbytes = 4 * field.shape[0] * field.shape[1] * field.shape[2]
    in_specs = [
        pl.BlockSpec(memory_space=pltpu.SMEM) if i in smem else _vmem() for i in range(len(inputs))
    ]
    return pl.pallas_call(
        lambda *refs: kernel(plan, *refs),
        out_shape=out_shapes,
        in_specs=in_specs,
        out_specs=tuple(_vmem() for _ in out_shapes),
        scratch_shapes=[pltpu.VMEM(field.shape, jnp.float32)] * scratch,
        cost_estimate=pl.CostEstimate(
            flops=40 * nbytes // 4,
            transcendentals=0,
            bytes_accessed=(len(inputs) + len(out_shapes)) * nbytes,
        ),
    )(*inputs)


def on_device(probes, observed, kappa_sq, variance_weight):
    probe_count, rows, cols = probes.shape
    assert rows >= HALO and cols % 2 == 0 and cols // 2 >= HALO
    half = cols // 2
    width = half + 2 * HALO
    sublanes = -(-width // 8) * 8
    slab_rows = rows + 2 * HALO
    lanes = 2 * probe_count
    stacked = jnp.concatenate(
        [probes, observed[None], kappa_sq[None], variance_weight[None]], axis=0
    )
    ext = extended(stacked, (("rows", 1), ("cols", 2)), HALO)
    halves = [
        jnp.pad(ext[:, :, h * half : h * half + width], ((0, 0), (0, 0), (0, sublanes - width)))
        for h in range(2)
    ]

    def plane_on_lanes(index):
        return jnp.concatenate(
            [jnp.broadcast_to(h[index][:, :, None], h.shape[1:] + (probe_count,)) for h in halves],
            axis=2,
        )

    z = jnp.concatenate([jnp.transpose(h[:probe_count], (1, 2, 0)) for h in halves], axis=2)
    gain = plane_on_lanes(probe_count + 1) + 20.0 / 6.0
    weight = plane_on_lanes(probe_count + 2)

    row_at = lax.axis_index("rows") * rows - HALO + lax.iota(jnp.int32, slab_rows)
    row_in = ((row_at >= 0) & (row_at < rows * lax.axis_size("rows"))).astype(jnp.float32)
    col_in = []
    col_inner = []
    for h in range(2):
        at = lax.iota(jnp.int32, sublanes)
        col_at = lax.axis_index("cols") * cols - HALO + h * half + at
        col_in.append((col_at >= 0) & (col_at < cols * lax.axis_size("cols")) & (at < width))
        col_inner.append((at >= HALO) & (at < HALO + half))

    def on_lanes_of(columns):
        return jnp.concatenate(
            [jnp.broadcast_to(c[:, None], (sublanes, probe_count)) for c in columns], axis=1
        ).astype(jnp.float32)

    inside = on_lanes_of(col_in)
    inner = on_lanes_of(col_inner)
    plan = _Plan(slab_rows, HALO, rows)

    field = jax.ShapeDtypeStruct((slab_rows, sublanes, lanes), jnp.float32)
    lane_row = jax.ShapeDtypeStruct((1, lanes), jnp.float32)

    def per_probe(lane_totals):
        return jnp.sum(lane_totals.reshape(lane_totals.shape[:-1] + (2, probe_count)), axis=-2)

    def on_lane(scalars):
        return jnp.tile(scalars, 2)[None, :]

    stiff_probe, applied, first = _call(
        _first_kernel, plan, (z, gain, weight, inside, row_in, inner),
        (field, field, jax.ShapeDtypeStruct((2, lanes), jnp.float32)), scratch=1, smem=(4,),
    )
    first = all_sum(per_probe(first))
    norm_now = first[0]
    step_len = norm_now / first[1]
    solution, residual, rr = _call(
        _start_kernel, plan, (on_lane(step_len), z, applied, inner), (field, field, lane_row)
    )
    direction = z
    for iteration in range(1, ITERS):
        norm_next = all_sum(per_probe(rr[0]))
        beta = norm_next / norm_now
        norm_now = norm_next
        direction, applied, pa = _call(
            _direction_kernel, plan,
            (on_lane(beta), residual, direction, gain, weight, inside, row_in, inner),
            (field, field, lane_row), scratch=1, smem=(6,),
        )
        step_len = norm_now / all_sum(per_probe(pa[0]))
        if iteration + 1 < ITERS:
            solution, residual, rr = _call(
                _update_kernel, plan,
                (on_lane(step_len), solution, direction, residual, applied, inner),
                (field, field, lane_row),
            )

    weight_terms, kappa_terms = _call(
        _final_kernel, plan, (on_lane(step_len), solution, direction, z, stiff_probe, gain),
        (field, field), scratch=1,
    )

    def probe_total(terms):
        terms = terms[HALO : HALO + rows, HALO : HALO + half]
        per_half = jnp.sum(terms.reshape(rows, half, 2, probe_count), axis=3)
        return jnp.transpose(per_half, (0, 2, 1)).reshape(rows, cols)

    weight_total = probe_total(weight_terms)
    kappa_total = probe_total(kappa_terms)
    stiff_obs = stiffen(ext[probe_count], ext[probe_count + 1])[HALO : HALO + rows, HALO : HALO + cols]
    grad_weight = 0.5 * weight_total / probe_count - 0.5 * stiff_obs * stiff_obs
    grad_kappa = (
        0.5 * variance_weight * (kappa_total / probe_count) - observed * variance_weight * stiff_obs
    )
    return (grad_kappa, grad_weight)


def solution(mesh):
    placed = (P(None, "rows", "cols"), P("rows", "cols"), P("rows", "cols"), P("rows", "cols"))
    return jax.shard_map(
        on_device,
        mesh=mesh,
        in_specs=placed,
        out_specs=(P("rows", "cols"), P("rows", "cols")),
        check_vma=False,
    )
```

```python
import jax
import jax.numpy as jnp
from jax import lax
from jax.experimental import pallas as pl
from jax.experimental.pallas import tpu as pltpu
from jax.sharding import PartitionSpec as P

ITERS = 3
HALO = 2 * ITERS


def extended(cells, sides, width):
    for axis, dim in sides:
        count = lax.axis_size(axis)
        ends = count - 1
        head = lax.slice_in_dim(cells, 0, width, axis=dim)
        tail = lax.slice_in_dim(cells, cells.shape[dim] - width, cells.shape[dim], axis=dim)
        cells = jnp.concatenate(
            [
                lax.ppermute(tail, axis, [(i, (i + 1) % count) for i in range(ends)]),
                cells,
                lax.ppermute(head, axis, [((i + 1) % count, i) for i in range(ends)]),
            ],
            axis=dim,
        )
    return cells


def stencil(padded, kappa_sq):
    centre = padded[..., 1:-1, 1:-1]
    edge_sum = (
        padded[..., :-2, 1:-1]
        + padded[..., 2:, 1:-1]
        + padded[..., 1:-1, :-2]
        + padded[..., 1:-1, 2:]
    )
    corners = (
        padded[..., :-2, :-2] + padded[..., :-2, 2:] + padded[..., 2:, :-2] + padded[..., 2:, 2:]
    )
    return (kappa_sq + 20.0 / 6.0) * centre - (4.0 * edge_sum + corners) / 6.0


def stiffen(field, kappa_sq):
    pads = ((0, 0),) * (field.ndim - 2) + ((1, 1), (1, 1))
    return stencil(jnp.pad(field, pads), kappa_sq)


def all_sum(terms):
    for axis in ("cols", "rows"):
        count = lax.axis_size(axis)
        if count & (count - 1):
            terms = lax.psum(terms, axis)
            continue
        hop = 1
        while hop < count:
            terms = terms + lax.ppermute(terms, axis, [(i, i ^ hop) for i in range(count)])
            hop *= 2
    return terms


def _stiffen_row(ref, r, gain):
    mid = ref[r]
    vertical = ref[r - 1] + ref[r + 1]
    n = mid.shape[0]
    edge_sum = vertical + pltpu.roll(mid, 1, 0) + pltpu.roll(mid, n - 1, 0)
    corners = pltpu.roll(vertical, 1, 0) + pltpu.roll(vertical, n - 1, 0)
    return gain * mid - (4.0 * edge_sum + corners) * (1.0 / 6.0)


def _total(ref, row):
    value = ref[row : row + 1, :]
    return value + pltpu.roll(value, value.shape[1] // 2, 1)


def _ratio(num_ref, num_row, den_ref, den_row):
    return _total(num_ref, num_row) / _total(den_ref, den_row)


def _row_sum(value, keep):
    return jnp.sum(jnp.where(keep, value, 0.0), axis=0, keepdims=True)


class _Plan:
    def __init__(self, slab_rows, first_inner, inner_rows):
        self.slab_rows = slab_rows
        self.first_inner = first_inner
        self.inner_rows = inner_rows

    def inner_row(self, r):
        return (r >= self.first_inner) & (r < self.first_inner + self.inner_rows)


def _zero_edges(ref):
    ref[0] = jnp.zeros(ref.shape[1:], ref.dtype)
    ref[ref.shape[0] - 1] = jnp.zeros(ref.shape[1:], ref.dtype)


def _apply_q(plan, source, gain_ref, weight_ref, inside_ref, row_ref, inner_ref, stiff_ref,
             applied_ref, dot_source):
    last = plan.slab_rows - 1
    _zero_edges(stiff_ref)
    _zero_edges(applied_ref)

    def first_pass(r, carry):
        stiff_ref[r] = weight_ref[r] * _stiffen_row(source, r, gain_ref[r])
        return carry

    lax.fori_loop(1, last, first_pass, 0)

    def second_pass(r, totals):
        applied = _stiffen_row(stiff_ref, r, gain_ref[r])
        keep = (inside_ref[...] > 0.5) & (row_ref[r] > 0.5)
        applied = jnp.where(keep, applied, 0.0)
        applied_ref[r] = applied
        inner = (inner_ref[...] > 0.5) & plan.inner_row(r)
        return totals + _row_sum(dot_source[r] * applied, inner)

    return lax.fori_loop(1, last, second_pass, jnp.zeros((1, source.shape[2]), jnp.float32))


def _first_kernel(plan, z_ref, gain_ref, weight_ref, inside_ref, row_ref, inner_ref,
                  stiff_out, applied_out, dots_out, scratch):
    last = plan.slab_rows - 1
    _zero_edges(stiff_out)

    def probe_pass(r, totals):
        stiff_out[r] = _stiffen_row(z_ref, r, gain_ref[r])
        z = z_ref[r]
        inner = (inner_ref[...] > 0.5) & plan.inner_row(r)
        return totals + _row_sum(z * z, inner)

    zz = lax.fori_loop(1, last, probe_pass, jnp.zeros((1, z_ref.shape[2]), jnp.float32))
    _zero_edges(scratch)

    def weigh(r, carry):
        scratch[r] = weight_ref[r] * stiff_out[r]
        return carry

    lax.fori_loop(1, last, weigh, 0)

    def second_pass(r, totals):
        applied = _stiffen_row(scratch, r, gain_ref[r])
        keep = (inside_ref[...] > 0.5) & (row_ref[r] > 0.5)
        applied = jnp.where(keep, applied, 0.0)
        applied_out[r] = applied
        inner = (inner_ref[...] > 0.5) & plan.inner_row(r)
        return totals + _row_sum(z_ref[r] * applied, inner)

    _zero_edges(applied_out)
    za = lax.fori_loop(1, last, second_pass, jnp.zeros((1, z_ref.shape[2]), jnp.float32))
    dots_out[0:1, :] = zz
    dots_out[1:2, :] = za


def _start_kernel(plan, first_ref, z_ref, applied_ref, inner_ref, solution_out, residual_out, rr_out):
    step = _ratio(first_ref, 0, first_ref, 1)

    def body(r, totals):
        z = z_ref[r]
        residual = z - step * applied_ref[r]
        solution_out[r] = step * z
        residual_out[r] = residual
        inner = (inner_ref[...] > 0.5) & plan.inner_row(r)
        return totals + _row_sum(residual * residual, inner)

    rr_out[...] = lax.fori_loop(0, plan.slab_rows, body, jnp.zeros((1, z_ref.shape[2]), jnp.float32))


def _update_kernel(plan, norm_ref, curvature_ref, solution_ref, direction_ref, residual_ref,
                   applied_ref, inner_ref, solution_out, residual_out, rr_out):
    step = _ratio(norm_ref, 0, curvature_ref, 0)

    def body(r, totals):
        residual = residual_ref[r] - step * applied_ref[r]
        solution_out[r] = solution_ref[r] + step * direction_ref[r]
        residual_out[r] = residual
        inner = (inner_ref[...] > 0.5) & plan.inner_row(r)
        return totals + _row_sum(residual * residual, inner)

    rr_out[...] = lax.fori_loop(
        0, plan.slab_rows, body, jnp.zeros((1, residual_ref.shape[2]), jnp.float32)
    )


def _direction_kernel(plan, next_ref, now_ref, residual_ref, direction_ref, gain_ref, weight_ref,
                      inside_ref, row_ref, inner_ref, direction_out, applied_out, pa_out, scratch):
    beta = _ratio(next_ref, 0, now_ref, 0)

    def new_direction(r, carry):
        direction_out[r] = residual_ref[r] + beta * direction_ref[r]
        return carry

    lax.fori_loop(0, plan.slab_rows, new_direction, 0)
    pa_out[...] = _apply_q(plan, direction_out, gain_ref, weight_ref, inside_ref, row_ref, inner_ref,
                           scratch, applied_out, direction_out)


def _final_kernel(plan, norm_ref, curvature_ref, solution_ref, direction_ref, z_ref, stiff_ref,
                  gain_ref, weight_out, kappa_out, scratch):
    step = _ratio(norm_ref, 0, curvature_ref, 0)
    last = plan.slab_rows - 1

    def new_solution(r, carry):
        scratch[r] = solution_ref[r] + step * direction_ref[r]
        return carry

    lax.fori_loop(0, plan.slab_rows, new_solution, 0)
    _zero_edges(weight_out)
    _zero_edges(kappa_out)

    def body(r, carry):
        stiff_solution = _stiffen_row(scratch, r, gain_ref[r])
        stiff_probe = stiff_ref[r]
        weight_out[r] = stiff_solution * stiff_probe
        kappa_out[r] = scratch[r] * stiff_probe + stiff_solution * z_ref[r]
        return carry

    lax.fori_loop(1, last, body, 0)


def _vmem():
    return pl.BlockSpec(memory_space=pltpu.VMEM)


def _call(kernel, plan, inputs, out_shapes, scratch=0, smem=()):
    field = out_shapes[0]
    nbytes = 4 * field.shape[0] * field.shape[1] * field.shape[2]
    in_specs = [
        pl.BlockSpec(memory_space=pltpu.SMEM) if i in smem else _vmem() for i in range(len(inputs))
    ]
    return pl.pallas_call(
        lambda *refs: kernel(plan, *refs),
        out_shape=out_shapes,
        in_specs=in_specs,
        out_specs=tuple(_vmem() for _ in out_shapes),
        scratch_shapes=[pltpu.VMEM(field.shape, jnp.float32)] * scratch,
        cost_estimate=pl.CostEstimate(
            flops=40 * nbytes // 4,
            transcendentals=0,
            bytes_accessed=(len(inputs) + len(out_shapes)) * nbytes,
        ),
    )(*inputs)


def on_device(probes, observed, kappa_sq, variance_weight):
    probe_count, rows, cols = probes.shape
    assert rows >= HALO and cols % 2 == 0 and cols // 2 >= HALO
    half = cols // 2
    width = half + 2 * HALO
    sublanes = -(-width // 8) * 8
    slab_rows = rows + 2 * HALO
    lanes = 2 * probe_count
    stacked = jnp.concatenate(
        [probes, observed[None], kappa_sq[None], variance_weight[None]], axis=0
    )
    ext = extended(stacked, (("rows", 1), ("cols", 2)), HALO)
    halves = [
        jnp.pad(ext[:, :, h * half : h * half + width], ((0, 0), (0, 0), (0, sublanes - width)))
        for h in range(2)
    ]

    def plane_on_lanes(index):
        return jnp.concatenate(
            [jnp.broadcast_to(h[index][:, :, None], h.shape[1:] + (probe_count,)) for h in halves],
            axis=2,
        )

    z = jnp.concatenate([jnp.transpose(h[:probe_count], (1, 2, 0)) for h in halves], axis=2)
    gain = plane_on_lanes(probe_count + 1) + 20.0 / 6.0
    weight = plane_on_lanes(probe_count + 2)

    row_at = lax.axis_index("rows") * rows - HALO + lax.iota(jnp.int32, slab_rows)
    row_in = ((row_at >= 0) & (row_at < rows * lax.axis_size("rows"))).astype(jnp.float32)
    col_in = []
    col_inner = []
    for h in range(2):
        at = lax.iota(jnp.int32, sublanes)
        col_at = lax.axis_index("cols") * cols - HALO + h * half + at
        col_in.append((col_at >= 0) & (col_at < cols * lax.axis_size("cols")) & (at < width))
        col_inner.append((at >= HALO) & (at < HALO + half))

    def on_lanes_of(columns):
        return jnp.concatenate(
            [jnp.broadcast_to(c[:, None], (sublanes, probe_count)) for c in columns], axis=1
        ).astype(jnp.float32)

    inside = on_lanes_of(col_in)
    inner = on_lanes_of(col_inner)
    plan = _Plan(slab_rows, HALO, rows)

    field = jax.ShapeDtypeStruct((slab_rows, sublanes, lanes), jnp.float32)
    lane_row = jax.ShapeDtypeStruct((1, lanes), jnp.float32)

    stiff_probe, applied, first = _call(
        _first_kernel, plan, (z, gain, weight, inside, row_in, inner),
        (field, field, jax.ShapeDtypeStruct((2, lanes), jnp.float32)), scratch=1, smem=(4,),
    )
    first = all_sum(first)
    solution, residual, rr = _call(
        _start_kernel, plan, (first, z, applied, inner), (field, field, lane_row)
    )
    direction = z
    norm_now = first
    for iteration in range(1, ITERS):
        norm_next = all_sum(rr)
        direction, applied, pa = _call(
            _direction_kernel, plan,
            (norm_next, norm_now, residual, direction, gain, weight, inside, row_in, inner),
            (field, field, lane_row), scratch=1, smem=(7,),
        )
        norm_now = norm_next
        curvature = all_sum(pa)
        if iteration + 1 < ITERS:
            solution, residual, rr = _call(
                _update_kernel, plan,
                (norm_now, curvature, solution, direction, residual, applied, inner),
                (field, field, lane_row),
            )

    weight_terms, kappa_terms = _call(
        _final_kernel, plan, (norm_now, curvature, solution, direction, z, stiff_probe, gain),
        (field, field), scratch=1,
    )

    def probe_total(terms):
        terms = terms[HALO : HALO + rows, HALO : HALO + half]
        per_half = jnp.sum(terms.reshape(rows, half, 2, probe_count), axis=3)
        return jnp.transpose(per_half, (0, 2, 1)).reshape(rows, cols)

    weight_total = probe_total(weight_terms)
    kappa_total = probe_total(kappa_terms)
    stiff_obs = stiffen(ext[probe_count], ext[probe_count + 1])[HALO : HALO + rows, HALO : HALO + cols]
    grad_weight = 0.5 * weight_total / probe_count - 0.5 * stiff_obs * stiff_obs
    grad_kappa = (
        0.5 * variance_weight * (kappa_total / probe_count) - observed * variance_weight * stiff_obs
    )
    return (grad_kappa, grad_weight)


def solution(mesh):
    placed = (P(None, "rows", "cols"), P("rows", "cols"), P("rows", "cols"), P("rows", "cols"))
    return jax.shard_map(
        on_device,
        mesh=mesh,
        in_specs=placed,
        out_specs=(P("rows", "cols"), P("rows", "cols")),
        check_vma=False,
    )
```

```python
import jax
import jax.numpy as jnp
from jax import lax
from jax.experimental import pallas as pl
from jax.experimental.pallas import tpu as pltpu
from jax.sharding import PartitionSpec as P

ITERS = 3
HALO = 2 * ITERS


def extended(cells, sides, width):
    for axis, dim in sides:
        count = lax.axis_size(axis)
        ends = count - 1
        head = lax.slice_in_dim(cells, 0, width, axis=dim)
        tail = lax.slice_in_dim(cells, cells.shape[dim] - width, cells.shape[dim], axis=dim)
        cells = jnp.concatenate(
            [
                lax.ppermute(tail, axis, [(i, (i + 1) % count) for i in range(ends)]),
                cells,
                lax.ppermute(head, axis, [((i + 1) % count, i) for i in range(ends)]),
            ],
            axis=dim,
        )
    return cells


def stencil(padded, kappa_sq):
    centre = padded[..., 1:-1, 1:-1]
    edge_sum = (
        padded[..., :-2, 1:-1]
        + padded[..., 2:, 1:-1]
        + padded[..., 1:-1, :-2]
        + padded[..., 1:-1, 2:]
    )
    corners = (
        padded[..., :-2, :-2] + padded[..., :-2, 2:] + padded[..., 2:, :-2] + padded[..., 2:, 2:]
    )
    return (kappa_sq + 20.0 / 6.0) * centre - (4.0 * edge_sum + corners) / 6.0


def stiffen(field, kappa_sq):
    pads = ((0, 0),) * (field.ndim - 2) + ((1, 1), (1, 1))
    return stencil(jnp.pad(field, pads), kappa_sq)


def all_sum(terms):
    for axis in ("cols", "rows"):
        count = lax.axis_size(axis)
        if count & (count - 1):
            terms = lax.psum(terms, axis)
            continue
        hop = 1
        while hop < count:
            terms = terms + lax.ppermute(terms, axis, [(i, i ^ hop) for i in range(count)])
            hop *= 2
    return terms


def _stiffen_row(ref, r, gain):
    mid = ref[r]
    vertical = ref[r - 1] + ref[r + 1]
    n = mid.shape[0]
    edge_sum = vertical + pltpu.roll(mid, 1, 0) + pltpu.roll(mid, n - 1, 0)
    corners = pltpu.roll(vertical, 1, 0) + pltpu.roll(vertical, n - 1, 0)
    return gain * mid - (4.0 * edge_sum + corners) * (1.0 / 6.0)


def _total(ref, row):
    value = ref[row : row + 1, :]
    return value + pltpu.roll(value, value.shape[1] // 2, 1)


def _ratio(num_ref, num_row, den_ref, den_row):
    return _total(num_ref, num_row) / _total(den_ref, den_row)


def _row_sum(value, keep):
    return jnp.sum(jnp.where(keep, value, 0.0), axis=0, keepdims=True)


class _Plan:
    def __init__(self, slab_rows, first_inner, inner_rows, half):
        self.half = half
        self.slab_rows = slab_rows
        self.first_inner = first_inner
        self.inner_rows = inner_rows

    def inner_row(self, r):
        return (r >= self.first_inner) & (r < self.first_inner + self.inner_rows)


def _zero_edges(ref):
    ref[0] = jnp.zeros(ref.shape[1:], ref.dtype)
    ref[ref.shape[0] - 1] = jnp.zeros(ref.shape[1:], ref.dtype)


def _apply_q(plan, source, gain_ref, weight_ref, inside_ref, row_ref, inner_ref, stiff_ref,
             applied_ref, dot_source):
    last = plan.slab_rows - 1
    _zero_edges(stiff_ref)
    _zero_edges(applied_ref)

    def first_pass(r, carry):
        stiff_ref[r] = weight_ref[r] * _stiffen_row(source, r, gain_ref[r])
        return carry

    lax.fori_loop(1, last, first_pass, 0)

    def second_pass(r, totals):
        applied = _stiffen_row(stiff_ref, r, gain_ref[r])
        keep = (inside_ref[...] > 0.5) & (row_ref[r] > 0.5)
        applied = jnp.where(keep, applied, 0.0)
        applied_ref[r] = applied
        inner = (inner_ref[...] > 0.5) & plan.inner_row(r)
        return totals + _row_sum(dot_source[r] * applied, inner)

    return lax.fori_loop(1, last, second_pass, jnp.zeros((1, source.shape[2]), jnp.float32))


def _spread(value, lane):
    return jnp.broadcast_to(value[:, lane : lane + 1], value.shape)


def _plane_row(value, diagonal):
    return jnp.sum(jnp.where(diagonal, value, 0.0), axis=0, keepdims=True)


def _first_kernel(plan, ext_ref, inside_ref, row_ref, inner_ref, diagonal_ref,
                  z_out, gain_out, weight_out, stiff_out, applied_out, dots_out, stiff_obs_out,
                  observed_scr, scratch):
    last = plan.slab_rows - 1
    sublanes = z_out.shape[1]
    lanes = z_out.shape[2]
    probes = lanes // 2

    def relayout(r, carry):
        cells = ext_ref[r]
        left = cells[0:sublanes]
        right = cells[plan.half : plan.half + sublanes]
        low = lax.broadcasted_iota(jnp.int32, (sublanes, lanes), 1) < probes
        z_out[r] = jnp.where(low, left, pltpu.roll(right, probes, 1))
        observed_scr[r] = jnp.where(low, _spread(left, probes), _spread(right, probes))
        gain_out[r] = jnp.where(low, _spread(left, probes + 1), _spread(right, probes + 1)) + 20.0 / 6.0
        weight_out[r] = jnp.where(low, _spread(left, probes + 2), _spread(right, probes + 2))
        return carry

    lax.fori_loop(0, plan.slab_rows, relayout, 0)
    _zero_edges(stiff_out)

    def probe_pass(r, totals):
        stiff_out[r] = _stiffen_row(z_out, r, gain_out[r])
        z = z_out[r]
        inner = (inner_ref[...] > 0.5) & plan.inner_row(r)
        return totals + _row_sum(z * z, inner)

    zz = lax.fori_loop(1, last, probe_pass, jnp.zeros((1, lanes), jnp.float32))
    _zero_edges(scratch)

    def weigh(r, carry):
        scratch[r] = weight_out[r] * stiff_out[r]
        return carry

    lax.fori_loop(1, last, weigh, 0)

    def second_pass(r, totals):
        applied = _stiffen_row(scratch, r, gain_out[r])
        keep = (inside_ref[...] > 0.5) & (row_ref[r] > 0.5)
        applied = jnp.where(keep, applied, 0.0)
        applied_out[r] = applied
        inner = (inner_ref[...] > 0.5) & plan.inner_row(r)
        return totals + _row_sum(z_out[r] * applied, inner)

    _zero_edges(applied_out)
    za = lax.fori_loop(1, last, second_pass, jnp.zeros((1, lanes), jnp.float32))
    dots_out[0:1, :] = zz
    dots_out[1:2, :] = za

    def observed_pass(r, carry):
        stiff_obs = _stiffen_row(observed_scr, plan.first_inner + r, gain_out[plan.first_inner + r])
        stiff_obs_out[pl.ds(r, 1), :] = _plane_row(stiff_obs, diagonal_ref[...] > 0.5)
        return carry

    lax.fori_loop(0, plan.inner_rows, observed_pass, 0)


def _start_kernel(plan, first_ref, z_ref, applied_ref, inner_ref, solution_out, residual_out, rr_out):
    step = _ratio(first_ref, 0, first_ref, 1)

    def body(r, totals):
        z = z_ref[r]
        residual = z - step * applied_ref[r]
        solution_out[r] = step * z
        residual_out[r] = residual
        inner = (inner_ref[...] > 0.5) & plan.inner_row(r)
        return totals + _row_sum(residual * residual, inner)

    rr_out[...] = lax.fori_loop(0, plan.slab_rows, body, jnp.zeros((1, z_ref.shape[2]), jnp.float32))


def _update_kernel(plan, norm_ref, curvature_ref, solution_ref, direction_ref, residual_ref,
                   applied_ref, inner_ref, solution_out, residual_out, rr_out):
    step = _ratio(norm_ref, 0, curvature_ref, 0)

    def body(r, totals):
        residual = residual_ref[r] - step * applied_ref[r]
        solution_out[r] = solution_ref[r] + step * direction_ref[r]
        residual_out[r] = residual
        inner = (inner_ref[...] > 0.5) & plan.inner_row(r)
        return totals + _row_sum(residual * residual, inner)

    rr_out[...] = lax.fori_loop(
        0, plan.slab_rows, body, jnp.zeros((1, residual_ref.shape[2]), jnp.float32)
    )


def _direction_kernel(plan, next_ref, now_ref, residual_ref, direction_ref, gain_ref, weight_ref,
                      inside_ref, row_ref, inner_ref, direction_out, applied_out, pa_out, scratch):
    beta = _ratio(next_ref, 0, now_ref, 0)

    def new_direction(r, carry):
        direction_out[r] = residual_ref[r] + beta * direction_ref[r]
        return carry

    lax.fori_loop(0, plan.slab_rows, new_direction, 0)
    pa_out[...] = _apply_q(plan, direction_out, gain_ref, weight_ref, inside_ref, row_ref, inner_ref,
                           scratch, applied_out, direction_out)


def _final_kernel(plan, norm_ref, curvature_ref, solution_ref, direction_ref, z_ref, stiff_ref,
                  gain_ref, stiff_obs_ref, observed_ref, weight_ref, diagonal_ref,
                  grad_kappa_out, grad_weight_out, scratch):
    step = _ratio(norm_ref, 0, curvature_ref, 0)
    lanes = z_ref.shape[2]
    probes = lanes // 2

    def new_solution(r, carry):
        scratch[r] = solution_ref[r] + step * direction_ref[r]
        return carry

    lax.fori_loop(0, plan.slab_rows, new_solution, 0)

    def probe_sum(value, low):
        first = jnp.sum(jnp.where(low, value, 0.0), axis=1, keepdims=True)
        second = jnp.sum(jnp.where(low, 0.0, value), axis=1, keepdims=True)
        return jnp.where(low, first, second)

    def body(i, carry):
        r = plan.first_inner + i
        solution = scratch[r]
        stiff_solution = _stiffen_row(scratch, r, gain_ref[r])
        stiff_probe = stiff_ref[r]
        low = lax.broadcasted_iota(jnp.int32, solution.shape, 1) < probes
        diagonal = diagonal_ref[...] > 0.5
        weight_total = _plane_row(probe_sum(stiff_solution * stiff_probe, low), diagonal)
        kappa_total = _plane_row(
            probe_sum(solution * stiff_probe + stiff_solution * z_ref[r], low), diagonal
        )
        stiff_obs = stiff_obs_ref[pl.ds(i, 1), :]
        observed = observed_ref[pl.ds(i, 1), :]
        weight = weight_ref[pl.ds(i, 1), :]
        grad_weight_out[pl.ds(i, 1), :] = (
            0.5 * weight_total / probes - 0.5 * stiff_obs * stiff_obs
        )
        grad_kappa_out[pl.ds(i, 1), :] = (
            0.5 * weight * (kappa_total / probes) - observed * weight * stiff_obs
        )
        return carry

    lax.fori_loop(0, plan.inner_rows, body, 0)


def _vmem():
    return pl.BlockSpec(memory_space=pltpu.VMEM)


def _call(kernel, plan, inputs, out_shapes, scratch=0, smem=(), field=None):
    field = out_shapes[0] if field is None else field
    nbytes = 4 * field.shape[0] * field.shape[1] * field.shape[2]
    in_specs = [
        pl.BlockSpec(memory_space=pltpu.SMEM) if i in smem else _vmem() for i in range(len(inputs))
    ]
    return pl.pallas_call(
        lambda *refs: kernel(plan, *refs),
        out_shape=out_shapes,
        in_specs=in_specs,
        out_specs=tuple(_vmem() for _ in out_shapes),
        scratch_shapes=[pltpu.VMEM(field.shape, jnp.float32)] * scratch,
        cost_estimate=pl.CostEstimate(
            flops=40 * nbytes // 4,
            transcendentals=0,
            bytes_accessed=(len(inputs) + len(out_shapes)) * nbytes,
        ),
    )(*inputs)


def on_device(probes, observed, kappa_sq, variance_weight):
    probe_count, rows, cols = probes.shape
    half = cols // 2
    assert rows >= HALO and cols % 2 == 0 and half >= HALO and half == probe_count
    width = half + 2 * HALO
    sublanes = -(-width // 8) * 8
    slab_rows = rows + 2 * HALO
    lanes = 2 * probe_count
    stacked = jnp.concatenate(
        [probes, observed[None], kappa_sq[None], variance_weight[None]], axis=0
    )
    ext = extended(stacked, (("rows", 1), ("cols", 2)), HALO)
    ext = jnp.pad(
        ext, ((0, lanes - ext.shape[0]), (0, 0), (0, half + sublanes - ext.shape[2]))
    )
    ext = jnp.transpose(ext, (1, 2, 0))

    row_at = lax.axis_index("rows") * rows - HALO + lax.iota(jnp.int32, slab_rows)
    row_in = ((row_at >= 0) & (row_at < rows * lax.axis_size("rows"))).astype(jnp.float32)
    col_in = []
    col_inner = []
    for h in range(2):
        at = lax.iota(jnp.int32, sublanes)
        col_at = lax.axis_index("cols") * cols - HALO + h * half + at
        col_in.append((col_at >= 0) & (col_at < cols * lax.axis_size("cols")) & (at < width))
        col_inner.append((at >= HALO) & (at < HALO + half))

    def on_lanes_of(columns):
        return jnp.concatenate(
            [jnp.broadcast_to(c[:, None], (sublanes, probe_count)) for c in columns], axis=1
        ).astype(jnp.float32)

    inside = on_lanes_of(col_in)
    inner = on_lanes_of(col_inner)
    lane_col = lax.iota(jnp.int32, lanes) % half + HALO
    diagonal = (lax.iota(jnp.int32, sublanes)[:, None] == lane_col[None, :]).astype(jnp.float32)
    plan = _Plan(slab_rows, HALO, rows, half)

    field = jax.ShapeDtypeStruct((slab_rows, sublanes, lanes), jnp.float32)
    lane_row = jax.ShapeDtypeStruct((1, lanes), jnp.float32)
    out_plane = jax.ShapeDtypeStruct((rows, cols), jnp.float32)

    z, gain, weight, stiff_probe, applied, first, stiff_obs = _call(
        _first_kernel, plan, (ext, inside, row_in, inner, diagonal),
        (field, field, field, field, field, jax.ShapeDtypeStruct((2, lanes), jnp.float32), out_plane),
        scratch=2, smem=(2,),
    )
    first = all_sum(first)
    solution, residual, rr = _call(
        _start_kernel, plan, (first, z, applied, inner), (field, field, lane_row)
    )
    direction = z
    norm_now = first
    for iteration in range(1, ITERS):
        norm_next = all_sum(rr)
        direction, applied, pa = _call(
            _direction_kernel, plan,
            (norm_next, norm_now, residual, direction, gain, weight, inside, row_in, inner),
            (field, field, lane_row), scratch=1, smem=(7,),
        )
        norm_now = norm_next
        curvature = all_sum(pa)
        if iteration + 1 < ITERS:
            solution, residual, rr = _call(
                _update_kernel, plan,
                (norm_now, curvature, solution, direction, residual, applied, inner),
                (field, field, lane_row),
            )

    grad_kappa, grad_weight = _call(
        _final_kernel, plan,
        (norm_now, curvature, solution, direction, z, stiff_probe, gain, stiff_obs, observed,
         variance_weight, diagonal),
        (out_plane, out_plane), scratch=1, field=field,
    )
    return (grad_kappa, grad_weight)


def solution(mesh):
    placed = (P(None, "rows", "cols"), P("rows", "cols"), P("rows", "cols"), P("rows", "cols"))
    return jax.shard_map(
        on_device,
        mesh=mesh,
        in_specs=placed,
        out_specs=(P("rows", "cols"), P("rows", "cols")),
        check_vma=False,
    )
```

```python
import jax
import jax.numpy as jnp
from jax import lax
from jax.experimental import pallas as pl
from jax.experimental.pallas import tpu as pltpu
from jax.sharding import PartitionSpec as P

ITERS = 3
HALO = 2 * ITERS


def extended(cells, sides, width):
    for axis, dim in sides:
        count = lax.axis_size(axis)
        ends = count - 1
        head = lax.slice_in_dim(cells, 0, width, axis=dim)
        tail = lax.slice_in_dim(cells, cells.shape[dim] - width, cells.shape[dim], axis=dim)
        below = lax.ppermute(tail.reshape(-1), axis, [(i, (i + 1) % count) for i in range(ends)])
        above = lax.ppermute(head.reshape(-1), axis, [((i + 1) % count, i) for i in range(ends)])
        cells = jnp.concatenate(
            [below.reshape(tail.shape), cells, above.reshape(head.shape)], axis=dim
        )
    return cells


def stencil(padded, kappa_sq):
    centre = padded[..., 1:-1, 1:-1]
    edge_sum = (
        padded[..., :-2, 1:-1]
        + padded[..., 2:, 1:-1]
        + padded[..., 1:-1, :-2]
        + padded[..., 1:-1, 2:]
    )
    corners = (
        padded[..., :-2, :-2] + padded[..., :-2, 2:] + padded[..., 2:, :-2] + padded[..., 2:, 2:]
    )
    return (kappa_sq + 20.0 / 6.0) * centre - (4.0 * edge_sum + corners) / 6.0


def stiffen(field, kappa_sq):
    pads = ((0, 0),) * (field.ndim - 2) + ((1, 1), (1, 1))
    return stencil(jnp.pad(field, pads), kappa_sq)


def all_sum(terms):
    for axis in ("cols", "rows"):
        count = lax.axis_size(axis)
        if count & (count - 1):
            terms = lax.psum(terms, axis)
            continue
        hop = 1
        while hop < count:
            terms = terms + lax.ppermute(terms, axis, [(i, i ^ hop) for i in range(count)])
            hop *= 2
    return terms


def _stiffen_row(ref, r, gain):
    mid = ref[r]
    vertical = ref[r - 1] + ref[r + 1]
    n = mid.shape[0]
    edge_sum = vertical + pltpu.roll(mid, 1, 0) + pltpu.roll(mid, n - 1, 0)
    corners = pltpu.roll(vertical, 1, 0) + pltpu.roll(vertical, n - 1, 0)
    return gain * mid - (4.0 * edge_sum + corners) * (1.0 / 6.0)


def _total(ref, row):
    value = ref[row : row + 1, :]
    return value + pltpu.roll(value, value.shape[1] // 2, 1)


def _ratio(num_ref, num_row, den_ref, den_row):
    return _total(num_ref, num_row) / _total(den_ref, den_row)


def _row_sum(value, keep):
    return jnp.sum(jnp.where(keep, value, 0.0), axis=0, keepdims=True)


class _Plan:
    def __init__(self, slab_rows, first_inner, inner_rows, half):
        self.half = half
        self.slab_rows = slab_rows
        self.first_inner = first_inner
        self.inner_rows = inner_rows

    def inner_row(self, r):
        return (r >= self.first_inner) & (r < self.first_inner + self.inner_rows)


def _zero_edges(ref):
    ref[0] = jnp.zeros(ref.shape[1:], ref.dtype)
    ref[ref.shape[0] - 1] = jnp.zeros(ref.shape[1:], ref.dtype)


def _apply_q(plan, source, gain_ref, weight_ref, inside_ref, row_ref, inner_ref, stiff_ref,
             applied_ref, dot_source):
    last = plan.slab_rows - 1
    _zero_edges(stiff_ref)
    _zero_edges(applied_ref)

    def first_pass(r, carry):
        stiff_ref[r] = weight_ref[r] * _stiffen_row(source, r, gain_ref[r])
        return carry

    lax.fori_loop(1, last, first_pass, 0)

    def second_pass(r, totals):
        applied = _stiffen_row(stiff_ref, r, gain_ref[r])
        keep = (inside_ref[...] > 0.5) & (row_ref[r] > 0.5)
        applied = jnp.where(keep, applied, 0.0)
        applied_ref[r] = applied
        inner = (inner_ref[...] > 0.5) & plan.inner_row(r)
        return totals + _row_sum(dot_source[r] * applied, inner)

    return lax.fori_loop(1, last, second_pass, jnp.zeros((1, source.shape[2]), jnp.float32))


def _spread(value, lane):
    return jnp.broadcast_to(value[:, lane : lane + 1], value.shape)


def _plane_row(value, diagonal):
    return jnp.sum(jnp.where(diagonal, value, 0.0), axis=0, keepdims=True)


def _first_kernel(plan, ext_ref, inside_ref, row_ref, inner_ref, diagonal_ref,
                  z_out, gain_out, weight_out, stiff_out, applied_out, dots_out, stiff_obs_out,
                  observed_scr, scratch):
    last = plan.slab_rows - 1
    sublanes = z_out.shape[1]
    lanes = z_out.shape[2]
    probes = lanes // 2

    def relayout(r, carry):
        cells = ext_ref[r]
        left = cells[0:sublanes]
        right = cells[plan.half : plan.half + sublanes]
        low = lax.broadcasted_iota(jnp.int32, (sublanes, lanes), 1) < probes
        z_out[r] = jnp.where(low, left, pltpu.roll(right, probes, 1))
        observed_scr[r] = jnp.where(low, _spread(left, probes), _spread(right, probes))
        gain_out[r] = jnp.where(low, _spread(left, probes + 1), _spread(right, probes + 1)) + 20.0 / 6.0
        weight_out[r] = jnp.where(low, _spread(left, probes + 2), _spread(right, probes + 2))
        return carry

    lax.fori_loop(0, plan.slab_rows, relayout, 0)
    _zero_edges(stiff_out)

    def probe_pass(r, totals):
        stiff_out[r] = _stiffen_row(z_out, r, gain_out[r])
        z = z_out[r]
        inner = (inner_ref[...] > 0.5) & plan.inner_row(r)
        return totals + _row_sum(z * z, inner)

    zz = lax.fori_loop(1, last, probe_pass, jnp.zeros((1, lanes), jnp.float32))
    _zero_edges(scratch)

    def weigh(r, carry):
        scratch[r] = weight_out[r] * stiff_out[r]
        return carry

    lax.fori_loop(1, last, weigh, 0)

    def second_pass(r, totals):
        applied = _stiffen_row(scratch, r, gain_out[r])
        keep = (inside_ref[...] > 0.5) & (row_ref[r] > 0.5)
        applied = jnp.where(keep, applied, 0.0)
        applied_out[r] = applied
        inner = (inner_ref[...] > 0.5) & plan.inner_row(r)
        return totals + _row_sum(z_out[r] * applied, inner)

    _zero_edges(applied_out)
    za = lax.fori_loop(1, last, second_pass, jnp.zeros((1, lanes), jnp.float32))
    dots_out[0:1, :] = zz
    dots_out[1:2, :] = za

    def observed_pass(r, carry):
        stiff_obs = _stiffen_row(observed_scr, plan.first_inner + r, gain_out[plan.first_inner + r])
        stiff_obs_out[pl.ds(r, 1), :] = _plane_row(stiff_obs, diagonal_ref[...] > 0.5)
        return carry

    lax.fori_loop(0, plan.inner_rows, observed_pass, 0)


def _start_kernel(plan, first_ref, z_ref, applied_ref, inner_ref, solution_out, residual_out, rr_out):
    step = _ratio(first_ref, 0, first_ref, 1)

    def body(r, totals):
        z = z_ref[r]
        residual = z - step * applied_ref[r]
        solution_out[r] = step * z
        residual_out[r] = residual
        inner = (inner_ref[...] > 0.5) & plan.inner_row(r)
        return totals + _row_sum(residual * residual, inner)

    rr_out[...] = lax.fori_loop(0, plan.slab_rows, body, jnp.zeros((1, z_ref.shape[2]), jnp.float32))


def _update_kernel(plan, norm_ref, curvature_ref, solution_ref, direction_ref, residual_ref,
                   applied_ref, inner_ref, solution_out, residual_out, rr_out):
    step = _ratio(norm_ref, 0, curvature_ref, 0)

    def body(r, totals):
        residual = residual_ref[r] - step * applied_ref[r]
        solution_out[r] = solution_ref[r] + step * direction_ref[r]
        residual_out[r] = residual
        inner = (inner_ref[...] > 0.5) & plan.inner_row(r)
        return totals + _row_sum(residual * residual, inner)

    rr_out[...] = lax.fori_loop(
        0, plan.slab_rows, body, jnp.zeros((1, residual_ref.shape[2]), jnp.float32)
    )


def _direction_kernel(plan, next_ref, now_ref, residual_ref, direction_ref, gain_ref, weight_ref,
                      inside_ref, row_ref, inner_ref, direction_out, applied_out, pa_out, scratch):
    beta = _ratio(next_ref, 0, now_ref, 0)

    def new_direction(r, carry):
        direction_out[r] = residual_ref[r] + beta * direction_ref[r]
        return carry

    lax.fori_loop(0, plan.slab_rows, new_direction, 0)
    pa_out[...] = _apply_q(plan, direction_out, gain_ref, weight_ref, inside_ref, row_ref, inner_ref,
                           scratch, applied_out, direction_out)


def _final_kernel(plan, norm_ref, curvature_ref, solution_ref, direction_ref, z_ref, stiff_ref,
                  gain_ref, stiff_obs_ref, observed_ref, weight_ref, diagonal_ref,
                  grad_kappa_out, grad_weight_out, scratch):
    step = _ratio(norm_ref, 0, curvature_ref, 0)
    lanes = z_ref.shape[2]
    probes = lanes // 2

    def new_solution(r, carry):
        scratch[r] = solution_ref[r] + step * direction_ref[r]
        return carry

    lax.fori_loop(0, plan.slab_rows, new_solution, 0)

    def probe_sum(value, low):
        first = jnp.sum(jnp.where(low, value, 0.0), axis=1, keepdims=True)
        second = jnp.sum(jnp.where(low, 0.0, value), axis=1, keepdims=True)
        return jnp.where(low, first, second)

    def body(i, carry):
        r = plan.first_inner + i
        solution = scratch[r]
        stiff_solution = _stiffen_row(scratch, r, gain_ref[r])
        stiff_probe = stiff_ref[r]
        low = lax.broadcasted_iota(jnp.int32, solution.shape, 1) < probes
        diagonal = diagonal_ref[...] > 0.5
        weight_total = _plane_row(probe_sum(stiff_solution * stiff_probe, low), diagonal)
        kappa_total = _plane_row(
            probe_sum(solution * stiff_probe + stiff_solution * z_ref[r], low), diagonal
        )
        stiff_obs = stiff_obs_ref[pl.ds(i, 1), :]
        observed = observed_ref[pl.ds(i, 1), :]
        weight = weight_ref[pl.ds(i, 1), :]
        grad_weight_out[pl.ds(i, 1), :] = (
            0.5 * weight_total / probes - 0.5 * stiff_obs * stiff_obs
        )
        grad_kappa_out[pl.ds(i, 1), :] = (
            0.5 * weight * (kappa_total / probes) - observed * weight * stiff_obs
        )
        return carry

    lax.fori_loop(0, plan.inner_rows, body, 0)


def _vmem():
    return pl.BlockSpec(memory_space=pltpu.VMEM)


def _call(kernel, plan, inputs, out_shapes, scratch=0, smem=(), field=None):
    field = out_shapes[0] if field is None else field
    nbytes = 4 * field.shape[0] * field.shape[1] * field.shape[2]
    in_specs = [
        pl.BlockSpec(memory_space=pltpu.SMEM) if i in smem else _vmem() for i in range(len(inputs))
    ]
    return pl.pallas_call(
        lambda *refs: kernel(plan, *refs),
        out_shape=out_shapes,
        in_specs=in_specs,
        out_specs=tuple(_vmem() for _ in out_shapes),
        scratch_shapes=[pltpu.VMEM(field.shape, jnp.float32)] * scratch,
        cost_estimate=pl.CostEstimate(
            flops=40 * nbytes // 4,
            transcendentals=0,
            bytes_accessed=(len(inputs) + len(out_shapes)) * nbytes,
        ),
    )(*inputs)


def on_device(probes, observed, kappa_sq, variance_weight):
    probe_count, rows, cols = probes.shape
    half = cols // 2
    assert rows >= HALO and cols % 2 == 0 and half >= HALO and half == probe_count
    width = half + 2 * HALO
    sublanes = -(-width // 8) * 8
    slab_rows = rows + 2 * HALO
    lanes = 2 * probe_count
    stacked = jnp.concatenate(
        [probes, observed[None], kappa_sq[None], variance_weight[None]], axis=0
    )
    ext = extended(stacked, (("rows", 1), ("cols", 2)), HALO)
    ext = jnp.pad(
        ext, ((0, lanes - ext.shape[0]), (0, 0), (0, half + sublanes - ext.shape[2]))
    )
    ext = jnp.transpose(ext, (1, 2, 0))

    row_at = lax.axis_index("rows") * rows - HALO + lax.iota(jnp.int32, slab_rows)
    row_in = ((row_at >= 0) & (row_at < rows * lax.axis_size("rows"))).astype(jnp.float32)
    col_in = []
    col_inner = []
    for h in range(2):
        at = lax.iota(jnp.int32, sublanes)
        col_at = lax.axis_index("cols") * cols - HALO + h * half + at
        col_in.append((col_at >= 0) & (col_at < cols * lax.axis_size("cols")) & (at < width))
        col_inner.append((at >= HALO) & (at < HALO + half))

    def on_lanes_of(columns):
        return jnp.concatenate(
            [jnp.broadcast_to(c[:, None], (sublanes, probe_count)) for c in columns], axis=1
        ).astype(jnp.float32)

    inside = on_lanes_of(col_in)
    inner = on_lanes_of(col_inner)
    lane_col = lax.iota(jnp.int32, lanes) % half + HALO
    diagonal = (lax.iota(jnp.int32, sublanes)[:, None] == lane_col[None, :]).astype(jnp.float32)
    plan = _Plan(slab_rows, HALO, rows, half)

    field = jax.ShapeDtypeStruct((slab_rows, sublanes, lanes), jnp.float32)
    lane_row = jax.ShapeDtypeStruct((1, lanes), jnp.float32)
    out_plane = jax.ShapeDtypeStruct((rows, cols), jnp.float32)

    z, gain, weight, stiff_probe, applied, first, stiff_obs = _call(
        _first_kernel, plan, (ext, inside, row_in, inner, diagonal),
        (field, field, field, field, field, jax.ShapeDtypeStruct((2, lanes), jnp.float32), out_plane),
        scratch=2, smem=(2,),
    )
    first = all_sum(first)
    solution, residual, rr = _call(
        _start_kernel, plan, (first, z, applied, inner), (field, field, lane_row)
    )
    direction = z
    norm_now = first
    for iteration in range(1, ITERS):
        norm_next = all_sum(rr)
        direction, applied, pa = _call(
            _direction_kernel, plan,
            (norm_next, norm_now, residual, direction, gain, weight, inside, row_in, inner),
            (field, field, lane_row), scratch=1, smem=(7,),
        )
        norm_now = norm_next
        curvature = all_sum(pa)
        if iteration + 1 < ITERS:
            solution, residual, rr = _call(
                _update_kernel, plan,
                (norm_now, curvature, solution, direction, residual, applied, inner),
                (field, field, lane_row),
            )

    grad_kappa, grad_weight = _call(
        _final_kernel, plan,
        (norm_now, curvature, solution, direction, z, stiff_probe, gain, stiff_obs, observed,
         variance_weight, diagonal),
        (out_plane, out_plane), scratch=1, field=field,
    )
    return (grad_kappa, grad_weight)


def solution(mesh):
    placed = (P(None, "rows", "cols"), P("rows", "cols"), P("rows", "cols"), P("rows", "cols"))
    return jax.shard_map(
        on_device,
        mesh=mesh,
        in_specs=placed,
        out_specs=(P("rows", "cols"), P("rows", "cols")),
        check_vma=False,
    )
```

```python
import jax
import jax.numpy as jnp
from jax import lax
from jax.experimental import pallas as pl
from jax.experimental.pallas import tpu as pltpu
from jax.sharding import PartitionSpec as P

ITERS = 3
HALO = 2 * ITERS


def extended(cells, sides, width):
    for axis, dim in sides:
        count = lax.axis_size(axis)
        ends = count - 1
        head = lax.slice_in_dim(cells, 0, width, axis=dim)
        tail = lax.slice_in_dim(cells, cells.shape[dim] - width, cells.shape[dim], axis=dim)
        cells = jnp.concatenate(
            [
                lax.ppermute(tail, axis, [(i, (i + 1) % count) for i in range(ends)]),
                cells,
                lax.ppermute(head, axis, [((i + 1) % count, i) for i in range(ends)]),
            ],
            axis=dim,
        )
    return cells


def stencil(padded, kappa_sq):
    centre = padded[..., 1:-1, 1:-1]
    edge_sum = (
        padded[..., :-2, 1:-1]
        + padded[..., 2:, 1:-1]
        + padded[..., 1:-1, :-2]
        + padded[..., 1:-1, 2:]
    )
    corners = (
        padded[..., :-2, :-2] + padded[..., :-2, 2:] + padded[..., 2:, :-2] + padded[..., 2:, 2:]
    )
    return (kappa_sq + 20.0 / 6.0) * centre - (4.0 * edge_sum + corners) / 6.0


def stiffen(field, kappa_sq):
    pads = ((0, 0),) * (field.ndim - 2) + ((1, 1), (1, 1))
    return stencil(jnp.pad(field, pads), kappa_sq)


def all_sum(terms):
    for axis in ("cols", "rows"):
        count = lax.axis_size(axis)
        if count & (count - 1):
            terms = lax.psum(terms, axis)
            continue
        hop = 1
        while hop < count:
            terms = terms + lax.ppermute(terms, axis, [(i, i ^ hop) for i in range(count)])
            hop *= 2
    return terms


def _stiffen_row(ref, r, gain):
    mid = ref[r]
    vertical = ref[r - 1] + ref[r + 1]
    n = mid.shape[0]
    edge_sum = vertical + pltpu.roll(mid, 1, 0) + pltpu.roll(mid, n - 1, 0)
    corners = pltpu.roll(vertical, 1, 0) + pltpu.roll(vertical, n - 1, 0)
    return gain * mid - (4.0 * edge_sum + corners) * (1.0 / 6.0)


def _total(ref, row):
    value = ref[row : row + 1, :]
    return value + pltpu.roll(value, value.shape[1] // 2, 1)


def _ratio(num_ref, num_row, den_ref, den_row):
    return _total(num_ref, num_row) / _total(den_ref, den_row)


def _row_sum(value, keep):
    return jnp.sum(jnp.where(keep, value, 0.0), axis=0, keepdims=True)


class _Plan:
    def __init__(self, slab_rows, first_inner, inner_rows, half):
        self.half = half
        self.slab_rows = slab_rows
        self.first_inner = first_inner
        self.inner_rows = inner_rows

    def inner_row(self, r):
        return (r >= self.first_inner) & (r < self.first_inner + self.inner_rows)


def _zero_edges(ref):
    ref[0] = jnp.zeros(ref.shape[1:], ref.dtype)
    ref[ref.shape[0] - 1] = jnp.zeros(ref.shape[1:], ref.dtype)


def _apply_q(plan, source, gain_ref, weight_ref, inside_ref, row_ref, inner_ref, stiff_ref,
             applied_ref, dot_source):
    last = plan.slab_rows - 1
    _zero_edges(stiff_ref)
    _zero_edges(applied_ref)

    def first_pass(r, carry):
        stiff_ref[r] = weight_ref[r] * _stiffen_row(source, r, gain_ref[r])
        return carry

    lax.fori_loop(1, last, first_pass, 0)

    def second_pass(r, totals):
        applied = _stiffen_row(stiff_ref, r, gain_ref[r])
        keep = (inside_ref[...] > 0.5) & (row_ref[r] > 0.5)
        applied = jnp.where(keep, applied, 0.0)
        applied_ref[r] = applied
        inner = (inner_ref[...] > 0.5) & plan.inner_row(r)
        return totals + _row_sum(dot_source[r] * applied, inner)

    return lax.fori_loop(1, last, second_pass, jnp.zeros((1, source.shape[2]), jnp.float32))


def _spread(value, lane):
    return jnp.broadcast_to(value[:, lane : lane + 1], value.shape)


def _plane_row(value, diagonal):
    return jnp.sum(jnp.where(diagonal, value, 0.0), axis=0, keepdims=True)


def _first_kernel(plan, ext_ref, inside_ref, row_ref, inner_ref, diagonal_ref,
                  z_out, gain_out, weight_out, stiff_out, applied_out, dots_out, stiff_obs_out,
                  observed_scr, scratch):
    last = plan.slab_rows - 1
    sublanes = z_out.shape[1]
    lanes = z_out.shape[2]
    probes = lanes // 2

    def relayout(r, carry):
        cells = ext_ref[r]
        left = cells[0:sublanes]
        right = cells[plan.half : plan.half + sublanes]
        low = lax.broadcasted_iota(jnp.int32, (sublanes, lanes), 1) < probes
        z_out[r] = jnp.where(low, left, pltpu.roll(right, probes, 1))
        observed_scr[r] = jnp.where(low, _spread(left, probes), _spread(right, probes))
        gain_out[r] = jnp.where(low, _spread(left, probes + 1), _spread(right, probes + 1)) + 20.0 / 6.0
        weight_out[r] = jnp.where(low, _spread(left, probes + 2), _spread(right, probes + 2))
        return carry

    lax.fori_loop(0, plan.slab_rows, relayout, 0)
    _zero_edges(stiff_out)

    def probe_pass(r, totals):
        stiff_out[r] = _stiffen_row(z_out, r, gain_out[r])
        z = z_out[r]
        inner = (inner_ref[...] > 0.5) & plan.inner_row(r)
        return totals + _row_sum(z * z, inner)

    zz = lax.fori_loop(1, last, probe_pass, jnp.zeros((1, lanes), jnp.float32))
    _zero_edges(scratch)

    def weigh(r, carry):
        scratch[r] = weight_out[r] * stiff_out[r]
        return carry

    lax.fori_loop(1, last, weigh, 0)

    def second_pass(r, totals):
        applied = _stiffen_row(scratch, r, gain_out[r])
        keep = (inside_ref[...] > 0.5) & (row_ref[r] > 0.5)
        applied = jnp.where(keep, applied, 0.0)
        applied_out[r] = applied
        inner = (inner_ref[...] > 0.5) & plan.inner_row(r)
        return totals + _row_sum(z_out[r] * applied, inner)

    _zero_edges(applied_out)
    za = lax.fori_loop(1, last, second_pass, jnp.zeros((1, lanes), jnp.float32))
    dots_out[0:1, :] = zz
    dots_out[1:2, :] = za

    def observed_pass(r, carry):
        stiff_obs = _stiffen_row(observed_scr, plan.first_inner + r, gain_out[plan.first_inner + r])
        stiff_obs_out[pl.ds(r, 1), :] = _plane_row(stiff_obs, diagonal_ref[...] > 0.5)
        return carry

    lax.fori_loop(0, plan.inner_rows, observed_pass, 0)


def _start_kernel(plan, first_ref, z_ref, applied_ref, inner_ref, solution_out, residual_out, rr_out):
    step = _ratio(first_ref, 0, first_ref, 1)

    def body(r, totals):
        z = z_ref[r]
        residual = z - step * applied_ref[r]
        solution_out[r] = step * z
        residual_out[r] = residual
        inner = (inner_ref[...] > 0.5) & plan.inner_row(r)
        return totals + _row_sum(residual * residual, inner)

    rr_out[...] = lax.fori_loop(0, plan.slab_rows, body, jnp.zeros((1, z_ref.shape[2]), jnp.float32))


def _update_kernel(plan, norm_ref, curvature_ref, solution_ref, direction_ref, residual_ref,
                   applied_ref, inner_ref, solution_out, residual_out, rr_out):
    step = _ratio(norm_ref, 0, curvature_ref, 0)

    def body(r, totals):
        residual = residual_ref[r] - step * applied_ref[r]
        solution_out[r] = solution_ref[r] + step * direction_ref[r]
        residual_out[r] = residual
        inner = (inner_ref[...] > 0.5) & plan.inner_row(r)
        return totals + _row_sum(residual * residual, inner)

    rr_out[...] = lax.fori_loop(
        0, plan.slab_rows, body, jnp.zeros((1, residual_ref.shape[2]), jnp.float32)
    )


def _direction_kernel(plan, next_ref, now_ref, residual_ref, direction_ref, gain_ref, weight_ref,
                      inside_ref, row_ref, inner_ref, direction_out, applied_out, pa_out, scratch):
    beta = _ratio(next_ref, 0, now_ref, 0)

    def new_direction(r, carry):
        direction_out[r] = residual_ref[r] + beta * direction_ref[r]
        return carry

    lax.fori_loop(0, plan.slab_rows, new_direction, 0)
    pa_out[...] = _apply_q(plan, direction_out, gain_ref, weight_ref, inside_ref, row_ref, inner_ref,
                           scratch, applied_out, direction_out)


def _final_kernel(plan, norm_ref, curvature_ref, solution_ref, direction_ref, z_ref, stiff_ref,
                  gain_ref, stiff_obs_ref, observed_ref, weight_ref, diagonal_ref,
                  grad_kappa_out, grad_weight_out, scratch):
    step = _ratio(norm_ref, 0, curvature_ref, 0)
    lanes = z_ref.shape[2]
    probes = lanes // 2

    def new_solution(r, carry):
        scratch[r] = solution_ref[r] + step * direction_ref[r]
        return carry

    lax.fori_loop(0, plan.slab_rows, new_solution, 0)

    def probe_sum(value, low):
        first = jnp.sum(jnp.where(low, value, 0.0), axis=1, keepdims=True)
        second = jnp.sum(jnp.where(low, 0.0, value), axis=1, keepdims=True)
        return jnp.where(low, first, second)

    def body(i, carry):
        r = plan.first_inner + i
        solution = scratch[r]
        stiff_solution = _stiffen_row(scratch, r, gain_ref[r])
        stiff_probe = stiff_ref[r]
        low = lax.broadcasted_iota(jnp.int32, solution.shape, 1) < probes
        diagonal = diagonal_ref[...] > 0.5
        weight_total = _plane_row(probe_sum(stiff_solution * stiff_probe, low), diagonal)
        kappa_total = _plane_row(
            probe_sum(solution * stiff_probe + stiff_solution * z_ref[r], low), diagonal
        )
        stiff_obs = stiff_obs_ref[pl.ds(i, 1), :]
        observed = observed_ref[pl.ds(i, 1), :]
        weight = weight_ref[pl.ds(i, 1), :]
        grad_weight_out[pl.ds(i, 1), :] = (
            0.5 * weight_total / probes - 0.5 * stiff_obs * stiff_obs
        )
        grad_kappa_out[pl.ds(i, 1), :] = (
            0.5 * weight * (kappa_total / probes) - observed * weight * stiff_obs
        )
        return carry

    lax.fori_loop(0, plan.inner_rows, body, 0)


def _vmem():
    return pl.BlockSpec(memory_space=pltpu.VMEM)


def _call(kernel, plan, inputs, out_shapes, scratch=0, smem=(), field=None):
    field = out_shapes[0] if field is None else field
    nbytes = 4 * field.shape[0] * field.shape[1] * field.shape[2]
    in_specs = [
        pl.BlockSpec(memory_space=pltpu.SMEM) if i in smem else _vmem() for i in range(len(inputs))
    ]
    return pl.pallas_call(
        lambda *refs: kernel(plan, *refs),
        out_shape=out_shapes,
        in_specs=in_specs,
        out_specs=tuple(_vmem() for _ in out_shapes),
        scratch_shapes=[pltpu.VMEM(field.shape, jnp.float32)] * scratch,
        cost_estimate=pl.CostEstimate(
            flops=40 * nbytes // 4,
            transcendentals=0,
            bytes_accessed=(len(inputs) + len(out_shapes)) * nbytes,
        ),
    )(*inputs)


def on_device(probes, observed, kappa_sq, variance_weight):
    probe_count, rows, cols = probes.shape
    half = cols // 2
    assert rows >= HALO and cols % 2 == 0 and half >= HALO and half == probe_count
    width = half + 2 * HALO
    sublanes = -(-width // 8) * 8
    slab_rows = rows + 2 * HALO
    lanes = 2 * probe_count
    stacked = jnp.concatenate(
        [probes, observed[None], kappa_sq[None], variance_weight[None]], axis=0
    )
    count = lax.axis_size("rows")
    sent = -(-HALO // 8) * 8
    assert sent <= rows
    planes = stacked.shape[0]
    below = lax.ppermute(
        stacked[:, rows - sent :].reshape(planes * sent, cols), "rows",
        [(i, i + 1) for i in range(count - 1)],
    ).reshape(planes, sent, cols)[:, sent - HALO :]
    above = lax.ppermute(
        stacked[:, :sent].reshape(planes * sent, cols), "rows",
        [(i + 1, i) for i in range(count - 1)],
    ).reshape(planes, sent, cols)[:, :HALO]
    ext = jnp.concatenate(
        [jnp.transpose(piece, (1, 2, 0)) for piece in (below, stacked, above)], axis=0
    )
    ext = extended(ext, (("cols", 1),), HALO)
    ext = jnp.pad(
        ext, ((0, 0), (0, half + sublanes - ext.shape[1]), (0, lanes - ext.shape[2]))
    )

    row_at = lax.axis_index("rows") * rows - HALO + lax.iota(jnp.int32, slab_rows)
    row_in = ((row_at >= 0) & (row_at < rows * lax.axis_size("rows"))).astype(jnp.float32)
    col_in = []
    col_inner = []
    for h in range(2):
        at = lax.iota(jnp.int32, sublanes)
        col_at = lax.axis_index("cols") * cols - HALO + h * half + at
        col_in.append((col_at >= 0) & (col_at < cols * lax.axis_size("cols")) & (at < width))
        col_inner.append((at >= HALO) & (at < HALO + half))

    def on_lanes_of(columns):
        return jnp.concatenate(
            [jnp.broadcast_to(c[:, None], (sublanes, probe_count)) for c in columns], axis=1
        ).astype(jnp.float32)

    inside = on_lanes_of(col_in)
    inner = on_lanes_of(col_inner)
    lane_col = lax.iota(jnp.int32, lanes) % half + HALO
    diagonal = (lax.iota(jnp.int32, sublanes)[:, None] == lane_col[None, :]).astype(jnp.float32)
    plan = _Plan(slab_rows, HALO, rows, half)

    field = jax.ShapeDtypeStruct((slab_rows, sublanes, lanes), jnp.float32)
    lane_row = jax.ShapeDtypeStruct((1, lanes), jnp.float32)
    out_plane = jax.ShapeDtypeStruct((rows, cols), jnp.float32)

    z, gain, weight, stiff_probe, applied, first, stiff_obs = _call(
        _first_kernel, plan, (ext, inside, row_in, inner, diagonal),
        (field, field, field, field, field, jax.ShapeDtypeStruct((2, lanes), jnp.float32), out_plane),
        scratch=2, smem=(2,),
    )
    first = all_sum(first)
    solution, residual, rr = _call(
        _start_kernel, plan, (first, z, applied, inner), (field, field, lane_row)
    )
    direction = z
    norm_now = first
    for iteration in range(1, ITERS):
        norm_next = all_sum(rr)
        direction, applied, pa = _call(
            _direction_kernel, plan,
            (norm_next, norm_now, residual, direction, gain, weight, inside, row_in, inner),
            (field, field, lane_row), scratch=1, smem=(7,),
        )
        norm_now = norm_next
        curvature = all_sum(pa)
        if iteration + 1 < ITERS:
            solution, residual, rr = _call(
                _update_kernel, plan,
                (norm_now, curvature, solution, direction, residual, applied, inner),
                (field, field, lane_row),
            )

    grad_kappa, grad_weight = _call(
        _final_kernel, plan,
        (norm_now, curvature, solution, direction, z, stiff_probe, gain, stiff_obs, observed,
         variance_weight, diagonal),
        (out_plane, out_plane), scratch=1, field=field,
    )
    return (grad_kappa, grad_weight)


def solution(mesh):
    placed = (P(None, "rows", "cols"), P("rows", "cols"), P("rows", "cols"), P("rows", "cols"))
    return jax.shard_map(
        on_device,
        mesh=mesh,
        in_specs=placed,
        out_specs=(P("rows", "cols"), P("rows", "cols")),
        check_vma=False,
    )
```

```python
import jax
import jax.numpy as jnp
from jax import lax
from jax.experimental import pallas as pl
from jax.experimental.pallas import tpu as pltpu
from jax.sharding import PartitionSpec as P

ITERS = 3
HALO = 2 * ITERS


def extended(cells, sides, width):
    for axis, dim in sides:
        count = lax.axis_size(axis)
        ends = count - 1
        head = lax.slice_in_dim(cells, 0, width, axis=dim)
        tail = lax.slice_in_dim(cells, cells.shape[dim] - width, cells.shape[dim], axis=dim)
        cells = jnp.concatenate(
            [
                lax.ppermute(tail, axis, [(i, (i + 1) % count) for i in range(ends)]),
                cells,
                lax.ppermute(head, axis, [((i + 1) % count, i) for i in range(ends)]),
            ],
            axis=dim,
        )
    return cells


def stencil(padded, kappa_sq):
    centre = padded[..., 1:-1, 1:-1]
    edge_sum = (
        padded[..., :-2, 1:-1]
        + padded[..., 2:, 1:-1]
        + padded[..., 1:-1, :-2]
        + padded[..., 1:-1, 2:]
    )
    corners = (
        padded[..., :-2, :-2] + padded[..., :-2, 2:] + padded[..., 2:, :-2] + padded[..., 2:, 2:]
    )
    return (kappa_sq + 20.0 / 6.0) * centre - (4.0 * edge_sum + corners) / 6.0


def stiffen(field, kappa_sq):
    pads = ((0, 0),) * (field.ndim - 2) + ((1, 1), (1, 1))
    return stencil(jnp.pad(field, pads), kappa_sq)


def all_sum(terms):
    for axis in ("cols", "rows"):
        count = lax.axis_size(axis)
        if count & (count - 1):
            terms = lax.psum(terms, axis)
            continue
        hop = 1
        while hop < count:
            terms = terms + lax.ppermute(terms, axis, [(i, i ^ hop) for i in range(count)])
            hop *= 2
    return terms


def _stiffen_row(ref, r, gain):
    mid = ref[r]
    vertical = ref[r - 1] + ref[r + 1]
    n = mid.shape[0]
    edge_sum = vertical + pltpu.roll(mid, 1, 0) + pltpu.roll(mid, n - 1, 0)
    corners = pltpu.roll(vertical, 1, 0) + pltpu.roll(vertical, n - 1, 0)
    return gain * mid - (4.0 * edge_sum + corners) * (1.0 / 6.0)


def _total(ref, row):
    value = ref[row : row + 1, :]
    return value + pltpu.roll(value, value.shape[1] // 2, 1)


def _ratio(num_ref, num_row, den_ref, den_row):
    return _total(num_ref, num_row) / _total(den_ref, den_row)


def _row_sum(value, keep):
    return jnp.sum(jnp.where(keep, value, 0.0), axis=0, keepdims=True)


class _Plan:
    def __init__(self, slab_rows, first_inner, inner_rows, half):
        self.half = half
        self.slab_rows = slab_rows
        self.first_inner = first_inner
        self.inner_rows = inner_rows

    def inner_row(self, r):
        return (r >= self.first_inner) & (r < self.first_inner + self.inner_rows)


def _zero_edges(ref):
    ref[0] = jnp.zeros(ref.shape[1:], ref.dtype)
    ref[ref.shape[0] - 1] = jnp.zeros(ref.shape[1:], ref.dtype)


def _apply_q(plan, source, gain_ref, weight_ref, inside_ref, row_ref, inner_ref, stiff_ref,
             applied_ref, dot_source):
    last = plan.slab_rows - 1
    _zero_edges(stiff_ref)
    _zero_edges(applied_ref)

    def first_pass(r, carry):
        stiff_ref[r] = weight_ref[r] * _stiffen_row(source, r, gain_ref[r])
        return carry

    lax.fori_loop(1, last, first_pass, 0)

    def second_pass(r, totals):
        applied = _stiffen_row(stiff_ref, r, gain_ref[r])
        keep = (inside_ref[...] > 0.5) & (row_ref[r] > 0.5)
        applied = jnp.where(keep, applied, 0.0)
        applied_ref[r] = applied
        inner = (inner_ref[...] > 0.5) & plan.inner_row(r)
        return totals + _row_sum(dot_source[r] * applied, inner)

    return lax.fori_loop(1, last, second_pass, jnp.zeros((1, source.shape[2]), jnp.float32))


def _spread(value, lane):
    return jnp.broadcast_to(value[:, lane : lane + 1], value.shape)


def _plane_row(value, diagonal):
    return jnp.sum(jnp.where(diagonal, value, 0.0), axis=0, keepdims=True)


def _first_kernel(plan, ext_ref, inside_ref, row_ref, inner_ref, diagonal_ref,
                  z_out, gain_out, weight_out, stiff_out, applied_out, dots_out, stiff_obs_out,
                  observed_scr, scratch):
    last = plan.slab_rows - 1
    sublanes = z_out.shape[1]
    lanes = z_out.shape[2]
    probes = lanes // 2

    def relayout(r, carry):
        cells = ext_ref[r]
        left = cells[0:sublanes]
        right = cells[plan.half : plan.half + sublanes]
        low = lax.broadcasted_iota(jnp.int32, (sublanes, lanes), 1) < probes
        z_out[r] = jnp.where(low, left, pltpu.roll(right, probes, 1))
        observed_scr[r] = jnp.where(low, _spread(left, probes), _spread(right, probes))
        gain_out[r] = jnp.where(low, _spread(left, probes + 1), _spread(right, probes + 1)) + 20.0 / 6.0
        weight_out[r] = jnp.where(low, _spread(left, probes + 2), _spread(right, probes + 2))
        return carry

    lax.fori_loop(0, plan.slab_rows, relayout, 0)
    _zero_edges(stiff_out)

    def probe_pass(r, totals):
        stiff_out[r] = _stiffen_row(z_out, r, gain_out[r])
        z = z_out[r]
        inner = (inner_ref[...] > 0.5) & plan.inner_row(r)
        return totals + _row_sum(z * z, inner)

    zz = lax.fori_loop(1, last, probe_pass, jnp.zeros((1, lanes), jnp.float32))
    _zero_edges(scratch)

    def weigh(r, carry):
        scratch[r] = weight_out[r] * stiff_out[r]
        return carry

    lax.fori_loop(1, last, weigh, 0)

    def second_pass(r, totals):
        applied = _stiffen_row(scratch, r, gain_out[r])
        keep = (inside_ref[...] > 0.5) & (row_ref[r] > 0.5)
        applied = jnp.where(keep, applied, 0.0)
        applied_out[r] = applied
        inner = (inner_ref[...] > 0.5) & plan.inner_row(r)
        return totals + _row_sum(z_out[r] * applied, inner)

    _zero_edges(applied_out)
    za = lax.fori_loop(1, last, second_pass, jnp.zeros((1, lanes), jnp.float32))
    dots_out[0:1, :] = zz
    dots_out[1:2, :] = za

    def observed_pass(r, carry):
        stiff_obs = _stiffen_row(observed_scr, plan.first_inner + r, gain_out[plan.first_inner + r])
        stiff_obs_out[pl.ds(r, 1), :] = _plane_row(stiff_obs, diagonal_ref[...] > 0.5)
        return carry

    lax.fori_loop(0, plan.inner_rows, observed_pass, 0)


def _start_kernel(plan, first_ref, z_ref, applied_ref, inner_ref, residual_out, rr_out):
    step = _ratio(first_ref, 0, first_ref, 1)

    def body(r, totals):
        residual = z_ref[r] - step * applied_ref[r]
        residual_out[r] = residual
        inner = (inner_ref[...] > 0.5) & plan.inner_row(r)
        return totals + _row_sum(residual * residual, inner)

    rr_out[...] = lax.fori_loop(0, plan.slab_rows, body, jnp.zeros((1, z_ref.shape[2]), jnp.float32))


def _update_kernel(plan, norm_ref, curvature_ref, residual_ref, applied_ref, inner_ref,
                   residual_out, rr_out):
    step = _ratio(norm_ref, 0, curvature_ref, 0)

    def body(r, totals):
        residual = residual_ref[r] - step * applied_ref[r]
        residual_out[r] = residual
        inner = (inner_ref[...] > 0.5) & plan.inner_row(r)
        return totals + _row_sum(residual * residual, inner)

    rr_out[...] = lax.fori_loop(
        0, plan.slab_rows, body, jnp.zeros((1, residual_ref.shape[2]), jnp.float32)
    )


def _direction_kernel(plan, next_ref, now_ref, residual_ref, direction_ref, gain_ref, weight_ref,
                      inside_ref, row_ref, inner_ref, direction_out, applied_out, pa_out, scratch):
    beta = _ratio(next_ref, 0, now_ref, 0)

    def new_direction(r, carry):
        direction_out[r] = residual_ref[r] + beta * direction_ref[r]
        return carry

    lax.fori_loop(0, plan.slab_rows, new_direction, 0)
    pa_out[...] = _apply_q(plan, direction_out, gain_ref, weight_ref, inside_ref, row_ref, inner_ref,
                           scratch, applied_out, direction_out)


def _final_kernel(plan, *refs):
    steps = ITERS
    ratio_refs = refs[: 2 * steps]
    direction_refs = refs[2 * steps : 3 * steps]
    (z_ref, stiff_ref, gain_ref, stiff_obs_ref, observed_ref, weight_ref, diagonal_ref,
     grad_kappa_out, grad_weight_out, scratch) = refs[3 * steps :]
    lanes = z_ref.shape[2]
    probes = lanes // 2
    step_lens = []
    for k in range(steps):
        num_ref, den_ref = ratio_refs[2 * k], ratio_refs[2 * k + 1]
        step_lens.append(_ratio(num_ref, 0, den_ref, 1 if k == 0 else 0))

    def new_solution(r, carry):
        solution = step_lens[0] * direction_refs[0][r]
        for k in range(1, steps):
            solution = solution + step_lens[k] * direction_refs[k][r]
        scratch[r] = solution
        return carry

    lax.fori_loop(0, plan.slab_rows, new_solution, 0)

    def probe_sum(value, low):
        first = jnp.sum(jnp.where(low, value, 0.0), axis=1, keepdims=True)
        second = jnp.sum(jnp.where(low, 0.0, value), axis=1, keepdims=True)
        return jnp.where(low, first, second)

    def body(i, carry):
        r = plan.first_inner + i
        solution = scratch[r]
        stiff_solution = _stiffen_row(scratch, r, gain_ref[r])
        stiff_probe = stiff_ref[r]
        low = lax.broadcasted_iota(jnp.int32, solution.shape, 1) < probes
        diagonal = diagonal_ref[...] > 0.5
        weight_total = _plane_row(probe_sum(stiff_solution * stiff_probe, low), diagonal)
        kappa_total = _plane_row(
            probe_sum(solution * stiff_probe + stiff_solution * z_ref[r], low), diagonal
        )
        stiff_obs = stiff_obs_ref[pl.ds(i, 1), :]
        observed = observed_ref[pl.ds(i, 1), :]
        weight = weight_ref[pl.ds(i, 1), :]
        grad_weight_out[pl.ds(i, 1), :] = (
            0.5 * weight_total / probes - 0.5 * stiff_obs * stiff_obs
        )
        grad_kappa_out[pl.ds(i, 1), :] = (
            0.5 * weight * (kappa_total / probes) - observed * weight * stiff_obs
        )
        return carry

    lax.fori_loop(0, plan.inner_rows, body, 0)


def _vmem():
    return pl.BlockSpec(memory_space=pltpu.VMEM)


def _call(kernel, plan, inputs, out_shapes, scratch=0, smem=(), field=None):
    field = out_shapes[0] if field is None else field
    nbytes = 4 * field.shape[0] * field.shape[1] * field.shape[2]
    in_specs = [
        pl.BlockSpec(memory_space=pltpu.SMEM) if i in smem else _vmem() for i in range(len(inputs))
    ]
    return pl.pallas_call(
        lambda *refs: kernel(plan, *refs),
        out_shape=out_shapes,
        in_specs=in_specs,
        out_specs=tuple(_vmem() for _ in out_shapes),
        scratch_shapes=[pltpu.VMEM(field.shape, jnp.float32)] * scratch,
        cost_estimate=pl.CostEstimate(
            flops=40 * nbytes // 4,
            transcendentals=0,
            bytes_accessed=(len(inputs) + len(out_shapes)) * nbytes,
        ),
    )(*inputs)


def on_device(probes, observed, kappa_sq, variance_weight):
    probe_count, rows, cols = probes.shape
    half = cols // 2
    assert rows >= HALO and cols % 2 == 0 and half >= HALO and half == probe_count
    width = half + 2 * HALO
    sublanes = -(-width // 8) * 8
    slab_rows = rows + 2 * HALO
    lanes = 2 * probe_count
    stacked = jnp.concatenate(
        [probes, observed[None], kappa_sq[None], variance_weight[None]], axis=0
    )
    count = lax.axis_size("rows")
    sent = -(-HALO // 8) * 8
    assert sent <= rows
    planes = stacked.shape[0]
    below = lax.ppermute(
        stacked[:, rows - sent :].reshape(planes * sent, cols), "rows",
        [(i, i + 1) for i in range(count - 1)],
    ).reshape(planes, sent, cols)[:, sent - HALO :]
    above = lax.ppermute(
        stacked[:, :sent].reshape(planes * sent, cols), "rows",
        [(i + 1, i) for i in range(count - 1)],
    ).reshape(planes, sent, cols)[:, :HALO]
    ext = jnp.concatenate(
        [jnp.transpose(piece, (1, 2, 0)) for piece in (below, stacked, above)], axis=0
    )
    ext = extended(ext, (("cols", 1),), HALO)
    ext = jnp.pad(
        ext, ((0, 0), (0, half + sublanes - ext.shape[1]), (0, lanes - ext.shape[2]))
    )

    row_at = lax.axis_index("rows") * rows - HALO + lax.iota(jnp.int32, slab_rows)
    row_in = ((row_at >= 0) & (row_at < rows * lax.axis_size("rows"))).astype(jnp.float32)
    col_in = []
    col_inner = []
    for h in range(2):
        at = lax.iota(jnp.int32, sublanes)
        col_at = lax.axis_index("cols") * cols - HALO + h * half + at
        col_in.append((col_at >= 0) & (col_at < cols * lax.axis_size("cols")) & (at < width))
        col_inner.append((at >= HALO) & (at < HALO + half))

    def on_lanes_of(columns):
        return jnp.concatenate(
            [jnp.broadcast_to(c[:, None], (sublanes, probe_count)) for c in columns], axis=1
        ).astype(jnp.float32)

    inside = on_lanes_of(col_in)
    inner = on_lanes_of(col_inner)
    lane_col = lax.iota(jnp.int32, lanes) % half + HALO
    diagonal = (lax.iota(jnp.int32, sublanes)[:, None] == lane_col[None, :]).astype(jnp.float32)
    plan = _Plan(slab_rows, HALO, rows, half)

    field = jax.ShapeDtypeStruct((slab_rows, sublanes, lanes), jnp.float32)
    lane_row = jax.ShapeDtypeStruct((1, lanes), jnp.float32)
    out_plane = jax.ShapeDtypeStruct((rows, cols), jnp.float32)

    z, gain, weight, stiff_probe, applied, first, stiff_obs = _call(
        _first_kernel, plan, (ext, inside, row_in, inner, diagonal),
        (field, field, field, field, field, jax.ShapeDtypeStruct((2, lanes), jnp.float32), out_plane),
        scratch=2, smem=(2,),
    )
    first = all_sum(first)
    residual, rr = _call(_start_kernel, plan, (first, z, applied, inner), (field, lane_row))
    directions = [z]
    ratios = [first, first]
    direction = z
    norm_now = first
    for iteration in range(1, ITERS):
        norm_next = all_sum(rr)
        direction, applied, pa = _call(
            _direction_kernel, plan,
            (norm_next, norm_now, residual, direction, gain, weight, inside, row_in, inner),
            (field, field, lane_row), scratch=1, smem=(7,),
        )
        norm_now = norm_next
        curvature = all_sum(pa)
        directions.append(direction)
        ratios += [norm_now, curvature]
        if iteration + 1 < ITERS:
            residual, rr = _call(
                _update_kernel, plan, (norm_now, curvature, residual, applied, inner),
                (field, lane_row),
            )

    grad_kappa, grad_weight = _call(
        _final_kernel, plan,
        (*ratios, *directions, z, stiff_probe, gain, stiff_obs, observed, variance_weight, diagonal),
        (out_plane, out_plane), scratch=1, field=field,
    )
    return (grad_kappa, grad_weight)


def solution(mesh):
    placed = (P(None, "rows", "cols"), P("rows", "cols"), P("rows", "cols"), P("rows", "cols"))
    return jax.shard_map(
        on_device,
        mesh=mesh,
        in_specs=placed,
        out_specs=(P("rows", "cols"), P("rows", "cols")),
        check_vma=False,
    )
```

```python
import jax
import jax.numpy as jnp
from jax import lax
from jax.experimental import pallas as pl
from jax.experimental.pallas import tpu as pltpu
from jax.sharding import PartitionSpec as P

ITERS = 3
HALO = 2 * ITERS


def extended(cells, sides, width):
    for axis, dim in sides:
        count = lax.axis_size(axis)
        ends = count - 1
        head = lax.slice_in_dim(cells, 0, width, axis=dim)
        tail = lax.slice_in_dim(cells, cells.shape[dim] - width, cells.shape[dim], axis=dim)
        cells = jnp.concatenate(
            [
                lax.ppermute(tail, axis, [(i, (i + 1) % count) for i in range(ends)]),
                cells,
                lax.ppermute(head, axis, [((i + 1) % count, i) for i in range(ends)]),
            ],
            axis=dim,
        )
    return cells


def stencil(padded, kappa_sq):
    centre = padded[..., 1:-1, 1:-1]
    edge_sum = (
        padded[..., :-2, 1:-1]
        + padded[..., 2:, 1:-1]
        + padded[..., 1:-1, :-2]
        + padded[..., 1:-1, 2:]
    )
    corners = (
        padded[..., :-2, :-2] + padded[..., :-2, 2:] + padded[..., 2:, :-2] + padded[..., 2:, 2:]
    )
    return (kappa_sq + 20.0 / 6.0) * centre - (4.0 * edge_sum + corners) / 6.0


def stiffen(field, kappa_sq):
    pads = ((0, 0),) * (field.ndim - 2) + ((1, 1), (1, 1))
    return stencil(jnp.pad(field, pads), kappa_sq)


def all_sum(terms):
    for axis in ("cols", "rows"):
        count = lax.axis_size(axis)
        if count & (count - 1):
            terms = lax.psum(terms, axis)
            continue
        hop = 1
        while hop < count:
            terms = terms + lax.ppermute(terms, axis, [(i, i ^ hop) for i in range(count)])
            hop *= 2
    return terms


def _stiffen_row(ref, r, gain):
    mid = ref[r]
    vertical = ref[r - 1] + ref[r + 1]
    n = mid.shape[0]
    edge_sum = vertical + pltpu.roll(mid, 1, 0) + pltpu.roll(mid, n - 1, 0)
    corners = pltpu.roll(vertical, 1, 0) + pltpu.roll(vertical, n - 1, 0)
    return gain * mid - (4.0 * edge_sum + corners) * (1.0 / 6.0)


def _total(ref, row):
    value = ref[row : row + 1, :]
    return value + pltpu.roll(value, value.shape[1] // 2, 1)


def _ratio(num_ref, num_row, den_ref, den_row):
    return _total(num_ref, num_row) / _total(den_ref, den_row)


def _row_sum(value, keep):
    return jnp.sum(jnp.where(keep, value, 0.0), axis=0, keepdims=True)


class _Plan:
    def __init__(self, slab_rows, first_inner, inner_rows, half):
        self.half = half
        self.slab_rows = slab_rows
        self.first_inner = first_inner
        self.inner_rows = inner_rows

    def inner_row(self, r):
        return (r >= self.first_inner) & (r < self.first_inner + self.inner_rows)


def _zero_edges(ref):
    ref[0] = jnp.zeros(ref.shape[1:], ref.dtype)
    ref[ref.shape[0] - 1] = jnp.zeros(ref.shape[1:], ref.dtype)


def _apply_q(plan, source, gain_ref, weight_ref, inside_ref, row_ref, inner_ref, stiff_ref,
             applied_ref, dot_source):
    last = plan.slab_rows - 1
    _zero_edges(stiff_ref)
    _zero_edges(applied_ref)

    def first_pass(r, carry):
        stiff_ref[r] = weight_ref[r] * _stiffen_row(source, r, gain_ref[r])
        return carry

    lax.fori_loop(1, last, first_pass, 0)

    def second_pass(r, totals):
        applied = _stiffen_row(stiff_ref, r, gain_ref[r])
        keep = (inside_ref[...] > 0.5) & (row_ref[r] > 0.5)
        applied = jnp.where(keep, applied, 0.0)
        applied_ref[r] = applied
        inner = (inner_ref[...] > 0.5) & plan.inner_row(r)
        return totals + _row_sum(dot_source[r] * applied, inner)

    return lax.fori_loop(1, last, second_pass, jnp.zeros((1, source.shape[2]), jnp.float32))


def _spread(value, lane):
    return jnp.broadcast_to(value[:, lane : lane + 1], value.shape)


def _plane_row(value, diagonal):
    return jnp.sum(jnp.where(diagonal, value, 0.0), axis=0, keepdims=True)


def _first_kernel(plan, ext_ref, inside_ref, row_ref, inner_ref, diagonal_ref,
                  z_out, gain_out, weight_out, stiff_out, applied_out, dots_out, stiff_obs_out,
                  observed_scr, scratch):
    last = plan.slab_rows - 1
    sublanes = z_out.shape[1]
    lanes = z_out.shape[2]
    probes = lanes // 2

    def relayout(r, carry):
        cells = ext_ref[r]
        left = cells[0:sublanes]
        right = cells[plan.half : plan.half + sublanes]
        low = lax.broadcasted_iota(jnp.int32, (sublanes, lanes), 1) < probes
        z_out[r] = jnp.where(low, left, pltpu.roll(right, probes, 1))
        observed_scr[r] = jnp.where(low, _spread(left, probes), _spread(right, probes))
        gain_out[r] = jnp.where(low, _spread(left, probes + 1), _spread(right, probes + 1)) + 20.0 / 6.0
        weight_out[r] = jnp.where(low, _spread(left, probes + 2), _spread(right, probes + 2))
        return carry

    lax.fori_loop(0, plan.slab_rows, relayout, 0)
    _zero_edges(stiff_out)

    def probe_pass(r, totals):
        stiff_out[r] = _stiffen_row(z_out, r, gain_out[r])
        z = z_out[r]
        inner = (inner_ref[...] > 0.5) & plan.inner_row(r)
        return totals + _row_sum(z * z, inner)

    zz = lax.fori_loop(1, last, probe_pass, jnp.zeros((1, lanes), jnp.float32))
    _zero_edges(scratch)

    def weigh(r, carry):
        scratch[r] = weight_out[r] * stiff_out[r]
        return carry

    lax.fori_loop(1, last, weigh, 0)

    def second_pass(r, totals):
        applied = _stiffen_row(scratch, r, gain_out[r])
        keep = (inside_ref[...] > 0.5) & (row_ref[r] > 0.5)
        applied = jnp.where(keep, applied, 0.0)
        applied_out[r] = applied
        inner = (inner_ref[...] > 0.5) & plan.inner_row(r)
        return totals + _row_sum(z_out[r] * applied, inner)

    _zero_edges(applied_out)
    za = lax.fori_loop(1, last, second_pass, jnp.zeros((1, lanes), jnp.float32))
    dots_out[0:1, :] = zz
    dots_out[1:2, :] = za

    def observed_pass(r, carry):
        stiff_obs = _stiffen_row(observed_scr, plan.first_inner + r, gain_out[plan.first_inner + r])
        stiff_obs_out[pl.ds(r, 1), :] = _plane_row(stiff_obs, diagonal_ref[...] > 0.5)
        return carry

    lax.fori_loop(0, plan.inner_rows, observed_pass, 0)


def _start_kernel(plan, first_ref, z_ref, applied_ref, inner_ref, residual_out, rr_out):
    step = _ratio(first_ref, 0, first_ref, 1)

    def body(r, totals):
        residual = z_ref[r] - step * applied_ref[r]
        residual_out[r] = residual
        inner = (inner_ref[...] > 0.5) & plan.inner_row(r)
        return totals + _row_sum(residual * residual, inner)

    rr_out[...] = lax.fori_loop(0, plan.slab_rows, body, jnp.zeros((1, z_ref.shape[2]), jnp.float32))


def _update_kernel(plan, norm_ref, curvature_ref, residual_ref, applied_ref, inner_ref,
                   residual_out, rr_out):
    step = _ratio(norm_ref, 0, curvature_ref, 0)

    def body(r, totals):
        residual = residual_ref[r] - step * applied_ref[r]
        residual_out[r] = residual
        inner = (inner_ref[...] > 0.5) & plan.inner_row(r)
        return totals + _row_sum(residual * residual, inner)

    rr_out[...] = lax.fori_loop(
        0, plan.slab_rows, body, jnp.zeros((1, residual_ref.shape[2]), jnp.float32)
    )


def _direction_kernel(plan, next_ref, now_ref, residual_ref, direction_ref, gain_ref, weight_ref,
                      inside_ref, row_ref, inner_ref, direction_out, applied_out, pa_out, scratch):
    beta = _ratio(next_ref, 0, now_ref, 0)

    def new_direction(r, carry):
        direction_out[r] = residual_ref[r] + beta * direction_ref[r]
        return carry

    lax.fori_loop(0, plan.slab_rows, new_direction, 0)
    pa_out[...] = _apply_q(plan, direction_out, gain_ref, weight_ref, inside_ref, row_ref, inner_ref,
                           scratch, applied_out, direction_out)


def _final_kernel(plan, *refs):
    steps = ITERS
    ratio_refs = refs[: 2 * steps]
    direction_refs = refs[2 * steps : 3 * steps]
    (z_ref, stiff_ref, gain_ref, stiff_obs_ref, observed_ref, weight_ref, diagonal_ref,
     grad_kappa_out, grad_weight_out, scratch) = refs[3 * steps :]
    lanes = z_ref.shape[2]
    probes = lanes // 2
    step_lens = []
    for k in range(steps):
        num_ref, den_ref = ratio_refs[2 * k], ratio_refs[2 * k + 1]
        step_lens.append(_ratio(num_ref, 0, den_ref, 1 if k == 0 else 0))

    def new_solution(r, carry):
        solution = step_lens[0] * direction_refs[0][r]
        for k in range(1, steps):
            solution = solution + step_lens[k] * direction_refs[k][r]
        scratch[r] = solution
        return carry

    lax.fori_loop(0, plan.slab_rows, new_solution, 0)

    def probe_sum(value, low):
        first = jnp.sum(jnp.where(low, value, 0.0), axis=1, keepdims=True)
        second = jnp.sum(jnp.where(low, 0.0, value), axis=1, keepdims=True)
        return jnp.where(low, first, second)

    def body(i, carry):
        r = plan.first_inner + i
        solution = scratch[r]
        stiff_solution = _stiffen_row(scratch, r, gain_ref[r])
        stiff_probe = stiff_ref[r]
        low = lax.broadcasted_iota(jnp.int32, solution.shape, 1) < probes
        diagonal = diagonal_ref[...] > 0.5
        weight_total = _plane_row(probe_sum(stiff_solution * stiff_probe, low), diagonal)
        kappa_total = _plane_row(
            probe_sum(solution * stiff_probe + stiff_solution * z_ref[r], low), diagonal
        )
        stiff_obs = stiff_obs_ref[pl.ds(i, 1), :]
        observed = observed_ref[pl.ds(i, 1), :]
        weight = weight_ref[pl.ds(i, 1), :]
        grad_weight_out[pl.ds(i, 1), :] = (
            0.5 * weight_total / probes - 0.5 * stiff_obs * stiff_obs
        )
        grad_kappa_out[pl.ds(i, 1), :] = (
            0.5 * weight * (kappa_total / probes) - observed * weight * stiff_obs
        )
        return carry

    lax.fori_loop(0, plan.inner_rows, body, 0)


def _vmem():
    return pl.BlockSpec(memory_space=pltpu.VMEM)


def _call(kernel, plan, inputs, out_shapes, scratch=0, smem=(), field=None):
    field = out_shapes[0] if field is None else field
    nbytes = 4 * field.shape[0] * field.shape[1] * field.shape[2]
    in_specs = [
        pl.BlockSpec(memory_space=pltpu.SMEM) if i in smem else _vmem() for i in range(len(inputs))
    ]
    return pl.pallas_call(
        lambda *refs: kernel(plan, *refs),
        out_shape=out_shapes,
        in_specs=in_specs,
        out_specs=tuple(_vmem() for _ in out_shapes),
        scratch_shapes=[pltpu.VMEM(field.shape, jnp.float32)] * scratch,
        cost_estimate=pl.CostEstimate(
            flops=40 * nbytes // 4,
            transcendentals=0,
            bytes_accessed=(len(inputs) + len(out_shapes)) * nbytes,
        ),
    )(*inputs)


def on_device(probes, observed, kappa_sq, variance_weight):
    probe_count, rows, cols = probes.shape
    half = cols // 2
    assert rows >= HALO and cols % 2 == 0 and half >= HALO and half == probe_count
    width = half + 2 * HALO
    sublanes = -(-width // 8) * 8
    slab_rows = rows + 2 * HALO
    lanes = 2 * probe_count
    stacked = jnp.concatenate(
        [probes, observed[None], kappa_sq[None], variance_weight[None]], axis=0
    )
    count = lax.axis_size("rows")
    sent = -(-HALO // 8) * 8
    assert sent <= rows
    planes = stacked.shape[0]
    fields = (probes, observed[None], kappa_sq[None], variance_weight[None])

    def edge_rows(start):
        rows_of = [lax.slice_in_dim(f, start, start + sent, axis=1) for f in fields]
        return jnp.concatenate(rows_of, axis=0).reshape(planes * sent, cols)

    below = lax.ppermute(
        edge_rows(rows - sent), "rows", [(i, i + 1) for i in range(count - 1)]
    ).reshape(planes, sent, cols)[:, sent - HALO :]
    above = lax.ppermute(
        edge_rows(0), "rows", [(i + 1, i) for i in range(count - 1)]
    ).reshape(planes, sent, cols)[:, :HALO]
    ext = jnp.concatenate(
        [jnp.transpose(piece, (1, 2, 0)) for piece in (below, stacked, above)], axis=0
    )
    ext = extended(ext, (("cols", 1),), HALO)
    ext = jnp.pad(
        ext, ((0, 0), (0, half + sublanes - ext.shape[1]), (0, lanes - ext.shape[2]))
    )

    row_at = lax.axis_index("rows") * rows - HALO + lax.iota(jnp.int32, slab_rows)
    row_in = ((row_at >= 0) & (row_at < rows * lax.axis_size("rows"))).astype(jnp.float32)
    col_in = []
    col_inner = []
    for h in range(2):
        at = lax.iota(jnp.int32, sublanes)
        col_at = lax.axis_index("cols") * cols - HALO + h * half + at
        col_in.append((col_at >= 0) & (col_at < cols * lax.axis_size("cols")) & (at < width))
        col_inner.append((at >= HALO) & (at < HALO + half))

    def on_lanes_of(columns):
        return jnp.concatenate(
            [jnp.broadcast_to(c[:, None], (sublanes, probe_count)) for c in columns], axis=1
        ).astype(jnp.float32)

    inside = on_lanes_of(col_in)
    inner = on_lanes_of(col_inner)
    lane_col = lax.iota(jnp.int32, lanes) % half + HALO
    diagonal = (lax.iota(jnp.int32, sublanes)[:, None] == lane_col[None, :]).astype(jnp.float32)
    plan = _Plan(slab_rows, HALO, rows, half)

    field = jax.ShapeDtypeStruct((slab_rows, sublanes, lanes), jnp.float32)
    lane_row = jax.ShapeDtypeStruct((1, lanes), jnp.float32)
    out_plane = jax.ShapeDtypeStruct((rows, cols), jnp.float32)

    z, gain, weight, stiff_probe, applied, first, stiff_obs = _call(
        _first_kernel, plan, (ext, inside, row_in, inner, diagonal),
        (field, field, field, field, field, jax.ShapeDtypeStruct((2, lanes), jnp.float32), out_plane),
        scratch=2, smem=(2,),
    )
    first = all_sum(first)
    residual, rr = _call(_start_kernel, plan, (first, z, applied, inner), (field, lane_row))
    directions = [z]
    ratios = [first, first]
    direction = z
    norm_now = first
    for iteration in range(1, ITERS):
        norm_next = all_sum(rr)
        direction, applied, pa = _call(
            _direction_kernel, plan,
            (norm_next, norm_now, residual, direction, gain, weight, inside, row_in, inner),
            (field, field, lane_row), scratch=1, smem=(7,),
        )
        norm_now = norm_next
        curvature = all_sum(pa)
        directions.append(direction)
        ratios += [norm_now, curvature]
        if iteration + 1 < ITERS:
            residual, rr = _call(
                _update_kernel, plan, (norm_now, curvature, residual, applied, inner),
                (field, lane_row),
            )

    grad_kappa, grad_weight = _call(
        _final_kernel, plan,
        (*ratios, *directions, z, stiff_probe, gain, stiff_obs, observed, variance_weight, diagonal),
        (out_plane, out_plane), scratch=1, field=field,
    )
    return (grad_kappa, grad_weight)


def solution(mesh):
    placed = (P(None, "rows", "cols"), P("rows", "cols"), P("rows", "cols"), P("rows", "cols"))
    return jax.shard_map(
        on_device,
        mesh=mesh,
        in_specs=placed,
        out_specs=(P("rows", "cols"), P("rows", "cols")),
        check_vma=False,
    )
```

```python
import jax
import jax.numpy as jnp
from jax import lax
from jax.experimental import pallas as pl
from jax.experimental.pallas import tpu as pltpu
from jax.sharding import PartitionSpec as P

ITERS = 3
HALO = 2 * ITERS


def extended(cells, sides, width):
    for axis, dim in sides:
        count = lax.axis_size(axis)
        ends = count - 1
        head = lax.slice_in_dim(cells, 0, width, axis=dim)
        tail = lax.slice_in_dim(cells, cells.shape[dim] - width, cells.shape[dim], axis=dim)
        cells = jnp.concatenate(
            [
                lax.ppermute(tail, axis, [(i, (i + 1) % count) for i in range(ends)]),
                cells,
                lax.ppermute(head, axis, [((i + 1) % count, i) for i in range(ends)]),
            ],
            axis=dim,
        )
    return cells


def stencil(padded, kappa_sq):
    centre = padded[..., 1:-1, 1:-1]
    edge_sum = (
        padded[..., :-2, 1:-1]
        + padded[..., 2:, 1:-1]
        + padded[..., 1:-1, :-2]
        + padded[..., 1:-1, 2:]
    )
    corners = (
        padded[..., :-2, :-2] + padded[..., :-2, 2:] + padded[..., 2:, :-2] + padded[..., 2:, 2:]
    )
    return (kappa_sq + 20.0 / 6.0) * centre - (4.0 * edge_sum + corners) / 6.0


def stiffen(field, kappa_sq):
    pads = ((0, 0),) * (field.ndim - 2) + ((1, 1), (1, 1))
    return stencil(jnp.pad(field, pads), kappa_sq)


def _span_sum(terms, basis, partner):
    if not basis:
        return partner(0)
    *rest, top = basis
    return _span_sum(terms, rest, partner) + _span_sum(terms, rest, lambda m: partner(m ^ top))


def all_sum(terms):
    axes = ("rows", "cols")
    count = lax.axis_size("rows") * lax.axis_size("cols")
    if count & (count - 1):
        for axis in axes:
            terms = lax.psum(terms, axis)
        return terms
    bits = [1 << k for k in range(count.bit_length() - 1)]
    groups = [bits[:1]] + [bits[k : k + 2] for k in range(1, len(bits), 2)]
    for basis in groups:
        received = {}

        def partner(mask, terms=terms, received=received):
            if mask == 0:
                return terms
            if mask not in received:
                received[mask] = lax.ppermute(terms, axes, [(i, i ^ mask) for i in range(count)])
            return received[mask]

        terms = _span_sum(terms, basis, partner)
    return terms


def _stiffen_row(ref, r, gain):
    mid = ref[r]
    vertical = ref[r - 1] + ref[r + 1]
    n = mid.shape[0]
    edge_sum = vertical + pltpu.roll(mid, 1, 0) + pltpu.roll(mid, n - 1, 0)
    corners = pltpu.roll(vertical, 1, 0) + pltpu.roll(vertical, n - 1, 0)
    return gain * mid - (4.0 * edge_sum + corners) * (1.0 / 6.0)


def _total(ref, row):
    value = ref[row : row + 1, :]
    return value + pltpu.roll(value, value.shape[1] // 2, 1)


def _ratio(num_ref, num_row, den_ref, den_row):
    return _total(num_ref, num_row) / _total(den_ref, den_row)


def _row_sum(value, keep):
    return jnp.sum(jnp.where(keep, value, 0.0), axis=0, keepdims=True)


class _Plan:
    def __init__(self, slab_rows, first_inner, inner_rows, half):
        self.half = half
        self.slab_rows = slab_rows
        self.first_inner = first_inner
        self.inner_rows = inner_rows

    def inner_row(self, r):
        return (r >= self.first_inner) & (r < self.first_inner + self.inner_rows)


def _zero_edges(ref):
    ref[0] = jnp.zeros(ref.shape[1:], ref.dtype)
    ref[ref.shape[0] - 1] = jnp.zeros(ref.shape[1:], ref.dtype)


def _apply_q(plan, source, gain_ref, weight_ref, inside_ref, row_ref, inner_ref, stiff_ref,
             applied_ref, dot_source):
    last = plan.slab_rows - 1
    _zero_edges(stiff_ref)
    _zero_edges(applied_ref)

    def first_pass(r, carry):
        stiff_ref[r] = weight_ref[r] * _stiffen_row(source, r, gain_ref[r])
        return carry

    lax.fori_loop(1, last, first_pass, 0)

    def second_pass(r, totals):
        applied = _stiffen_row(stiff_ref, r, gain_ref[r])
        keep = (inside_ref[...] > 0.5) & (row_ref[r] > 0.5)
        applied = jnp.where(keep, applied, 0.0)
        applied_ref[r] = applied
        inner = (inner_ref[...] > 0.5) & plan.inner_row(r)
        return totals + _row_sum(dot_source[r] * applied, inner)

    return lax.fori_loop(1, last, second_pass, jnp.zeros((1, source.shape[2]), jnp.float32))


def _spread(value, lane):
    return jnp.broadcast_to(value[:, lane : lane + 1], value.shape)


def _plane_row(value, diagonal):
    return jnp.sum(jnp.where(diagonal, value, 0.0), axis=0, keepdims=True)


def _first_kernel(plan, ext_ref, inside_ref, row_ref, inner_ref, diagonal_ref,
                  z_out, gain_out, weight_out, stiff_out, applied_out, dots_out, stiff_obs_out,
                  observed_scr, scratch):
    last = plan.slab_rows - 1
    sublanes = z_out.shape[1]
    lanes = z_out.shape[2]
    probes = lanes // 2

    def relayout(r, carry):
        cells = ext_ref[r]
        left = cells[0:sublanes]
        right = cells[plan.half : plan.half + sublanes]
        low = lax.broadcasted_iota(jnp.int32, (sublanes, lanes), 1) < probes
        z_out[r] = jnp.where(low, left, pltpu.roll(right, probes, 1))
        observed_scr[r] = jnp.where(low, _spread(left, probes), _spread(right, probes))
        gain_out[r] = jnp.where(low, _spread(left, probes + 1), _spread(right, probes + 1)) + 20.0 / 6.0
        weight_out[r] = jnp.where(low, _spread(left, probes + 2), _spread(right, probes + 2))
        return carry

    lax.fori_loop(0, plan.slab_rows, relayout, 0)
    _zero_edges(stiff_out)

    def probe_pass(r, totals):
        stiff_out[r] = _stiffen_row(z_out, r, gain_out[r])
        z = z_out[r]
        inner = (inner_ref[...] > 0.5) & plan.inner_row(r)
        return totals + _row_sum(z * z, inner)

    zz = lax.fori_loop(1, last, probe_pass, jnp.zeros((1, lanes), jnp.float32))
    _zero_edges(scratch)

    def weigh(r, carry):
        scratch[r] = weight_out[r] * stiff_out[r]
        return carry

    lax.fori_loop(1, last, weigh, 0)

    def second_pass(r, totals):
        applied = _stiffen_row(scratch, r, gain_out[r])
        keep = (inside_ref[...] > 0.5) & (row_ref[r] > 0.5)
        applied = jnp.where(keep, applied, 0.0)
        applied_out[r] = applied
        inner = (inner_ref[...] > 0.5) & plan.inner_row(r)
        return totals + _row_sum(z_out[r] * applied, inner)

    _zero_edges(applied_out)
    za = lax.fori_loop(1, last, second_pass, jnp.zeros((1, lanes), jnp.float32))
    dots_out[0:1, :] = zz
    dots_out[1:2, :] = za

    def observed_pass(r, carry):
        stiff_obs = _stiffen_row(observed_scr, plan.first_inner + r, gain_out[plan.first_inner + r])
        stiff_obs_out[pl.ds(r, 1), :] = _plane_row(stiff_obs, diagonal_ref[...] > 0.5)
        return carry

    lax.fori_loop(0, plan.inner_rows, observed_pass, 0)


def _start_kernel(plan, first_ref, z_ref, applied_ref, inner_ref, residual_out, rr_out):
    step = _ratio(first_ref, 0, first_ref, 1)

    def body(r, totals):
        residual = z_ref[r] - step * applied_ref[r]
        residual_out[r] = residual
        inner = (inner_ref[...] > 0.5) & plan.inner_row(r)
        return totals + _row_sum(residual * residual, inner)

    rr_out[...] = lax.fori_loop(0, plan.slab_rows, body, jnp.zeros((1, z_ref.shape[2]), jnp.float32))


def _update_kernel(plan, norm_ref, curvature_ref, residual_ref, applied_ref, inner_ref,
                   residual_out, rr_out):
    step = _ratio(norm_ref, 0, curvature_ref, 0)

    def body(r, totals):
        residual = residual_ref[r] - step * applied_ref[r]
        residual_out[r] = residual
        inner = (inner_ref[...] > 0.5) & plan.inner_row(r)
        return totals + _row_sum(residual * residual, inner)

    rr_out[...] = lax.fori_loop(
        0, plan.slab_rows, body, jnp.zeros((1, residual_ref.shape[2]), jnp.float32)
    )


def _direction_kernel(plan, next_ref, now_ref, residual_ref, direction_ref, gain_ref, weight_ref,
                      inside_ref, row_ref, inner_ref, direction_out, applied_out, pa_out, scratch):
    beta = _ratio(next_ref, 0, now_ref, 0)

    def new_direction(r, carry):
        direction_out[r] = residual_ref[r] + beta * direction_ref[r]
        return carry

    lax.fori_loop(0, plan.slab_rows, new_direction, 0)
    pa_out[...] = _apply_q(plan, direction_out, gain_ref, weight_ref, inside_ref, row_ref, inner_ref,
                           scratch, applied_out, direction_out)


def _final_kernel(plan, *refs):
    steps = ITERS
    ratio_refs = refs[: 2 * steps]
    direction_refs = refs[2 * steps : 3 * steps]
    (z_ref, stiff_ref, gain_ref, stiff_obs_ref, observed_ref, weight_ref, diagonal_ref,
     grad_kappa_out, grad_weight_out, scratch) = refs[3 * steps :]
    lanes = z_ref.shape[2]
    probes = lanes // 2
    step_lens = []
    for k in range(steps):
        num_ref, den_ref = ratio_refs[2 * k], ratio_refs[2 * k + 1]
        step_lens.append(_ratio(num_ref, 0, den_ref, 1 if k == 0 else 0))

    def new_solution(r, carry):
        solution = step_lens[0] * direction_refs[0][r]
        for k in range(1, steps):
            solution = solution + step_lens[k] * direction_refs[k][r]
        scratch[r] = solution
        return carry

    lax.fori_loop(0, plan.slab_rows, new_solution, 0)

    def probe_sum(value, low):
        first = jnp.sum(jnp.where(low, value, 0.0), axis=1, keepdims=True)
        second = jnp.sum(jnp.where(low, 0.0, value), axis=1, keepdims=True)
        return jnp.where(low, first, second)

    def body(i, carry):
        r = plan.first_inner + i
        solution = scratch[r]
        stiff_solution = _stiffen_row(scratch, r, gain_ref[r])
        stiff_probe = stiff_ref[r]
        low = lax.broadcasted_iota(jnp.int32, solution.shape, 1) < probes
        diagonal = diagonal_ref[...] > 0.5
        weight_total = _plane_row(probe_sum(stiff_solution * stiff_probe, low), diagonal)
        kappa_total = _plane_row(
            probe_sum(solution * stiff_probe + stiff_solution * z_ref[r], low), diagonal
        )
        stiff_obs = stiff_obs_ref[pl.ds(i, 1), :]
        observed = observed_ref[pl.ds(i, 1), :]
        weight = weight_ref[pl.ds(i, 1), :]
        grad_weight_out[pl.ds(i, 1), :] = (
            0.5 * weight_total / probes - 0.5 * stiff_obs * stiff_obs
        )
        grad_kappa_out[pl.ds(i, 1), :] = (
            0.5 * weight * (kappa_total / probes) - observed * weight * stiff_obs
        )
        return carry

    lax.fori_loop(0, plan.inner_rows, body, 0)


def _vmem():
    return pl.BlockSpec(memory_space=pltpu.VMEM)


def _call(kernel, plan, inputs, out_shapes, scratch=0, smem=(), field=None):
    field = out_shapes[0] if field is None else field
    nbytes = 4 * field.shape[0] * field.shape[1] * field.shape[2]
    in_specs = [
        pl.BlockSpec(memory_space=pltpu.SMEM) if i in smem else _vmem() for i in range(len(inputs))
    ]
    return pl.pallas_call(
        lambda *refs: kernel(plan, *refs),
        out_shape=out_shapes,
        in_specs=in_specs,
        out_specs=tuple(_vmem() for _ in out_shapes),
        scratch_shapes=[pltpu.VMEM(field.shape, jnp.float32)] * scratch,
        cost_estimate=pl.CostEstimate(
            flops=40 * nbytes // 4,
            transcendentals=0,
            bytes_accessed=(len(inputs) + len(out_shapes)) * nbytes,
        ),
    )(*inputs)


def on_device(probes, observed, kappa_sq, variance_weight):
    probe_count, rows, cols = probes.shape
    half = cols // 2
    assert rows >= HALO and cols % 2 == 0 and half >= HALO and half == probe_count
    width = half + 2 * HALO
    sublanes = -(-width // 8) * 8
    slab_rows = rows + 2 * HALO
    lanes = 2 * probe_count
    stacked = jnp.concatenate(
        [probes, observed[None], kappa_sq[None], variance_weight[None]], axis=0
    )
    count = lax.axis_size("rows")
    sent = -(-HALO // 8) * 8
    assert sent <= rows
    planes = stacked.shape[0]
    fields = (probes, observed[None], kappa_sq[None], variance_weight[None])

    def edge_rows(start):
        rows_of = [lax.slice_in_dim(f, start, start + sent, axis=1) for f in fields]
        return jnp.concatenate(rows_of, axis=0).reshape(planes * sent, cols)

    below = lax.ppermute(
        edge_rows(rows - sent), "rows", [(i, i + 1) for i in range(count - 1)]
    ).reshape(planes, sent, cols)[:, sent - HALO :]
    above = lax.ppermute(
        edge_rows(0), "rows", [(i + 1, i) for i in range(count - 1)]
    ).reshape(planes, sent, cols)[:, :HALO]
    ext = jnp.concatenate(
        [jnp.transpose(piece, (1, 2, 0)) for piece in (below, stacked, above)], axis=0
    )
    ext = extended(ext, (("cols", 1),), HALO)
    ext = jnp.pad(
        ext, ((0, 0), (0, half + sublanes - ext.shape[1]), (0, lanes - ext.shape[2]))
    )

    row_at = lax.axis_index("rows") * rows - HALO + lax.iota(jnp.int32, slab_rows)
    row_in = ((row_at >= 0) & (row_at < rows * lax.axis_size("rows"))).astype(jnp.float32)
    col_in = []
    col_inner = []
    for h in range(2):
        at = lax.iota(jnp.int32, sublanes)
        col_at = lax.axis_index("cols") * cols - HALO + h * half + at
        col_in.append((col_at >= 0) & (col_at < cols * lax.axis_size("cols")) & (at < width))
        col_inner.append((at >= HALO) & (at < HALO + half))

    def on_lanes_of(columns):
        return jnp.concatenate(
            [jnp.broadcast_to(c[:, None], (sublanes, probe_count)) for c in columns], axis=1
        ).astype(jnp.float32)

    inside = on_lanes_of(col_in)
    inner = on_lanes_of(col_inner)
    lane_col = lax.iota(jnp.int32, lanes) % half + HALO
    diagonal = (lax.iota(jnp.int32, sublanes)[:, None] == lane_col[None, :]).astype(jnp.float32)
    plan = _Plan(slab_rows, HALO, rows, half)

    field = jax.ShapeDtypeStruct((slab_rows, sublanes, lanes), jnp.float32)
    lane_row = jax.ShapeDtypeStruct((1, lanes), jnp.float32)
    out_plane = jax.ShapeDtypeStruct((rows, cols), jnp.float32)

    z, gain, weight, stiff_probe, applied, first, stiff_obs = _call(
        _first_kernel, plan, (ext, inside, row_in, inner, diagonal),
        (field, field, field, field, field, jax.ShapeDtypeStruct((2, lanes), jnp.float32), out_plane),
        scratch=2, smem=(2,),
    )
    first = all_sum(first)
    residual, rr = _call(_start_kernel, plan, (first, z, applied, inner), (field, lane_row))
    directions = [z]
    ratios = [first, first]
    direction = z
    norm_now = first
    for iteration in range(1, ITERS):
        norm_next = all_sum(rr)
        direction, applied, pa = _call(
            _direction_kernel, plan,
            (norm_next, norm_now, residual, direction, gain, weight, inside, row_in, inner),
            (field, field, lane_row), scratch=1, smem=(7,),
        )
        norm_now = norm_next
        curvature = all_sum(pa)
        directions.append(direction)
        ratios += [norm_now, curvature]
        if iteration + 1 < ITERS:
            residual, rr = _call(
                _update_kernel, plan, (norm_now, curvature, residual, applied, inner),
                (field, lane_row),
            )

    grad_kappa, grad_weight = _call(
        _final_kernel, plan,
        (*ratios, *directions, z, stiff_probe, gain, stiff_obs, observed, variance_weight, diagonal),
        (out_plane, out_plane), scratch=1, field=field,
    )
    return (grad_kappa, grad_weight)


def solution(mesh):
    placed = (P(None, "rows", "cols"), P("rows", "cols"), P("rows", "cols"), P("rows", "cols"))
    return jax.shard_map(
        on_device,
        mesh=mesh,
        in_specs=placed,
        out_specs=(P("rows", "cols"), P("rows", "cols")),
        check_vma=False,
    )
```

```python
import jax
import jax.numpy as jnp
from jax import lax
from jax.experimental import pallas as pl
from jax.experimental.pallas import tpu as pltpu
from jax.sharding import PartitionSpec as P

ITERS = 3
HALO = 2 * ITERS


def extended(cells, sides, width):
    for axis, dim in sides:
        count = lax.axis_size(axis)
        ends = count - 1
        head = lax.slice_in_dim(cells, 0, width, axis=dim)
        tail = lax.slice_in_dim(cells, cells.shape[dim] - width, cells.shape[dim], axis=dim)
        cells = jnp.concatenate(
            [
                lax.ppermute(tail, axis, [(i, (i + 1) % count) for i in range(ends)]),
                cells,
                lax.ppermute(head, axis, [((i + 1) % count, i) for i in range(ends)]),
            ],
            axis=dim,
        )
    return cells


def stencil(padded, kappa_sq):
    centre = padded[..., 1:-1, 1:-1]
    edge_sum = (
        padded[..., :-2, 1:-1]
        + padded[..., 2:, 1:-1]
        + padded[..., 1:-1, :-2]
        + padded[..., 1:-1, 2:]
    )
    corners = (
        padded[..., :-2, :-2] + padded[..., :-2, 2:] + padded[..., 2:, :-2] + padded[..., 2:, 2:]
    )
    return (kappa_sq + 20.0 / 6.0) * centre - (4.0 * edge_sum + corners) / 6.0


def stiffen(field, kappa_sq):
    pads = ((0, 0),) * (field.ndim - 2) + ((1, 1), (1, 1))
    return stencil(jnp.pad(field, pads), kappa_sq)


def _span_sum(terms, basis, partner):
    if not basis:
        return partner(0)
    *rest, top = basis
    return _span_sum(terms, rest, partner) + _span_sum(terms, rest, lambda m: partner(m ^ top))


def all_sum(terms):
    axes = ("rows", "cols")
    count = lax.axis_size("rows") * lax.axis_size("cols")
    if count & (count - 1):
        for axis in axes:
            terms = lax.psum(terms, axis)
        return terms
    bits = [1 << k for k in range(count.bit_length() - 1)]
    groups = [bits[:1]] + [bits[k : k + 2] for k in range(1, len(bits), 2)]
    for basis in groups:
        received = {}

        def partner(mask, terms=terms, received=received):
            if mask == 0:
                return terms
            if mask not in received:
                received[mask] = lax.ppermute(terms, axes, [(i, i ^ mask) for i in range(count)])
            return received[mask]

        terms = _span_sum(terms, basis, partner)
    return terms


def _stiffen_row(ref, r, gain):
    mid = ref[r]
    vertical = ref[r - 1] + ref[r + 1]
    n = mid.shape[0]
    edge_sum = vertical + pltpu.roll(mid, 1, 0) + pltpu.roll(mid, n - 1, 0)
    corners = pltpu.roll(vertical, 1, 0) + pltpu.roll(vertical, n - 1, 0)
    return gain * mid - (4.0 * edge_sum + corners) * (1.0 / 6.0)


def _total(ref, row):
    value = ref[row : row + 1, :]
    return value + pltpu.roll(value, value.shape[1] // 2, 1)


def _ratio(num_ref, num_row, den_ref, den_row):
    return _total(num_ref, num_row) / _total(den_ref, den_row)


def _row_sum(value, keep):
    return jnp.sum(jnp.where(keep, value, 0.0), axis=0, keepdims=True)


class _Plan:
    def __init__(self, slab_rows, first_inner, inner_rows, half):
        self.half = half
        self.slab_rows = slab_rows
        self.first_inner = first_inner
        self.inner_rows = inner_rows

    def inner_row(self, r):
        return (r >= self.first_inner) & (r < self.first_inner + self.inner_rows)


def _zero_edges(ref):
    ref[0] = jnp.zeros(ref.shape[1:], ref.dtype)
    ref[ref.shape[0] - 1] = jnp.zeros(ref.shape[1:], ref.dtype)


def _apply_q(plan, source, gain_ref, weight_ref, inside_ref, row_ref, inner_ref, stiff_ref,
             applied_ref, dot_source):
    last = plan.slab_rows - 1
    _zero_edges(stiff_ref)
    _zero_edges(applied_ref)

    def first_pass(r, carry):
        stiff_ref[r] = weight_ref[r] * _stiffen_row(source, r, gain_ref[r])
        return carry

    lax.fori_loop(1, last, first_pass, 0)

    def second_pass(r, totals):
        applied = _stiffen_row(stiff_ref, r, gain_ref[r])
        keep = (inside_ref[...] > 0.5) & (row_ref[r] > 0.5)
        applied = jnp.where(keep, applied, 0.0)
        applied_ref[r] = applied
        inner = (inner_ref[...] > 0.5) & plan.inner_row(r)
        return totals + _row_sum(dot_source[r] * applied, inner)

    return lax.fori_loop(1, last, second_pass, jnp.zeros((1, source.shape[2]), jnp.float32))


def _spread(value, lane):
    return jnp.broadcast_to(value[:, lane : lane + 1], value.shape)


def _plane_row(value, diagonal):
    return jnp.sum(jnp.where(diagonal, value, 0.0), axis=0, keepdims=True)


def _first_kernel(plan, ext_ref, inside_ref, row_ref, inner_ref, diagonal_ref,
                  z_out, gain_out, weight_out, stiff_out, applied_out, dots_out, stiff_obs_out,
                  observed_scr, scratch):
    last = plan.slab_rows - 1
    sublanes = z_out.shape[1]
    lanes = z_out.shape[2]
    probes = lanes // 2

    def relayout(r, carry):
        cells = ext_ref[r]
        left = cells[0:sublanes]
        right = cells[plan.half : plan.half + sublanes]
        low = lax.broadcasted_iota(jnp.int32, (sublanes, lanes), 1) < probes
        z_out[r] = jnp.where(low, left, pltpu.roll(right, probes, 1))
        observed_scr[r] = jnp.where(low, _spread(left, probes), _spread(right, probes))
        gain_out[r] = jnp.where(low, _spread(left, probes + 1), _spread(right, probes + 1)) + 20.0 / 6.0
        weight_out[r] = jnp.where(low, _spread(left, probes + 2), _spread(right, probes + 2))
        return carry

    lax.fori_loop(0, plan.slab_rows, relayout, 0)
    _zero_edges(stiff_out)

    def probe_pass(r, totals):
        stiff_out[r] = _stiffen_row(z_out, r, gain_out[r])
        z = z_out[r]
        inner = (inner_ref[...] > 0.5) & plan.inner_row(r)
        return totals + _row_sum(z * z, inner)

    zz = lax.fori_loop(1, last, probe_pass, jnp.zeros((1, lanes), jnp.float32))
    _zero_edges(scratch)

    def weigh(r, carry):
        scratch[r] = weight_out[r] * stiff_out[r]
        return carry

    lax.fori_loop(1, last, weigh, 0)

    def second_pass(r, totals):
        applied = _stiffen_row(scratch, r, gain_out[r])
        keep = (inside_ref[...] > 0.5) & (row_ref[r] > 0.5)
        applied = jnp.where(keep, applied, 0.0)
        applied_out[r] = applied
        inner = (inner_ref[...] > 0.5) & plan.inner_row(r)
        return totals + _row_sum(z_out[r] * applied, inner)

    _zero_edges(applied_out)
    za = lax.fori_loop(1, last, second_pass, jnp.zeros((1, lanes), jnp.float32))
    dots_out[0:1, :] = zz
    dots_out[1:2, :] = za

    def observed_pass(r, carry):
        stiff_obs = _stiffen_row(observed_scr, plan.first_inner + r, gain_out[plan.first_inner + r])
        stiff_obs_out[pl.ds(r, 1), :] = _plane_row(stiff_obs, diagonal_ref[...] > 0.5)
        return carry

    lax.fori_loop(0, plan.inner_rows, observed_pass, 0)


def _accumulate(rr_out, totals):
    @pl.when(pl.program_id(0) == 0)
    def _():
        rr_out[...] = jnp.zeros_like(rr_out)

    rr_out[...] = rr_out[...] + totals


def _start_kernel(plan, first_ref, z_ref, applied_ref, inner_ref, residual_out, rr_out):
    step = _ratio(first_ref, 0, first_ref, 1)
    base = pl.program_id(0) * z_ref.shape[0]

    def body(r, totals):
        residual = z_ref[r] - step * applied_ref[r]
        residual_out[r] = residual
        inner = (inner_ref[...] > 0.5) & plan.inner_row(base + r)
        return totals + _row_sum(residual * residual, inner)

    _accumulate(rr_out, lax.fori_loop(0, z_ref.shape[0], body, jnp.zeros((1, z_ref.shape[2]), jnp.float32)))


def _update_kernel(plan, norm_ref, curvature_ref, residual_ref, applied_ref, inner_ref,
                   residual_out, rr_out):
    step = _ratio(norm_ref, 0, curvature_ref, 0)
    base = pl.program_id(0) * residual_ref.shape[0]

    def body(r, totals):
        residual = residual_ref[r] - step * applied_ref[r]
        residual_out[r] = residual
        inner = (inner_ref[...] > 0.5) & plan.inner_row(base + r)
        return totals + _row_sum(residual * residual, inner)

    _accumulate(rr_out, lax.fori_loop(
        0, residual_ref.shape[0], body, jnp.zeros((1, residual_ref.shape[2]), jnp.float32)
    ))


def _row_call(kernel, plan, inputs, fields, out_shapes):
    field = out_shapes[0]
    block = max(d for d in range(1, 9) if field.shape[0] % d == 0)
    nbytes = 4 * field.shape[0] * field.shape[1] * field.shape[2]

    def spec(value, is_field):
        if is_field:
            return pl.BlockSpec((block,) + value.shape[1:], lambda g: (g, 0, 0))
        return pl.BlockSpec(value.shape, lambda g: (0,) * len(value.shape))

    return pl.pallas_call(
        lambda *refs: kernel(plan, *refs),
        out_shape=out_shapes,
        grid=(field.shape[0] // block,),
        in_specs=[spec(v, i in fields) for i, v in enumerate(inputs)],
        out_specs=tuple(spec(o, len(o.shape) == 3) for o in out_shapes),
        compiler_params=pltpu.CompilerParams(dimension_semantics=("arbitrary",)),
        cost_estimate=pl.CostEstimate(
            flops=4 * nbytes // 4, transcendentals=0,
            bytes_accessed=(len(fields) + 1) * nbytes,
        ),
    )(*inputs)


def _direction_kernel(plan, next_ref, now_ref, residual_ref, direction_ref, gain_ref, weight_ref,
                      inside_ref, row_ref, inner_ref, direction_out, applied_out, pa_out, scratch):
    beta = _ratio(next_ref, 0, now_ref, 0)

    def new_direction(r, carry):
        direction_out[r] = residual_ref[r] + beta * direction_ref[r]
        return carry

    lax.fori_loop(0, plan.slab_rows, new_direction, 0)
    pa_out[...] = _apply_q(plan, direction_out, gain_ref, weight_ref, inside_ref, row_ref, inner_ref,
                           scratch, applied_out, direction_out)


def _final_kernel(plan, *refs):
    steps = ITERS
    ratio_refs = refs[: 2 * steps]
    direction_refs = refs[2 * steps : 3 * steps]
    (z_ref, stiff_ref, gain_ref, stiff_obs_ref, observed_ref, weight_ref, diagonal_ref,
     grad_kappa_out, grad_weight_out, scratch) = refs[3 * steps :]
    lanes = z_ref.shape[2]
    probes = lanes // 2
    step_lens = []
    for k in range(steps):
        num_ref, den_ref = ratio_refs[2 * k], ratio_refs[2 * k + 1]
        step_lens.append(_ratio(num_ref, 0, den_ref, 1 if k == 0 else 0))

    def new_solution(r, carry):
        solution = step_lens[0] * direction_refs[0][r]
        for k in range(1, steps):
            solution = solution + step_lens[k] * direction_refs[k][r]
        scratch[r] = solution
        return carry

    lax.fori_loop(0, plan.slab_rows, new_solution, 0)

    def probe_sum(value, low):
        first = jnp.sum(jnp.where(low, value, 0.0), axis=1, keepdims=True)
        second = jnp.sum(jnp.where(low, 0.0, value), axis=1, keepdims=True)
        return jnp.where(low, first, second)

    def body(i, carry):
        r = plan.first_inner + i
        solution = scratch[r]
        stiff_solution = _stiffen_row(scratch, r, gain_ref[r])
        stiff_probe = stiff_ref[r]
        low = lax.broadcasted_iota(jnp.int32, solution.shape, 1) < probes
        diagonal = diagonal_ref[...] > 0.5
        weight_total = _plane_row(probe_sum(stiff_solution * stiff_probe, low), diagonal)
        kappa_total = _plane_row(
            probe_sum(solution * stiff_probe + stiff_solution * z_ref[r], low), diagonal
        )
        stiff_obs = stiff_obs_ref[pl.ds(i, 1), :]
        observed = observed_ref[pl.ds(i, 1), :]
        weight = weight_ref[pl.ds(i, 1), :]
        grad_weight_out[pl.ds(i, 1), :] = (
            0.5 * weight_total / probes - 0.5 * stiff_obs * stiff_obs
        )
        grad_kappa_out[pl.ds(i, 1), :] = (
            0.5 * weight * (kappa_total / probes) - observed * weight * stiff_obs
        )
        return carry

    lax.fori_loop(0, plan.inner_rows, body, 0)


def _vmem():
    return pl.BlockSpec(memory_space=pltpu.VMEM)


def _call(kernel, plan, inputs, out_shapes, scratch=0, smem=(), field=None):
    field = out_shapes[0] if field is None else field
    nbytes = 4 * field.shape[0] * field.shape[1] * field.shape[2]
    in_specs = [
        pl.BlockSpec(memory_space=pltpu.SMEM) if i in smem else _vmem() for i in range(len(inputs))
    ]
    return pl.pallas_call(
        lambda *refs: kernel(plan, *refs),
        out_shape=out_shapes,
        in_specs=in_specs,
        out_specs=tuple(_vmem() for _ in out_shapes),
        scratch_shapes=[pltpu.VMEM(field.shape, jnp.float32)] * scratch,
        cost_estimate=pl.CostEstimate(
            flops=40 * nbytes // 4,
            transcendentals=0,
            bytes_accessed=(len(inputs) + len(out_shapes)) * nbytes,
        ),
    )(*inputs)


def on_device(probes, observed, kappa_sq, variance_weight):
    probe_count, rows, cols = probes.shape
    half = cols // 2
    assert rows >= HALO and cols % 2 == 0 and half >= HALO and half == probe_count
    width = half + 2 * HALO
    sublanes = -(-width // 8) * 8
    slab_rows = rows + 2 * HALO
    lanes = 2 * probe_count
    stacked = jnp.concatenate(
        [probes, observed[None], kappa_sq[None], variance_weight[None]], axis=0
    )
    count = lax.axis_size("rows")
    sent = -(-HALO // 8) * 8
    assert sent <= rows
    planes = stacked.shape[0]
    fields = (probes, observed[None], kappa_sq[None], variance_weight[None])

    def edge_rows(start):
        rows_of = [lax.slice_in_dim(f, start, start + sent, axis=1) for f in fields]
        return jnp.concatenate(rows_of, axis=0).reshape(planes * sent, cols)

    below = lax.ppermute(
        edge_rows(rows - sent), "rows", [(i, i + 1) for i in range(count - 1)]
    ).reshape(planes, sent, cols)[:, sent - HALO :]
    above = lax.ppermute(
        edge_rows(0), "rows", [(i + 1, i) for i in range(count - 1)]
    ).reshape(planes, sent, cols)[:, :HALO]
    ext = jnp.concatenate(
        [jnp.transpose(piece, (1, 2, 0)) for piece in (below, stacked, above)], axis=0
    )
    ext = extended(ext, (("cols", 1),), HALO)
    ext = jnp.pad(
        ext, ((0, 0), (0, half + sublanes - ext.shape[1]), (0, lanes - ext.shape[2]))
    )

    row_at = lax.axis_index("rows") * rows - HALO + lax.iota(jnp.int32, slab_rows)
    row_in = ((row_at >= 0) & (row_at < rows * lax.axis_size("rows"))).astype(jnp.float32)
    col_in = []
    col_inner = []
    for h in range(2):
        at = lax.iota(jnp.int32, sublanes)
        col_at = lax.axis_index("cols") * cols - HALO + h * half + at
        col_in.append((col_at >= 0) & (col_at < cols * lax.axis_size("cols")) & (at < width))
        col_inner.append((at >= HALO) & (at < HALO + half))

    def on_lanes_of(columns):
        return jnp.concatenate(
            [jnp.broadcast_to(c[:, None], (sublanes, probe_count)) for c in columns], axis=1
        ).astype(jnp.float32)

    inside = on_lanes_of(col_in)
    inner = on_lanes_of(col_inner)
    lane_col = lax.iota(jnp.int32, lanes) % half + HALO
    diagonal = (lax.iota(jnp.int32, sublanes)[:, None] == lane_col[None, :]).astype(jnp.float32)
    plan = _Plan(slab_rows, HALO, rows, half)

    field = jax.ShapeDtypeStruct((slab_rows, sublanes, lanes), jnp.float32)
    lane_row = jax.ShapeDtypeStruct((1, lanes), jnp.float32)
    out_plane = jax.ShapeDtypeStruct((rows, cols), jnp.float32)

    z, gain, weight, stiff_probe, applied, first, stiff_obs = _call(
        _first_kernel, plan, (ext, inside, row_in, inner, diagonal),
        (field, field, field, field, field, jax.ShapeDtypeStruct((2, lanes), jnp.float32), out_plane),
        scratch=2, smem=(2,),
    )
    first = all_sum(first)
    residual, rr = _row_call(_start_kernel, plan, (first, z, applied, inner), (1, 2), (field, lane_row))
    directions = [z]
    ratios = [first, first]
    direction = z
    norm_now = first
    for iteration in range(1, ITERS):
        norm_next = all_sum(rr)
        direction, applied, pa = _call(
            _direction_kernel, plan,
            (norm_next, norm_now, residual, direction, gain, weight, inside, row_in, inner),
            (field, field, lane_row), scratch=1, smem=(7,),
        )
        norm_now = norm_next
        curvature = all_sum(pa)
        directions.append(direction)
        ratios += [norm_now, curvature]
        if iteration + 1 < ITERS:
            residual, rr = _row_call(
                _update_kernel, plan, (norm_now, curvature, residual, applied, inner), (2, 3),
                (field, lane_row),
            )

    grad_kappa, grad_weight = _call(
        _final_kernel, plan,
        (*ratios, *directions, z, stiff_probe, gain, stiff_obs, observed, variance_weight, diagonal),
        (out_plane, out_plane), scratch=1, field=field,
    )
    return (grad_kappa, grad_weight)


def solution(mesh):
    placed = (P(None, "rows", "cols"), P("rows", "cols"), P("rows", "cols"), P("rows", "cols"))
    return jax.shard_map(
        on_device,
        mesh=mesh,
        in_specs=placed,
        out_specs=(P("rows", "cols"), P("rows", "cols")),
        check_vma=False,
    )
```

```python
import jax
import jax.numpy as jnp
from jax import lax
from jax.experimental import pallas as pl
from jax.experimental.pallas import tpu as pltpu
from jax.sharding import PartitionSpec as P

ITERS = 3
HALO = 2 * ITERS


def extended(cells, sides, width):
    for axis, dim in sides:
        count = lax.axis_size(axis)
        ends = count - 1
        head = lax.slice_in_dim(cells, 0, width, axis=dim)
        tail = lax.slice_in_dim(cells, cells.shape[dim] - width, cells.shape[dim], axis=dim)
        cells = jnp.concatenate(
            [
                lax.ppermute(tail, axis, [(i, (i + 1) % count) for i in range(ends)]),
                cells,
                lax.ppermute(head, axis, [((i + 1) % count, i) for i in range(ends)]),
            ],
            axis=dim,
        )
    return cells


def stencil(padded, kappa_sq):
    centre = padded[..., 1:-1, 1:-1]
    edge_sum = (
        padded[..., :-2, 1:-1]
        + padded[..., 2:, 1:-1]
        + padded[..., 1:-1, :-2]
        + padded[..., 1:-1, 2:]
    )
    corners = (
        padded[..., :-2, :-2] + padded[..., :-2, 2:] + padded[..., 2:, :-2] + padded[..., 2:, 2:]
    )
    return (kappa_sq + 20.0 / 6.0) * centre - (4.0 * edge_sum + corners) / 6.0


def stiffen(field, kappa_sq):
    pads = ((0, 0),) * (field.ndim - 2) + ((1, 1), (1, 1))
    return stencil(jnp.pad(field, pads), kappa_sq)


def _span_sum(terms, basis, partner):
    if not basis:
        return partner(0)
    *rest, top = basis
    return _span_sum(terms, rest, partner) + _span_sum(terms, rest, lambda m: partner(m ^ top))


def all_sum(terms):
    axes = ("rows", "cols")
    count = lax.axis_size("rows") * lax.axis_size("cols")
    if count & (count - 1):
        for axis in axes:
            terms = lax.psum(terms, axis)
        return terms
    bits = [1 << k for k in range(count.bit_length() - 1)]
    groups = [bits[:1]] + [bits[k : k + 2] for k in range(1, len(bits), 2)]
    for basis in groups:
        received = {}

        def partner(mask, terms=terms, received=received):
            if mask == 0:
                return terms
            if mask not in received:
                received[mask] = lax.ppermute(terms, axes, [(i, i ^ mask) for i in range(count)])
            return received[mask]

        terms = _span_sum(terms, basis, partner)
    return terms


def _stiffen_row(ref, r, gain):
    mid = ref[r]
    vertical = ref[r - 1] + ref[r + 1]
    n = mid.shape[0]
    edge_sum = vertical + pltpu.roll(mid, 1, 0) + pltpu.roll(mid, n - 1, 0)
    corners = pltpu.roll(vertical, 1, 0) + pltpu.roll(vertical, n - 1, 0)
    return gain * mid - (4.0 * edge_sum + corners) * (1.0 / 6.0)


def _total(ref, row):
    value = ref[row : row + 1, :]
    return value + pltpu.roll(value, value.shape[1] // 2, 1)


def _ratio(num_ref, num_row, den_ref, den_row):
    return _total(num_ref, num_row) / _total(den_ref, den_row)


def _row_sum(value, keep):
    return jnp.sum(jnp.where(keep, value, 0.0), axis=0, keepdims=True)


class _Plan:
    def __init__(self, slab_rows, first_inner, inner_rows, half):
        self.half = half
        self.slab_rows = slab_rows
        self.first_inner = first_inner
        self.inner_rows = inner_rows

    def span(self, halo):
        return self.first_inner - halo, self.first_inner + self.inner_rows + halo

    def inner_row(self, r):
        return (r >= self.first_inner) & (r < self.first_inner + self.inner_rows)


def _zero_edges(ref):
    ref[0] = jnp.zeros(ref.shape[1:], ref.dtype)
    ref[ref.shape[0] - 1] = jnp.zeros(ref.shape[1:], ref.dtype)


def _apply_q(plan, reach, source, gain_ref, weight_ref, inside_ref, row_ref, inner_ref, stiff_ref,
             applied_ref, dot_source):

    def first_pass(r, carry):
        stiff_ref[r] = weight_ref[r] * _stiffen_row(source, r, gain_ref[r])
        return carry

    lax.fori_loop(*plan.span(reach + 1), first_pass, 0)

    def second_pass(r, totals):
        applied = _stiffen_row(stiff_ref, r, gain_ref[r])
        keep = (inside_ref[...] > 0.5) & (row_ref[r] > 0.5)
        applied = jnp.where(keep, applied, 0.0)
        applied_ref[r] = applied
        inner = (inner_ref[...] > 0.5) & plan.inner_row(r)
        return totals + _row_sum(dot_source[r] * applied, inner)

    return lax.fori_loop(*plan.span(reach), second_pass, jnp.zeros((1, source.shape[2]), jnp.float32))


def _spread(value, lane):
    return jnp.broadcast_to(value[:, lane : lane + 1], value.shape)


def _plane_row(value, diagonal):
    return jnp.sum(jnp.where(diagonal, value, 0.0), axis=0, keepdims=True)


def _first_kernel(plan, ext_ref, inside_ref, row_ref, inner_ref, diagonal_ref,
                  z_out, gain_out, weight_out, stiff_out, applied_out, dots_out, stiff_obs_out,
                  observed_scr, scratch):
    sublanes = z_out.shape[1]
    lanes = z_out.shape[2]
    probes = lanes // 2

    def relayout(r, carry):
        cells = ext_ref[r]
        left = cells[0:sublanes]
        right = cells[plan.half : plan.half + sublanes]
        low = lax.broadcasted_iota(jnp.int32, (sublanes, lanes), 1) < probes
        z_out[r] = jnp.where(low, left, pltpu.roll(right, probes, 1))
        observed_scr[r] = jnp.where(low, _spread(left, probes), _spread(right, probes))
        gain_out[r] = jnp.where(low, _spread(left, probes + 1), _spread(right, probes + 1)) + 20.0 / 6.0
        weight_out[r] = jnp.where(low, _spread(left, probes + 2), _spread(right, probes + 2))
        return carry

    lax.fori_loop(0, plan.slab_rows, relayout, 0)
    reach = 2 * (ITERS - 1)

    def probe_pass(r, totals):
        stiffness = _stiffen_row(z_out, r, gain_out[r])
        stiff_out[r] = stiffness
        scratch[r] = weight_out[r] * stiffness
        z = z_out[r]
        inner = (inner_ref[...] > 0.5) & plan.inner_row(r)
        return totals + _row_sum(z * z, inner)

    zz = lax.fori_loop(*plan.span(reach + 1), probe_pass, jnp.zeros((1, lanes), jnp.float32))

    def second_pass(r, totals):
        applied = _stiffen_row(scratch, r, gain_out[r])
        keep = (inside_ref[...] > 0.5) & (row_ref[r] > 0.5)
        applied = jnp.where(keep, applied, 0.0)
        applied_out[r] = applied
        inner = (inner_ref[...] > 0.5) & plan.inner_row(r)
        return totals + _row_sum(z_out[r] * applied, inner)

    za = lax.fori_loop(*plan.span(reach), second_pass, jnp.zeros((1, lanes), jnp.float32))
    dots_out[0:1, :] = zz
    dots_out[1:2, :] = za

    def observed_pass(r, carry):
        stiff_obs = _stiffen_row(observed_scr, plan.first_inner + r, gain_out[plan.first_inner + r])
        stiff_obs_out[pl.ds(r, 1), :] = _plane_row(stiff_obs, diagonal_ref[...] > 0.5)
        return carry

    lax.fori_loop(0, plan.inner_rows, observed_pass, 0)


def _start_kernel(plan, first_ref, z_ref, applied_ref, inner_ref, residual_out, rr_out):
    step = _ratio(first_ref, 0, first_ref, 1)

    def body(r, totals):
        residual = z_ref[r] - step * applied_ref[r]
        residual_out[r] = residual
        inner = (inner_ref[...] > 0.5) & plan.inner_row(r)
        return totals + _row_sum(residual * residual, inner)

    rr_out[...] = lax.fori_loop(
        *plan.span(2 * (ITERS - 1)), body, jnp.zeros((1, z_ref.shape[2]), jnp.float32)
    )


def _update_kernel(plan, reach, norm_ref, curvature_ref, residual_ref, applied_ref, inner_ref,
                   residual_out, rr_out):
    step = _ratio(norm_ref, 0, curvature_ref, 0)

    def body(r, totals):
        residual = residual_ref[r] - step * applied_ref[r]
        residual_out[r] = residual
        inner = (inner_ref[...] > 0.5) & plan.inner_row(r)
        return totals + _row_sum(residual * residual, inner)

    rr_out[...] = lax.fori_loop(
        *plan.span(reach), body, jnp.zeros((1, residual_ref.shape[2]), jnp.float32)
    )


def _direction_kernel(plan, reach, next_ref, now_ref, residual_ref, direction_ref, gain_ref,
                      weight_ref, inside_ref, row_ref, inner_ref, direction_out, applied_out, pa_out,
                      scratch):
    beta = _ratio(next_ref, 0, now_ref, 0)

    def new_direction(r, carry):
        direction_out[r] = residual_ref[r] + beta * direction_ref[r]
        return carry

    lax.fori_loop(*plan.span(reach + 2), new_direction, 0)
    pa_out[...] = _apply_q(plan, reach, direction_out, gain_ref, weight_ref, inside_ref, row_ref, inner_ref,
                           scratch, applied_out, direction_out)


def _final_kernel(plan, *refs):
    steps = ITERS
    ratio_refs = refs[: 2 * steps]
    direction_refs = refs[2 * steps : 3 * steps]
    (z_ref, stiff_ref, gain_ref, stiff_obs_ref, observed_ref, weight_ref, diagonal_ref,
     grad_kappa_out, grad_weight_out, scratch) = refs[3 * steps :]
    lanes = z_ref.shape[2]
    probes = lanes // 2
    step_lens = []
    for k in range(steps):
        num_ref, den_ref = ratio_refs[2 * k], ratio_refs[2 * k + 1]
        step_lens.append(_ratio(num_ref, 0, den_ref, 1 if k == 0 else 0))

    def new_solution(r, carry):
        solution = step_lens[0] * direction_refs[0][r]
        for k in range(1, steps):
            solution = solution + step_lens[k] * direction_refs[k][r]
        scratch[r] = solution
        return carry

    lax.fori_loop(*plan.span(1), new_solution, 0)

    def probe_sum(value, low):
        first = jnp.sum(jnp.where(low, value, 0.0), axis=1, keepdims=True)
        second = jnp.sum(jnp.where(low, 0.0, value), axis=1, keepdims=True)
        return jnp.where(low, first, second)

    def body(i, carry):
        r = plan.first_inner + i
        solution = scratch[r]
        stiff_solution = _stiffen_row(scratch, r, gain_ref[r])
        stiff_probe = stiff_ref[r]
        low = lax.broadcasted_iota(jnp.int32, solution.shape, 1) < probes
        diagonal = diagonal_ref[...] > 0.5
        weight_total = _plane_row(probe_sum(stiff_solution * stiff_probe, low), diagonal)
        kappa_total = _plane_row(
            probe_sum(solution * stiff_probe + stiff_solution * z_ref[r], low), diagonal
        )
        stiff_obs = stiff_obs_ref[pl.ds(i, 1), :]
        observed = observed_ref[pl.ds(i, 1), :]
        weight = weight_ref[pl.ds(i, 1), :]
        grad_weight_out[pl.ds(i, 1), :] = (
            0.5 * weight_total / probes - 0.5 * stiff_obs * stiff_obs
        )
        grad_kappa_out[pl.ds(i, 1), :] = (
            0.5 * weight * (kappa_total / probes) - observed * weight * stiff_obs
        )
        return carry

    lax.fori_loop(0, plan.inner_rows, body, 0)


def _vmem():
    return pl.BlockSpec(memory_space=pltpu.VMEM)


def _call(kernel, plan, inputs, out_shapes, scratch=0, smem=(), field=None):
    field = out_shapes[0] if field is None else field
    nbytes = 4 * field.shape[0] * field.shape[1] * field.shape[2]
    in_specs = [
        pl.BlockSpec(memory_space=pltpu.SMEM) if i in smem else _vmem() for i in range(len(inputs))
    ]
    return pl.pallas_call(
        lambda *refs: kernel(plan, *refs),
        out_shape=out_shapes,
        in_specs=in_specs,
        out_specs=tuple(_vmem() for _ in out_shapes),
        scratch_shapes=[pltpu.VMEM(field.shape, jnp.float32)] * scratch,
        cost_estimate=pl.CostEstimate(
            flops=40 * nbytes // 4,
            transcendentals=0,
            bytes_accessed=(len(inputs) + len(out_shapes)) * nbytes,
        ),
    )(*inputs)


def on_device(probes, observed, kappa_sq, variance_weight):
    probe_count, rows, cols = probes.shape
    half = cols // 2
    assert rows >= HALO and cols % 2 == 0 and half >= HALO and half == probe_count
    width = half + 2 * HALO
    sublanes = -(-width // 8) * 8
    slab_rows = rows + 2 * HALO
    lanes = 2 * probe_count
    stacked = jnp.concatenate(
        [probes, observed[None], kappa_sq[None], variance_weight[None]], axis=0
    )
    count = lax.axis_size("rows")
    sent = -(-HALO // 8) * 8
    assert sent <= rows
    planes = stacked.shape[0]
    fields = (probes, observed[None], kappa_sq[None], variance_weight[None])

    def edge_rows(start):
        rows_of = [lax.slice_in_dim(f, start, start + sent, axis=1) for f in fields]
        return jnp.concatenate(rows_of, axis=0).reshape(planes * sent, cols)

    below = lax.ppermute(
        edge_rows(rows - sent), "rows", [(i, i + 1) for i in range(count - 1)]
    ).reshape(planes, sent, cols)[:, sent - HALO :]
    above = lax.ppermute(
        edge_rows(0), "rows", [(i + 1, i) for i in range(count - 1)]
    ).reshape(planes, sent, cols)[:, :HALO]
    ext = jnp.concatenate(
        [jnp.transpose(piece, (1, 2, 0)) for piece in (below, stacked, above)], axis=0
    )
    ext = extended(ext, (("cols", 1),), HALO)
    ext = jnp.pad(
        ext, ((0, 0), (0, half + sublanes - ext.shape[1]), (0, lanes - ext.shape[2]))
    )

    row_at = lax.axis_index("rows") * rows - HALO + lax.iota(jnp.int32, slab_rows)
    row_in = ((row_at >= 0) & (row_at < rows * lax.axis_size("rows"))).astype(jnp.float32)
    col_in = []
    col_inner = []
    for h in range(2):
        at = lax.iota(jnp.int32, sublanes)
        col_at = lax.axis_index("cols") * cols - HALO + h * half + at
        col_in.append((col_at >= 0) & (col_at < cols * lax.axis_size("cols")) & (at < width))
        col_inner.append((at >= HALO) & (at < HALO + half))

    def on_lanes_of(columns):
        return jnp.concatenate(
            [jnp.broadcast_to(c[:, None], (sublanes, probe_count)) for c in columns], axis=1
        ).astype(jnp.float32)

    inside = on_lanes_of(col_in)
    inner = on_lanes_of(col_inner)
    lane_col = lax.iota(jnp.int32, lanes) % half + HALO
    diagonal = (lax.iota(jnp.int32, sublanes)[:, None] == lane_col[None, :]).astype(jnp.float32)
    plan = _Plan(slab_rows, HALO, rows, half)

    field = jax.ShapeDtypeStruct((slab_rows, sublanes, lanes), jnp.float32)
    lane_row = jax.ShapeDtypeStruct((1, lanes), jnp.float32)
    out_plane = jax.ShapeDtypeStruct((rows, cols), jnp.float32)

    z, gain, weight, stiff_probe, applied, first, stiff_obs = _call(
        _first_kernel, plan, (ext, inside, row_in, inner, diagonal),
        (field, field, field, field, field, jax.ShapeDtypeStruct((2, lanes), jnp.float32), out_plane),
        scratch=2, smem=(2,),
    )
    first = all_sum(first)
    residual, rr = _call(_start_kernel, plan, (first, z, applied, inner), (field, lane_row))
    directions = [z]
    ratios = [first, first]
    direction = z
    norm_now = first
    for iteration in range(1, ITERS):
        norm_next = all_sum(rr)
        reach = 2 * (ITERS - 1 - iteration)
        direction, applied, pa = _call(
            lambda plan, *refs, reach=reach: _direction_kernel(plan, reach, *refs), plan,
            (norm_next, norm_now, residual, direction, gain, weight, inside, row_in, inner),
            (field, field, lane_row), scratch=1, smem=(7,),
        )
        norm_now = norm_next
        curvature = all_sum(pa)
        directions.append(direction)
        ratios += [norm_now, curvature]
        if iteration + 1 < ITERS:
            residual, rr = _call(
                lambda plan, *refs, reach=reach: _update_kernel(plan, reach, *refs), plan, (norm_now, curvature, residual, applied, inner),
                (field, lane_row),
            )

    grad_kappa, grad_weight = _call(
        _final_kernel, plan,
        (*ratios, *directions, z, stiff_probe, gain, stiff_obs, observed, variance_weight, diagonal),
        (out_plane, out_plane), scratch=1, field=field,
    )
    return (grad_kappa, grad_weight)


def solution(mesh):
    placed = (P(None, "rows", "cols"), P("rows", "cols"), P("rows", "cols"), P("rows", "cols"))
    return jax.shard_map(
        on_device,
        mesh=mesh,
        in_specs=placed,
        out_specs=(P("rows", "cols"), P("rows", "cols")),
        check_vma=False,
    )
```

```python
import jax
import jax.numpy as jnp
from jax import lax
from jax.experimental import pallas as pl
from jax.experimental.pallas import tpu as pltpu
from jax.sharding import PartitionSpec as P


ITERS = 3
HALO = 2 * ITERS


def extended(cells, sides, width):
    for axis, dim in sides:
        count = lax.axis_size(axis)
        ends = count - 1
        head = lax.slice_in_dim(cells, 0, width, axis=dim)
        tail = lax.slice_in_dim(cells, cells.shape[dim] - width, cells.shape[dim], axis=dim)
        cells = jnp.concatenate(
            [
                lax.ppermute(tail, axis, [(i, (i + 1) % count) for i in range(ends)]),
                cells,
                lax.ppermute(head, axis, [((i + 1) % count, i) for i in range(ends)]),
            ],
            axis=dim,
        )
    return cells


def _span_sum(terms, basis, partner):
    if not basis:
        return partner(0)
    *rest, top = basis
    return _span_sum(terms, rest, partner) + _span_sum(terms, rest, lambda m: partner(m ^ top))


def all_sum(terms):
    axes = ("rows", "cols")
    count = lax.axis_size("rows") * lax.axis_size("cols")
    if count & (count - 1):
        for axis in axes:
            terms = lax.psum(terms, axis)
        return terms
    bits = [1 << k for k in range(count.bit_length() - 1)]
    groups = [bits[:1]] + [bits[k : k + 2] for k in range(1, len(bits), 2)]
    for basis in groups:
        received = {}

        def partner(mask, terms=terms, received=received):
            if mask == 0:
                return terms
            if mask not in received:
                received[mask] = lax.ppermute(terms, axes, [(i, i ^ mask) for i in range(count)])
            return received[mask]

        terms = _span_sum(terms, basis, partner)
    return terms


def _stiffen_row(ref, r, gain):
    mid = ref[r]
    vertical = ref[r - 1] + ref[r + 1]
    n = mid.shape[0]
    edge_sum = vertical + pltpu.roll(mid, 1, 0) + pltpu.roll(mid, n - 1, 0)
    corners = pltpu.roll(vertical, 1, 0) + pltpu.roll(vertical, n - 1, 0)
    return gain * mid - (4.0 * edge_sum + corners) * (1.0 / 6.0)


def _total(ref, row):
    value = ref[row : row + 1, :]
    return value + pltpu.roll(value, value.shape[1] // 2, 1)


def _ratio(num_ref, num_row, den_ref, den_row):
    return _total(num_ref, num_row) / _total(den_ref, den_row)


def _row_sum(value, keep):
    return jnp.sum(jnp.where(keep, value, 0.0), axis=0, keepdims=True)


class _Plan:
    def __init__(self, slab_rows, first_inner, inner_rows, half):
        self.half = half
        self.slab_rows = slab_rows
        self.first_inner = first_inner
        self.inner_rows = inner_rows

    def span(self, halo):
        return self.first_inner - halo, self.first_inner + self.inner_rows + halo

    def inner_row(self, r):
        return (r >= self.first_inner) & (r < self.first_inner + self.inner_rows)


def _apply_q(plan, reach, source, gain_ref, weight_ref, inside_ref, row_ref, inner_ref, stiff_ref,
             applied_ref, dot_source):

    def first_pass(r, carry):
        stiff_ref[r] = weight_ref[r] * _stiffen_row(source, r, gain_ref[r])
        return carry

    lax.fori_loop(*plan.span(reach + 1), first_pass, 0)

    def second_pass(r, totals):
        applied = _stiffen_row(stiff_ref, r, gain_ref[r])
        keep = (inside_ref[...] > 0.5) & (row_ref[r] > 0.5)
        applied = jnp.where(keep, applied, 0.0)
        applied_ref[r] = applied
        inner = (inner_ref[...] > 0.5) & plan.inner_row(r)
        return totals + _row_sum(dot_source[r] * applied, inner)

    return lax.fori_loop(*plan.span(reach), second_pass, jnp.zeros((1, source.shape[2]), jnp.float32))


def _spread(value, lane):
    return jnp.broadcast_to(value[:, lane : lane + 1], value.shape)


def _plane_row(value, diagonal):
    return jnp.sum(jnp.where(diagonal, value, 0.0), axis=0, keepdims=True)


def _first_kernel(plan, ext_ref, inside_ref, row_ref, inner_ref, diagonal_ref,
                  z_out, gain_out, weight_out, stiff_out, applied_out, dots_out, observed_scr,
                  scratch):
    sublanes = z_out.shape[1]
    lanes = z_out.shape[2]
    probes = lanes // 2

    def relayout(r, carry):
        cells = ext_ref[r]
        left = cells[0:sublanes]
        right = cells[plan.half : plan.half + sublanes]
        low = lax.broadcasted_iota(jnp.int32, (sublanes, lanes), 1) < probes
        z_out[r] = jnp.where(low, left, pltpu.roll(right, probes, 1))
        observed_scr[r] = jnp.where(low, _spread(left, probes), _spread(right, probes))
        gain_out[r] = jnp.where(low, _spread(left, probes + 1), _spread(right, probes + 1)) + 20.0 / 6.0
        weight_out[r] = jnp.where(low, _spread(left, probes + 2), _spread(right, probes + 2))
        return carry

    lax.fori_loop(0, plan.slab_rows, relayout, 0)
    reach = 2 * (ITERS - 1)

    def probe_pass(r, totals):
        stiffness = _stiffen_row(z_out, r, gain_out[r])
        stiff_out[r] = stiffness
        scratch[r] = weight_out[r] * stiffness
        z = z_out[r]
        inner = (inner_ref[...] > 0.5) & plan.inner_row(r)
        return totals + _row_sum(z * z, inner)

    zz = lax.fori_loop(*plan.span(reach + 1), probe_pass, jnp.zeros((1, lanes), jnp.float32))

    def second_pass(r, totals):
        applied = _stiffen_row(scratch, r, gain_out[r])
        keep = (inside_ref[...] > 0.5) & (row_ref[r] > 0.5)
        applied = jnp.where(keep, applied, 0.0)
        applied_out[r] = applied
        inner = (inner_ref[...] > 0.5) & plan.inner_row(r)
        return totals + _row_sum(z_out[r] * applied, inner)

    za = lax.fori_loop(*plan.span(reach), second_pass, jnp.zeros((1, lanes), jnp.float32))
    dots_out[0:1, :] = zz
    dots_out[1:2, :] = za


def _observed_kernel(plan, observed_ref, gain_ref, diagonal_ref, stiff_obs_out):
    def observed_pass(r, carry):
        row = plan.first_inner + r
        stiff_obs = _stiffen_row(observed_ref, row, gain_ref[row])
        stiff_obs_out[pl.ds(r, 1), :] = _plane_row(stiff_obs, diagonal_ref[...] > 0.5)
        return carry

    lax.fori_loop(0, plan.inner_rows, observed_pass, 0)


def _start_kernel(plan, first_ref, z_ref, applied_ref, inner_ref, residual_out, rr_out):
    step = _ratio(first_ref, 0, first_ref, 1)

    def body(r, totals):
        residual = z_ref[r] - step * applied_ref[r]
        residual_out[r] = residual
        inner = (inner_ref[...] > 0.5) & plan.inner_row(r)
        return totals + _row_sum(residual * residual, inner)

    rr_out[...] = lax.fori_loop(
        *plan.span(2 * (ITERS - 1)), body, jnp.zeros((1, z_ref.shape[2]), jnp.float32)
    )


def _update_kernel(plan, reach, norm_ref, curvature_ref, residual_ref, applied_ref, inner_ref,
                   residual_out, rr_out):
    step = _ratio(norm_ref, 0, curvature_ref, 0)

    def body(r, totals):
        residual = residual_ref[r] - step * applied_ref[r]
        residual_out[r] = residual
        inner = (inner_ref[...] > 0.5) & plan.inner_row(r)
        return totals + _row_sum(residual * residual, inner)

    rr_out[...] = lax.fori_loop(
        *plan.span(reach), body, jnp.zeros((1, residual_ref.shape[2]), jnp.float32)
    )


def _direction_kernel(plan, reach, next_ref, now_ref, residual_ref, direction_ref, gain_ref,
                      weight_ref, inside_ref, row_ref, inner_ref, direction_out, applied_out, pa_out,
                      scratch):
    beta = _ratio(next_ref, 0, now_ref, 0)

    def new_direction(r, carry):
        direction_out[r] = residual_ref[r] + beta * direction_ref[r]
        return carry

    lax.fori_loop(*plan.span(reach + 2), new_direction, 0)
    pa_out[...] = _apply_q(plan, reach, direction_out, gain_ref, weight_ref, inside_ref, row_ref, inner_ref,
                           scratch, applied_out, direction_out)


def _final_kernel(plan, *refs):
    steps = ITERS
    ratio_refs = refs[: 2 * steps]
    direction_refs = refs[2 * steps : 3 * steps]
    (z_ref, stiff_ref, gain_ref, stiff_obs_ref, observed_ref, weight_ref, diagonal_ref,
     grad_kappa_out, grad_weight_out, scratch) = refs[3 * steps :]
    lanes = z_ref.shape[2]
    probes = lanes // 2
    step_lens = []
    for k in range(steps):
        num_ref, den_ref = ratio_refs[2 * k], ratio_refs[2 * k + 1]
        step_lens.append(_ratio(num_ref, 0, den_ref, 1 if k == 0 else 0))

    def new_solution(r, carry):
        solution = step_lens[0] * direction_refs[0][r]
        for k in range(1, steps):
            solution = solution + step_lens[k] * direction_refs[k][r]
        scratch[r] = solution
        return carry

    lax.fori_loop(*plan.span(1), new_solution, 0)

    def probe_sum(value, low):
        first = jnp.sum(jnp.where(low, value, 0.0), axis=1, keepdims=True)
        second = jnp.sum(jnp.where(low, 0.0, value), axis=1, keepdims=True)
        return jnp.where(low, first, second)

    def body(i, carry):
        r = plan.first_inner + i
        solution = scratch[r]
        stiff_solution = _stiffen_row(scratch, r, gain_ref[r])
        stiff_probe = stiff_ref[r]
        low = lax.broadcasted_iota(jnp.int32, solution.shape, 1) < probes
        diagonal = diagonal_ref[...] > 0.5
        weight_total = _plane_row(probe_sum(stiff_solution * stiff_probe, low), diagonal)
        kappa_total = _plane_row(
            probe_sum(solution * stiff_probe + stiff_solution * z_ref[r], low), diagonal
        )
        stiff_obs = stiff_obs_ref[pl.ds(i, 1), :]
        observed = observed_ref[pl.ds(i, 1), :]
        weight = weight_ref[pl.ds(i, 1), :]
        grad_weight_out[pl.ds(i, 1), :] = (
            0.5 * weight_total / probes - 0.5 * stiff_obs * stiff_obs
        )
        grad_kappa_out[pl.ds(i, 1), :] = (
            0.5 * weight * (kappa_total / probes) - observed * weight * stiff_obs
        )
        return carry

    lax.fori_loop(0, plan.inner_rows, body, 0)


def _vmem():
    return pl.BlockSpec(memory_space=pltpu.VMEM)


def _call(kernel, plan, inputs, out_shapes, scratch=0, smem=(), field=None):
    field = out_shapes[0] if field is None else field
    nbytes = 4 * field.shape[0] * field.shape[1] * field.shape[2]
    in_specs = [
        pl.BlockSpec(memory_space=pltpu.SMEM) if i in smem else _vmem() for i in range(len(inputs))
    ]
    return pl.pallas_call(
        lambda *refs: kernel(plan, *refs),
        out_shape=out_shapes,
        in_specs=in_specs,
        out_specs=tuple(_vmem() for _ in out_shapes),
        scratch_shapes=[pltpu.VMEM(field.shape, jnp.float32)] * scratch,
        cost_estimate=pl.CostEstimate(
            flops=40 * nbytes // 4,
            transcendentals=0,
            bytes_accessed=(len(inputs) + len(out_shapes)) * nbytes,
        ),
    )(*inputs)


def on_device(probes, observed, kappa_sq, variance_weight):
    probe_count, rows, cols = probes.shape
    half = cols // 2
    assert rows >= HALO and cols % 2 == 0 and half >= HALO and half == probe_count
    width = half + 2 * HALO
    sublanes = -(-width // 8) * 8
    slab_rows = rows + 2 * HALO
    lanes = 2 * probe_count
    stacked = jnp.concatenate(
        [probes, observed[None], kappa_sq[None], variance_weight[None]], axis=0
    )
    count = lax.axis_size("rows")
    sent = -(-HALO // 8) * 8
    assert sent <= rows
    planes = stacked.shape[0]
    fields = (probes, observed[None], kappa_sq[None], variance_weight[None])

    def edge_rows(start):
        rows_of = [lax.slice_in_dim(f, start, start + sent, axis=1) for f in fields]
        return jnp.concatenate(rows_of, axis=0).reshape(planes * sent, cols)

    below = lax.ppermute(
        edge_rows(rows - sent), "rows", [(i, i + 1) for i in range(count - 1)]
    ).reshape(planes, sent, cols)[:, sent - HALO :]
    above = lax.ppermute(
        edge_rows(0), "rows", [(i + 1, i) for i in range(count - 1)]
    ).reshape(planes, sent, cols)[:, :HALO]
    ext = jnp.concatenate(
        [jnp.transpose(piece, (1, 2, 0)) for piece in (below, stacked, above)], axis=0
    )
    ext = extended(ext, (("cols", 1),), HALO)
    ext = jnp.pad(
        ext, ((0, 0), (0, half + sublanes - ext.shape[1]), (0, lanes - ext.shape[2]))
    )

    row_at = lax.axis_index("rows") * rows - HALO + lax.iota(jnp.int32, slab_rows)
    row_in = ((row_at >= 0) & (row_at < rows * lax.axis_size("rows"))).astype(jnp.float32)
    col_in = []
    col_inner = []
    for h in range(2):
        at = lax.iota(jnp.int32, sublanes)
        col_at = lax.axis_index("cols") * cols - HALO + h * half + at
        col_in.append((col_at >= 0) & (col_at < cols * lax.axis_size("cols")) & (at < width))
        col_inner.append((at >= HALO) & (at < HALO + half))

    def on_lanes_of(columns):
        return jnp.concatenate(
            [jnp.broadcast_to(c[:, None], (sublanes, probe_count)) for c in columns], axis=1
        ).astype(jnp.float32)

    inside = on_lanes_of(col_in)
    inner = on_lanes_of(col_inner)
    lane_col = lax.iota(jnp.int32, lanes) % half + HALO
    diagonal = (lax.iota(jnp.int32, sublanes)[:, None] == lane_col[None, :]).astype(jnp.float32)
    plan = _Plan(slab_rows, HALO, rows, half)

    field = jax.ShapeDtypeStruct((slab_rows, sublanes, lanes), jnp.float32)
    lane_row = jax.ShapeDtypeStruct((1, lanes), jnp.float32)
    out_plane = jax.ShapeDtypeStruct((rows, cols), jnp.float32)

    z, gain, weight, stiff_probe, applied, first, observed_lanes = _call(
        _first_kernel, plan, (ext, inside, row_in, inner, diagonal),
        (field, field, field, field, field, jax.ShapeDtypeStruct((2, lanes), jnp.float32), field),
        scratch=1, smem=(2,),
    )
    (stiff_obs,) = _call(
        _observed_kernel, plan, (observed_lanes, gain, diagonal), (out_plane,), field=field
    )
    first = all_sum(first)
    residual, rr = _call(_start_kernel, plan, (first, z, applied, inner), (field, lane_row))
    directions = [z]
    ratios = [first, first]
    direction = z
    norm_now = first
    for iteration in range(1, ITERS):
        norm_next = all_sum(rr)
        reach = 2 * (ITERS - 1 - iteration)
        direction, applied, pa = _call(
            lambda plan, *refs, reach=reach: _direction_kernel(plan, reach, *refs), plan,
            (norm_next, norm_now, residual, direction, gain, weight, inside, row_in, inner),
            (field, field, lane_row), scratch=1, smem=(7,),
        )
        norm_now = norm_next
        curvature = all_sum(pa)
        directions.append(direction)
        ratios += [norm_now, curvature]
        if iteration + 1 < ITERS:
            residual, rr = _call(
                lambda plan, *refs, reach=reach: _update_kernel(plan, reach, *refs), plan, (norm_now, curvature, residual, applied, inner),
                (field, lane_row),
            )

    grad_kappa, grad_weight = _call(
        _final_kernel, plan,
        (*ratios, *directions, z, stiff_probe, gain, stiff_obs, observed, variance_weight, diagonal),
        (out_plane, out_plane), scratch=1, field=field,
    )
    return (grad_kappa, grad_weight)


def solution(mesh):
    placed = (P(None, "rows", "cols"), P("rows", "cols"), P("rows", "cols"), P("rows", "cols"))
    return jax.shard_map(
        on_device,
        mesh=mesh,
        in_specs=placed,
        out_specs=(P("rows", "cols"), P("rows", "cols")),
        check_vma=False,
    )
```

```python
import jax
import jax.numpy as jnp
from jax import lax
from jax.experimental import pallas as pl
from jax.experimental.pallas import tpu as pltpu
from jax.sharding import PartitionSpec as P

ITERS = 3
HALO = 2 * ITERS


def extended(cells, sides, width):
    for axis, dim in sides:
        count = lax.axis_size(axis)
        ends = count - 1
        head = lax.slice_in_dim(cells, 0, width, axis=dim)
        tail = lax.slice_in_dim(cells, cells.shape[dim] - width, cells.shape[dim], axis=dim)
        cells = jnp.concatenate(
            [
                lax.ppermute(tail, axis, [(i, (i + 1) % count) for i in range(ends)]),
                cells,
                lax.ppermute(head, axis, [((i + 1) % count, i) for i in range(ends)]),
            ],
            axis=dim,
        )
    return cells


def stencil(padded, kappa_sq):
    centre = padded[..., 1:-1, 1:-1]
    edge_sum = (
        padded[..., :-2, 1:-1]
        + padded[..., 2:, 1:-1]
        + padded[..., 1:-1, :-2]
        + padded[..., 1:-1, 2:]
    )
    corners = (
        padded[..., :-2, :-2] + padded[..., :-2, 2:] + padded[..., 2:, :-2] + padded[..., 2:, 2:]
    )
    return (kappa_sq + 20.0 / 6.0) * centre - (4.0 * edge_sum + corners) / 6.0


def stiffen(field, kappa_sq):
    pads = ((0, 0),) * (field.ndim - 2) + ((1, 1), (1, 1))
    return stencil(jnp.pad(field, pads), kappa_sq)


def _span_sum(terms, basis, partner):
    if not basis:
        return partner(0)
    *rest, top = basis
    return _span_sum(terms, rest, partner) + _span_sum(terms, rest, lambda m: partner(m ^ top))


def all_sum(terms):
    axes = ("rows", "cols")
    count = lax.axis_size("rows") * lax.axis_size("cols")
    if count & (count - 1):
        for axis in axes:
            terms = lax.psum(terms, axis)
        return terms
    bits = [1 << k for k in range(count.bit_length() - 1)]
    groups = [bits[:1]] + [bits[k : k + 2] for k in range(1, len(bits), 2)]
    for basis in groups:
        received = {}

        def partner(mask, terms=terms, received=received):
            if mask == 0:
                return terms
            if mask not in received:
                received[mask] = lax.ppermute(terms, axes, [(i, i ^ mask) for i in range(count)])
            return received[mask]

        terms = _span_sum(terms, basis, partner)
    return terms


def _stiffen_row(ref, r, gain):
    mid = ref[r]
    vertical = ref[r - 1] + ref[r + 1]
    n = mid.shape[0]
    edge_sum = vertical + pltpu.roll(mid, 1, 0) + pltpu.roll(mid, n - 1, 0)
    corners = pltpu.roll(vertical, 1, 0) + pltpu.roll(vertical, n - 1, 0)
    return gain * mid - (4.0 * edge_sum + corners) * (1.0 / 6.0)


def _total(ref, row):
    value = ref[row : row + 1, :]
    return value + pltpu.roll(value, value.shape[1] // 2, 1)


def _ratio(num_ref, num_row, den_ref, den_row):
    return _total(num_ref, num_row) / _total(den_ref, den_row)


def _row_sum(value, keep):
    return jnp.sum(jnp.where(keep, value, 0.0), axis=0, keepdims=True)


class _Plan:
    def __init__(self, slab_rows, first_inner, inner_rows, half):
        self.half = half
        self.slab_rows = slab_rows
        self.first_inner = first_inner
        self.inner_rows = inner_rows

    def span(self, halo):
        return self.first_inner - halo, self.first_inner + self.inner_rows + halo

    def inner_row(self, r):
        return (r >= self.first_inner) & (r < self.first_inner + self.inner_rows)


def _zero_edges(ref):
    ref[0] = jnp.zeros(ref.shape[1:], ref.dtype)
    ref[ref.shape[0] - 1] = jnp.zeros(ref.shape[1:], ref.dtype)


def _apply_q(plan, reach, source, gain_ref, weight_ref, inside_ref, row_ref, inner_ref, stiff_ref,
             applied_ref, dot_source):

    def first_pass(r, carry):
        stiff_ref[r] = weight_ref[r] * _stiffen_row(source, r, gain_ref[r])
        return carry

    lax.fori_loop(*plan.span(reach + 1), first_pass, 0)

    def second_pass(r, totals):
        applied = _stiffen_row(stiff_ref, r, gain_ref[r])
        keep = (inside_ref[...] > 0.5) & (row_ref[r] > 0.5)
        applied = jnp.where(keep, applied, 0.0)
        applied_ref[r] = applied
        inner = (inner_ref[...] > 0.5) & plan.inner_row(r)
        return totals + _row_sum(dot_source[r] * applied, inner)

    return lax.fori_loop(*plan.span(reach), second_pass, jnp.zeros((1, source.shape[2]), jnp.float32))


def _spread(value, lane):
    return jnp.broadcast_to(value[:, lane : lane + 1], value.shape)


def _plane_row(value, diagonal):
    return jnp.sum(jnp.where(diagonal, value, 0.0), axis=0, keepdims=True)


def _first_kernel(plan, ext_ref, inside_ref, row_ref, inner_ref, diagonal_ref,
                  z_out, gain_out, weight_out, stiff_out, applied_out, dots_out, stiff_obs_out,
                  observed_scr, scratch):
    sublanes = z_out.shape[1]
    lanes = z_out.shape[2]
    probes = lanes // 2

    reach = 2 * (ITERS - 1)

    def halves(r):
        cells = ext_ref[r]
        low = lax.broadcasted_iota(jnp.int32, (sublanes, lanes), 1) < probes
        return cells[0:sublanes], cells[plan.half : plan.half + sublanes], low

    def probe_rows(r, carry):
        left, right, low = halves(r)
        z_out[r] = jnp.where(low, left, pltpu.roll(right, probes, 1))
        return carry

    lax.fori_loop(0, plan.slab_rows, probe_rows, 0)

    def parameter_rows(r, carry):
        left, right, low = halves(r)
        gain_out[r] = jnp.where(low, _spread(left, probes + 1), _spread(right, probes + 1)) + 20.0 / 6.0
        weight_out[r] = jnp.where(low, _spread(left, probes + 2), _spread(right, probes + 2))
        return carry

    lax.fori_loop(*plan.span(reach + 1), parameter_rows, 0)

    def observed_rows(r, carry):
        left, right, low = halves(r)
        observed_scr[r] = jnp.where(low, _spread(left, probes), _spread(right, probes))
        return carry

    lax.fori_loop(*plan.span(1), observed_rows, 0)

    def probe_pass(r, totals):
        stiffness = _stiffen_row(z_out, r, gain_out[r])
        stiff_out[r] = stiffness
        scratch[r] = weight_out[r] * stiffness
        z = z_out[r]
        inner = (inner_ref[...] > 0.5) & plan.inner_row(r)
        return totals + _row_sum(z * z, inner)

    zz = lax.fori_loop(*plan.span(reach + 1), probe_pass, jnp.zeros((1, lanes), jnp.float32))

    def second_pass(r, totals):
        applied = _stiffen_row(scratch, r, gain_out[r])
        keep = (inside_ref[...] > 0.5) & (row_ref[r] > 0.5)
        applied = jnp.where(keep, applied, 0.0)
        applied_out[r] = applied
        inner = (inner_ref[...] > 0.5) & plan.inner_row(r)
        return totals + _row_sum(z_out[r] * applied, inner)

    za = lax.fori_loop(*plan.span(reach), second_pass, jnp.zeros((1, lanes), jnp.float32))
    dots_out[0:1, :] = zz
    dots_out[1:2, :] = za

    def observed_pass(r, carry):
        stiff_obs = _stiffen_row(observed_scr, plan.first_inner + r, gain_out[plan.first_inner + r])
        stiff_obs_out[pl.ds(r, 1), :] = _plane_row(stiff_obs, diagonal_ref[...] > 0.5)
        return carry

    lax.fori_loop(0, plan.inner_rows, observed_pass, 0)


def _start_kernel(plan, first_ref, z_ref, applied_ref, inner_ref, residual_out, rr_out):
    step = _ratio(first_ref, 0, first_ref, 1)

    def body(r, totals):
        residual = z_ref[r] - step * applied_ref[r]
        residual_out[r] = residual
        inner = (inner_ref[...] > 0.5) & plan.inner_row(r)
        return totals + _row_sum(residual * residual, inner)

    rr_out[...] = lax.fori_loop(
        *plan.span(2 * (ITERS - 1)), body, jnp.zeros((1, z_ref.shape[2]), jnp.float32)
    )


def _update_kernel(plan, reach, norm_ref, curvature_ref, residual_ref, applied_ref, inner_ref,
                   residual_out, rr_out):
    step = _ratio(norm_ref, 0, curvature_ref, 0)

    def body(r, totals):
        residual = residual_ref[r] - step * applied_ref[r]
        residual_out[r] = residual
        inner = (inner_ref[...] > 0.5) & plan.inner_row(r)
        return totals + _row_sum(residual * residual, inner)

    rr_out[...] = lax.fori_loop(
        *plan.span(reach), body, jnp.zeros((1, residual_ref.shape[2]), jnp.float32)
    )


def _direction_kernel(plan, reach, next_ref, now_ref, residual_ref, direction_ref, gain_ref,
                      weight_ref, inside_ref, row_ref, inner_ref, direction_out, applied_out, pa_out,
                      scratch):
    beta = _ratio(next_ref, 0, now_ref, 0)

    def new_direction(r, carry):
        direction_out[r] = residual_ref[r] + beta * direction_ref[r]
        return carry

    lax.fori_loop(*plan.span(reach + 2), new_direction, 0)
    pa_out[...] = _apply_q(plan, reach, direction_out, gain_ref, weight_ref, inside_ref, row_ref, inner_ref,
                           scratch, applied_out, direction_out)


def _final_kernel(plan, *refs):
    steps = ITERS
    ratio_refs = refs[: 2 * steps]
    direction_refs = refs[2 * steps : 3 * steps]
    (z_ref, stiff_ref, gain_ref, stiff_obs_ref, observed_ref, weight_ref, diagonal_ref,
     grad_kappa_out, grad_weight_out, scratch) = refs[3 * steps :]
    lanes = z_ref.shape[2]
    probes = lanes // 2
    step_lens = []
    for k in range(steps):
        num_ref, den_ref = ratio_refs[2 * k], ratio_refs[2 * k + 1]
        step_lens.append(_ratio(num_ref, 0, den_ref, 1 if k == 0 else 0))

    def new_solution(r, carry):
        solution = step_lens[0] * direction_refs[0][r]
        for k in range(1, steps):
            solution = solution + step_lens[k] * direction_refs[k][r]
        scratch[r] = solution
        return carry

    lax.fori_loop(*plan.span(1), new_solution, 0)

    def probe_sum(value, low):
        first = jnp.sum(jnp.where(low, value, 0.0), axis=1, keepdims=True)
        second = jnp.sum(jnp.where(low, 0.0, value), axis=1, keepdims=True)
        return jnp.where(low, first, second)

    def body(i, carry):
        r = plan.first_inner + i
        solution = scratch[r]
        stiff_solution = _stiffen_row(scratch, r, gain_ref[r])
        stiff_probe = stiff_ref[r]
        low = lax.broadcasted_iota(jnp.int32, solution.shape, 1) < probes
        diagonal = diagonal_ref[...] > 0.5
        weight_total = _plane_row(probe_sum(stiff_solution * stiff_probe, low), diagonal)
        kappa_total = _plane_row(
            probe_sum(solution * stiff_probe + stiff_solution * z_ref[r], low), diagonal
        )
        stiff_obs = stiff_obs_ref[pl.ds(i, 1), :]
        observed = observed_ref[pl.ds(i, 1), :]
        weight = weight_ref[pl.ds(i, 1), :]
        grad_weight_out[pl.ds(i, 1), :] = (
            0.5 * weight_total / probes - 0.5 * stiff_obs * stiff_obs
        )
        grad_kappa_out[pl.ds(i, 1), :] = (
            0.5 * weight * (kappa_total / probes) - observed * weight * stiff_obs
        )
        return carry

    lax.fori_loop(0, plan.inner_rows, body, 0)


def _vmem():
    return pl.BlockSpec(memory_space=pltpu.VMEM)


def _call(kernel, plan, inputs, out_shapes, scratch=0, smem=(), field=None):
    field = out_shapes[0] if field is None else field
    nbytes = 4 * field.shape[0] * field.shape[1] * field.shape[2]
    in_specs = [
        pl.BlockSpec(memory_space=pltpu.SMEM) if i in smem else _vmem() for i in range(len(inputs))
    ]
    return pl.pallas_call(
        lambda *refs: kernel(plan, *refs),
        out_shape=out_shapes,
        in_specs=in_specs,
        out_specs=tuple(_vmem() for _ in out_shapes),
        scratch_shapes=[pltpu.VMEM(field.shape, jnp.float32)] * scratch,
        cost_estimate=pl.CostEstimate(
            flops=40 * nbytes // 4,
            transcendentals=0,
            bytes_accessed=(len(inputs) + len(out_shapes)) * nbytes,
        ),
    )(*inputs)


def on_device(probes, observed, kappa_sq, variance_weight):
    probe_count, rows, cols = probes.shape
    half = cols // 2
    assert rows >= HALO and cols % 2 == 0 and half >= HALO and half == probe_count
    width = half + 2 * HALO
    sublanes = -(-width // 8) * 8
    slab_rows = rows + 2 * HALO
    lanes = 2 * probe_count
    stacked = jnp.concatenate(
        [probes, observed[None], kappa_sq[None], variance_weight[None]], axis=0
    )
    count = lax.axis_size("rows")
    sent = -(-HALO // 8) * 8
    assert sent <= rows
    planes = stacked.shape[0]
    fields = (probes, observed[None], kappa_sq[None], variance_weight[None])

    def edge_rows(start):
        rows_of = [lax.slice_in_dim(f, start, start + sent, axis=1) for f in fields]
        return jnp.concatenate(rows_of, axis=0).reshape(planes * sent, cols)

    below = lax.ppermute(
        edge_rows(rows - sent), "rows", [(i, i + 1) for i in range(count - 1)]
    ).reshape(planes, sent, cols)[:, sent - HALO :]
    above = lax.ppermute(
        edge_rows(0), "rows", [(i + 1, i) for i in range(count - 1)]
    ).reshape(planes, sent, cols)[:, :HALO]
    ext = jnp.concatenate(
        [jnp.transpose(piece, (1, 2, 0)) for piece in (below, stacked, above)], axis=0
    )
    ext = extended(ext, (("cols", 1),), HALO)
    ext = jnp.pad(
        ext, ((0, 0), (0, half + sublanes - ext.shape[1]), (0, lanes - ext.shape[2]))
    )

    row_at = lax.axis_index("rows") * rows - HALO + lax.iota(jnp.int32, slab_rows)
    row_in = ((row_at >= 0) & (row_at < rows * lax.axis_size("rows"))).astype(jnp.float32)
    col_in = []
    col_inner = []
    for h in range(2):
        at = lax.iota(jnp.int32, sublanes)
        col_at = lax.axis_index("cols") * cols - HALO + h * half + at
        col_in.append((col_at >= 0) & (col_at < cols * lax.axis_size("cols")) & (at < width))
        col_inner.append((at >= HALO) & (at < HALO + half))

    def on_lanes_of(columns):
        return jnp.concatenate(
            [jnp.broadcast_to(c[:, None], (sublanes, probe_count)) for c in columns], axis=1
        ).astype(jnp.float32)

    inside = on_lanes_of(col_in)
    inner = on_lanes_of(col_inner)
    lane_col = lax.iota(jnp.int32, lanes) % half + HALO
    diagonal = (lax.iota(jnp.int32, sublanes)[:, None] == lane_col[None, :]).astype(jnp.float32)
    plan = _Plan(slab_rows, HALO, rows, half)

    field = jax.ShapeDtypeStruct((slab_rows, sublanes, lanes), jnp.float32)
    lane_row = jax.ShapeDtypeStruct((1, lanes), jnp.float32)
    out_plane = jax.ShapeDtypeStruct((rows, cols), jnp.float32)

    z, gain, weight, stiff_probe, applied, first, stiff_obs = _call(
        _first_kernel, plan, (ext, inside, row_in, inner, diagonal),
        (field, field, field, field, field, jax.ShapeDtypeStruct((2, lanes), jnp.float32), out_plane),
        scratch=2, smem=(2,),
    )
    first = all_sum(first)
    residual, rr = _call(_start_kernel, plan, (first, z, applied, inner), (field, lane_row))
    directions = [z]
    ratios = [first, first]
    direction = z
    norm_now = first
    for iteration in range(1, ITERS):
        norm_next = all_sum(rr)
        reach = 2 * (ITERS - 1 - iteration)
        direction, applied, pa = _call(
            lambda plan, *refs, reach=reach: _direction_kernel(plan, reach, *refs), plan,
            (norm_next, norm_now, residual, direction, gain, weight, inside, row_in, inner),
            (field, field, lane_row), scratch=1, smem=(7,),
        )
        norm_now = norm_next
        curvature = all_sum(pa)
        directions.append(direction)
        ratios += [norm_now, curvature]
        if iteration + 1 < ITERS:
            residual, rr = _call(
                lambda plan, *refs, reach=reach: _update_kernel(plan, reach, *refs), plan, (norm_now, curvature, residual, applied, inner),
                (field, lane_row),
            )

    grad_kappa, grad_weight = _call(
        _final_kernel, plan,
        (*ratios, *directions, z, stiff_probe, gain, stiff_obs, observed, variance_weight, diagonal),
        (out_plane, out_plane), scratch=1, field=field,
    )
    return (grad_kappa, grad_weight)


def solution(mesh):
    placed = (P(None, "rows", "cols"), P("rows", "cols"), P("rows", "cols"), P("rows", "cols"))
    return jax.shard_map(
        on_device,
        mesh=mesh,
        in_specs=placed,
        out_specs=(P("rows", "cols"), P("rows", "cols")),
        check_vma=False,
    )
```

```python
import jax
import jax.numpy as jnp
from jax import lax
from jax.experimental import pallas as pl
from jax.experimental.pallas import tpu as pltpu
from jax.sharding import PartitionSpec as P

ITERS = 3
HALO = 2 * ITERS


def extended(cells, sides, width):
    for axis, dim in sides:
        count = lax.axis_size(axis)
        ends = count - 1
        head = lax.slice_in_dim(cells, 0, width, axis=dim)
        tail = lax.slice_in_dim(cells, cells.shape[dim] - width, cells.shape[dim], axis=dim)
        cells = jnp.concatenate(
            [
                lax.ppermute(tail, axis, [(i, (i + 1) % count) for i in range(ends)]),
                cells,
                lax.ppermute(head, axis, [((i + 1) % count, i) for i in range(ends)]),
            ],
            axis=dim,
        )
    return cells


def stencil(padded, kappa_sq):
    centre = padded[..., 1:-1, 1:-1]
    edge_sum = (
        padded[..., :-2, 1:-1]
        + padded[..., 2:, 1:-1]
        + padded[..., 1:-1, :-2]
        + padded[..., 1:-1, 2:]
    )
    corners = (
        padded[..., :-2, :-2] + padded[..., :-2, 2:] + padded[..., 2:, :-2] + padded[..., 2:, 2:]
    )
    return (kappa_sq + 20.0 / 6.0) * centre - (4.0 * edge_sum + corners) / 6.0


def stiffen(field, kappa_sq):
    pads = ((0, 0),) * (field.ndim - 2) + ((1, 1), (1, 1))
    return stencil(jnp.pad(field, pads), kappa_sq)


def _span_sum(terms, basis, partner):
    if not basis:
        return partner(0)
    *rest, top = basis
    return _span_sum(terms, rest, partner) + _span_sum(terms, rest, lambda m: partner(m ^ top))


def all_sum(terms):
    axes = ("rows", "cols")
    count = lax.axis_size("rows") * lax.axis_size("cols")
    if count & (count - 1):
        for axis in axes:
            terms = lax.psum(terms, axis)
        return terms
    bits = [1 << k for k in range(count.bit_length() - 1)]
    groups = [bits[:1]] + [bits[k : k + 2] for k in range(1, len(bits), 2)]
    for basis in groups:
        received = {}

        def partner(mask, terms=terms, received=received):
            if mask == 0:
                return terms
            if mask not in received:
                received[mask] = lax.ppermute(terms, axes, [(i, i ^ mask) for i in range(count)])
            return received[mask]

        terms = _span_sum(terms, basis, partner)
    return terms


def _stiffen_row(ref, r, gain):
    mid = ref[r]
    vertical = ref[r - 1] + ref[r + 1]
    n = mid.shape[0]
    edge_sum = vertical + pltpu.roll(mid, 1, 0) + pltpu.roll(mid, n - 1, 0)
    corners = pltpu.roll(vertical, 1, 0) + pltpu.roll(vertical, n - 1, 0)
    return gain * mid - (4.0 * edge_sum + corners) * (1.0 / 6.0)


def _total(ref, row):
    value = ref[row : row + 1, :]
    return value + pltpu.roll(value, value.shape[1] // 2, 1)


def _ratio(num_ref, num_row, den_ref, den_row):
    return _total(num_ref, num_row) / _total(den_ref, den_row)


def _row_sum(value, keep):
    return jnp.sum(jnp.where(keep, value, 0.0), axis=0, keepdims=True)


class _Plan:
    def __init__(self, slab_rows, first_inner, inner_rows, half):
        self.half = half
        self.slab_rows = slab_rows
        self.first_inner = first_inner
        self.inner_rows = inner_rows

    def span(self, halo):
        return self.first_inner - halo, self.first_inner + self.inner_rows + halo

    def inner_row(self, r):
        return (r >= self.first_inner) & (r < self.first_inner + self.inner_rows)


def _zero_edges(ref):
    ref[0] = jnp.zeros(ref.shape[1:], ref.dtype)
    ref[ref.shape[0] - 1] = jnp.zeros(ref.shape[1:], ref.dtype)


def _apply_q(plan, reach, source, gain_ref, weight_ref, inside_ref, row_ref, inner_ref, stiff_ref,
             applied_ref, dot_source):

    def first_pass(r, carry):
        stiff_ref[r] = weight_ref[r] * _stiffen_row(source, r, gain_ref[r])
        return carry

    lax.fori_loop(*plan.span(reach + 1), first_pass, 0)

    def second_pass(r, totals):
        applied = _stiffen_row(stiff_ref, r, gain_ref[r])
        keep = (inside_ref[...] > 0.5) & (row_ref[r] > 0.5)
        applied = jnp.where(keep, applied, 0.0)
        applied_ref[r] = applied
        inner = (inner_ref[...] > 0.5) & plan.inner_row(r)
        return totals + _row_sum(dot_source[r] * applied, inner)

    return lax.fori_loop(*plan.span(reach), second_pass, jnp.zeros((1, source.shape[2]), jnp.float32))


def _spread(value, lane):
    return jnp.broadcast_to(value[:, lane : lane + 1], value.shape)


def _plane_row(value, diagonal):
    return jnp.sum(jnp.where(diagonal, value, 0.0), axis=0, keepdims=True)


def _first_kernel(plan, ext_ref, inside_ref, row_ref, inner_ref, diagonal_ref,
                  z_out, gain_out, weight_out, stiff_out, applied_out, dots_out, stiff_obs_out,
                  observed_scr, scratch):
    sublanes = z_out.shape[1]
    lanes = z_out.shape[2]
    probes = lanes // 2

    def relayout(r, carry):
        cells = ext_ref[r]
        left = cells[0:sublanes]
        right = cells[plan.half : plan.half + sublanes]
        low = lax.broadcasted_iota(jnp.int32, (sublanes, lanes), 1) < probes
        z_out[r] = jnp.where(low, left, pltpu.roll(right, probes, 1))
        observed_scr[r] = jnp.where(low, _spread(left, probes), _spread(right, probes))
        gain_out[r] = jnp.where(low, _spread(left, probes + 1), _spread(right, probes + 1)) + 20.0 / 6.0
        weight_out[r] = jnp.where(low, _spread(left, probes + 2), _spread(right, probes + 2))
        return carry

    reach = 2 * (ITERS - 1)
    start, stop = plan.span(reach + 1)
    assert start >= 1 and stop == plan.slab_rows - 1
    lax.fori_loop(0, start + 1, relayout, 0)

    def probe_pass(r, totals):
        relayout(r + 1, 0)
        stiffness = _stiffen_row(z_out, r, gain_out[r])
        stiff_out[r] = stiffness
        scratch[r] = weight_out[r] * stiffness
        z = z_out[r]
        inner = (inner_ref[...] > 0.5) & plan.inner_row(r)
        return totals + _row_sum(z * z, inner)

    zz = lax.fori_loop(*plan.span(reach + 1), probe_pass, jnp.zeros((1, lanes), jnp.float32))

    def second_pass(r, totals):
        applied = _stiffen_row(scratch, r, gain_out[r])
        keep = (inside_ref[...] > 0.5) & (row_ref[r] > 0.5)
        applied = jnp.where(keep, applied, 0.0)
        applied_out[r] = applied
        inner = (inner_ref[...] > 0.5) & plan.inner_row(r)
        return totals + _row_sum(z_out[r] * applied, inner)

    za = lax.fori_loop(*plan.span(reach), second_pass, jnp.zeros((1, lanes), jnp.float32))
    dots_out[0:1, :] = zz
    dots_out[1:2, :] = za

    def observed_pass(r, carry):
        stiff_obs = _stiffen_row(observed_scr, plan.first_inner + r, gain_out[plan.first_inner + r])
        stiff_obs_out[pl.ds(r, 1), :] = _plane_row(stiff_obs, diagonal_ref[...] > 0.5)
        return carry

    lax.fori_loop(0, plan.inner_rows, observed_pass, 0)


def _start_kernel(plan, first_ref, z_ref, applied_ref, inner_ref, residual_out, rr_out):
    step = _ratio(first_ref, 0, first_ref, 1)

    def body(r, totals):
        residual = z_ref[r] - step * applied_ref[r]
        residual_out[r] = residual
        inner = (inner_ref[...] > 0.5) & plan.inner_row(r)
        return totals + _row_sum(residual * residual, inner)

    rr_out[...] = lax.fori_loop(
        *plan.span(2 * (ITERS - 1)), body, jnp.zeros((1, z_ref.shape[2]), jnp.float32)
    )


def _update_kernel(plan, reach, norm_ref, curvature_ref, residual_ref, applied_ref, inner_ref,
                   residual_out, rr_out):
    step = _ratio(norm_ref, 0, curvature_ref, 0)

    def body(r, totals):
        residual = residual_ref[r] - step * applied_ref[r]
        residual_out[r] = residual
        inner = (inner_ref[...] > 0.5) & plan.inner_row(r)
        return totals + _row_sum(residual * residual, inner)

    rr_out[...] = lax.fori_loop(
        *plan.span(reach), body, jnp.zeros((1, residual_ref.shape[2]), jnp.float32)
    )


def _direction_kernel(plan, reach, next_ref, now_ref, residual_ref, direction_ref, gain_ref,
                      weight_ref, inside_ref, row_ref, inner_ref, direction_out, applied_out, pa_out,
                      scratch):
    beta = _ratio(next_ref, 0, now_ref, 0)

    def new_direction(r, carry):
        direction_out[r] = residual_ref[r] + beta * direction_ref[r]
        return carry

    lax.fori_loop(*plan.span(reach + 2), new_direction, 0)
    pa_out[...] = _apply_q(plan, reach, direction_out, gain_ref, weight_ref, inside_ref, row_ref, inner_ref,
                           scratch, applied_out, direction_out)


def _final_kernel(plan, *refs):
    steps = ITERS
    ratio_refs = refs[: 2 * steps]
    direction_refs = refs[2 * steps : 3 * steps]
    (z_ref, stiff_ref, gain_ref, stiff_obs_ref, observed_ref, weight_ref, diagonal_ref,
     grad_kappa_out, grad_weight_out, scratch) = refs[3 * steps :]
    lanes = z_ref.shape[2]
    probes = lanes // 2
    step_lens = []
    for k in range(steps):
        num_ref, den_ref = ratio_refs[2 * k], ratio_refs[2 * k + 1]
        step_lens.append(_ratio(num_ref, 0, den_ref, 1 if k == 0 else 0))

    def new_solution(r, carry):
        solution = step_lens[0] * direction_refs[0][r]
        for k in range(1, steps):
            solution = solution + step_lens[k] * direction_refs[k][r]
        scratch[r] = solution
        return carry

    lax.fori_loop(*plan.span(1), new_solution, 0)

    def probe_sum(value, low):
        first = jnp.sum(jnp.where(low, value, 0.0), axis=1, keepdims=True)
        second = jnp.sum(jnp.where(low, 0.0, value), axis=1, keepdims=True)
        return jnp.where(low, first, second)

    def body(i, carry):
        r = plan.first_inner + i
        solution = scratch[r]
        stiff_solution = _stiffen_row(scratch, r, gain_ref[r])
        stiff_probe = stiff_ref[r]
        low = lax.broadcasted_iota(jnp.int32, solution.shape, 1) < probes
        diagonal = diagonal_ref[...] > 0.5
        weight_total = _plane_row(probe_sum(stiff_solution * stiff_probe, low), diagonal)
        kappa_total = _plane_row(
            probe_sum(solution * stiff_probe + stiff_solution * z_ref[r], low), diagonal
        )
        stiff_obs = stiff_obs_ref[pl.ds(i, 1), :]
        observed = observed_ref[pl.ds(i, 1), :]
        weight = weight_ref[pl.ds(i, 1), :]
        grad_weight_out[pl.ds(i, 1), :] = (
            0.5 * weight_total / probes - 0.5 * stiff_obs * stiff_obs
        )
        grad_kappa_out[pl.ds(i, 1), :] = (
            0.5 * weight * (kappa_total / probes) - observed * weight * stiff_obs
        )
        return carry

    lax.fori_loop(0, plan.inner_rows, body, 0)


def _vmem():
    return pl.BlockSpec(memory_space=pltpu.VMEM)


def _call(kernel, plan, inputs, out_shapes, scratch=0, smem=(), field=None):
    field = out_shapes[0] if field is None else field
    nbytes = 4 * field.shape[0] * field.shape[1] * field.shape[2]
    in_specs = [
        pl.BlockSpec(memory_space=pltpu.SMEM) if i in smem else _vmem() for i in range(len(inputs))
    ]
    return pl.pallas_call(
        lambda *refs: kernel(plan, *refs),
        out_shape=out_shapes,
        in_specs=in_specs,
        out_specs=tuple(_vmem() for _ in out_shapes),
        scratch_shapes=[pltpu.VMEM(field.shape, jnp.float32)] * scratch,
        cost_estimate=pl.CostEstimate(
            flops=40 * nbytes // 4,
            transcendentals=0,
            bytes_accessed=(len(inputs) + len(out_shapes)) * nbytes,
        ),
    )(*inputs)


def on_device(probes, observed, kappa_sq, variance_weight):
    probe_count, rows, cols = probes.shape
    half = cols // 2
    assert rows >= HALO and cols % 2 == 0 and half >= HALO and half == probe_count
    width = half + 2 * HALO
    sublanes = -(-width // 8) * 8
    slab_rows = rows + 2 * HALO
    lanes = 2 * probe_count
    stacked = jnp.concatenate(
        [probes, observed[None], kappa_sq[None], variance_weight[None]], axis=0
    )
    count = lax.axis_size("rows")
    sent = -(-HALO // 8) * 8
    assert sent <= rows
    planes = stacked.shape[0]
    fields = (probes, observed[None], kappa_sq[None], variance_weight[None])

    def edge_rows(start):
        rows_of = [lax.slice_in_dim(f, start, start + sent, axis=1) for f in fields]
        return jnp.concatenate(rows_of, axis=0).reshape(planes * sent, cols)

    below = lax.ppermute(
        edge_rows(rows - sent), "rows", [(i, i + 1) for i in range(count - 1)]
    ).reshape(planes, sent, cols)[:, sent - HALO :]
    above = lax.ppermute(
        edge_rows(0), "rows", [(i + 1, i) for i in range(count - 1)]
    ).reshape(planes, sent, cols)[:, :HALO]
    ext = jnp.concatenate(
        [jnp.transpose(piece, (1, 2, 0)) for piece in (below, stacked, above)], axis=0
    )
    ext = extended(ext, (("cols", 1),), HALO)
    ext = jnp.pad(
        ext, ((0, 0), (0, half + sublanes - ext.shape[1]), (0, lanes - ext.shape[2]))
    )

    row_at = lax.axis_index("rows") * rows - HALO + lax.iota(jnp.int32, slab_rows)
    row_in = ((row_at >= 0) & (row_at < rows * lax.axis_size("rows"))).astype(jnp.float32)
    col_in = []
    col_inner = []
    for h in range(2):
        at = lax.iota(jnp.int32, sublanes)
        col_at = lax.axis_index("cols") * cols - HALO + h * half + at
        col_in.append((col_at >= 0) & (col_at < cols * lax.axis_size("cols")) & (at < width))
        col_inner.append((at >= HALO) & (at < HALO + half))

    def on_lanes_of(columns):
        return jnp.concatenate(
            [jnp.broadcast_to(c[:, None], (sublanes, probe_count)) for c in columns], axis=1
        ).astype(jnp.float32)

    inside = on_lanes_of(col_in)
    inner = on_lanes_of(col_inner)
    lane_col = lax.iota(jnp.int32, lanes) % half + HALO
    diagonal = (lax.iota(jnp.int32, sublanes)[:, None] == lane_col[None, :]).astype(jnp.float32)
    plan = _Plan(slab_rows, HALO, rows, half)

    field = jax.ShapeDtypeStruct((slab_rows, sublanes, lanes), jnp.float32)
    lane_row = jax.ShapeDtypeStruct((1, lanes), jnp.float32)
    out_plane = jax.ShapeDtypeStruct((rows, cols), jnp.float32)

    z, gain, weight, stiff_probe, applied, first, stiff_obs = _call(
        _first_kernel, plan, (ext, inside, row_in, inner, diagonal),
        (field, field, field, field, field, jax.ShapeDtypeStruct((2, lanes), jnp.float32), out_plane),
        scratch=2, smem=(2,),
    )
    first = all_sum(first)
    residual, rr = _call(_start_kernel, plan, (first, z, applied, inner), (field, lane_row))
    directions = [z]
    ratios = [first, first]
    direction = z
    norm_now = first
    for iteration in range(1, ITERS):
        norm_next = all_sum(rr)
        reach = 2 * (ITERS - 1 - iteration)
        direction, applied, pa = _call(
            lambda plan, *refs, reach=reach: _direction_kernel(plan, reach, *refs), plan,
            (norm_next, norm_now, residual, direction, gain, weight, inside, row_in, inner),
            (field, field, lane_row), scratch=1, smem=(7,),
        )
        norm_now = norm_next
        curvature = all_sum(pa)
        directions.append(direction)
        ratios += [norm_now, curvature]
        if iteration + 1 < ITERS:
            residual, rr = _call(
                lambda plan, *refs, reach=reach: _update_kernel(plan, reach, *refs), plan, (norm_now, curvature, residual, applied, inner),
                (field, lane_row),
            )

    grad_kappa, grad_weight = _call(
        _final_kernel, plan,
        (*ratios, *directions, z, stiff_probe, gain, stiff_obs, observed, variance_weight, diagonal),
        (out_plane, out_plane), scratch=1, field=field,
    )
    return (grad_kappa, grad_weight)


def solution(mesh):
    placed = (P(None, "rows", "cols"), P("rows", "cols"), P("rows", "cols"), P("rows", "cols"))
    return jax.shard_map(
        on_device,
        mesh=mesh,
        in_specs=placed,
        out_specs=(P("rows", "cols"), P("rows", "cols")),
        check_vma=False,
    )
```

```python
import jax
import jax.numpy as jnp
from jax import lax
from jax.experimental import pallas as pl
from jax.experimental.pallas import tpu as pltpu
from jax.sharding import PartitionSpec as P

ITERS = 3
HALO = 2 * ITERS


def extended(cells, sides, width):
    for axis, dim in sides:
        count = lax.axis_size(axis)
        ends = count - 1
        head = lax.slice_in_dim(cells, 0, width, axis=dim)
        tail = lax.slice_in_dim(cells, cells.shape[dim] - width, cells.shape[dim], axis=dim)
        cells = jnp.concatenate(
            [
                lax.ppermute(tail, axis, [(i, (i + 1) % count) for i in range(ends)]),
                cells,
                lax.ppermute(head, axis, [((i + 1) % count, i) for i in range(ends)]),
            ],
            axis=dim,
        )
    return cells


def stencil(padded, kappa_sq):
    centre = padded[..., 1:-1, 1:-1]
    edge_sum = (
        padded[..., :-2, 1:-1]
        + padded[..., 2:, 1:-1]
        + padded[..., 1:-1, :-2]
        + padded[..., 1:-1, 2:]
    )
    corners = (
        padded[..., :-2, :-2] + padded[..., :-2, 2:] + padded[..., 2:, :-2] + padded[..., 2:, 2:]
    )
    return (kappa_sq + 20.0 / 6.0) * centre - (4.0 * edge_sum + corners) / 6.0


def stiffen(field, kappa_sq):
    pads = ((0, 0),) * (field.ndim - 2) + ((1, 1), (1, 1))
    return stencil(jnp.pad(field, pads), kappa_sq)


def _span_sum(terms, basis, partner):
    if not basis:
        return partner(0)
    *rest, top = basis
    return _span_sum(terms, rest, partner) + _span_sum(terms, rest, lambda m: partner(m ^ top))


def all_sum(terms):
    axes = ("rows", "cols")
    count = lax.axis_size("rows") * lax.axis_size("cols")
    if count & (count - 1):
        for axis in axes:
            terms = lax.psum(terms, axis)
        return terms
    bits = [1 << k for k in range(count.bit_length() - 1)]
    groups = [bits[:1]] + [bits[k : k + 2] for k in range(1, len(bits), 2)]
    for basis in groups:
        received = {}

        def partner(mask, terms=terms, received=received):
            if mask == 0:
                return terms
            if mask not in received:
                received[mask] = lax.ppermute(terms, axes, [(i, i ^ mask) for i in range(count)])
            return received[mask]

        terms = _span_sum(terms, basis, partner)
    return terms


def _stiffen_row(ref, r, gain):
    mid = ref[r]
    vertical = ref[r - 1] + ref[r + 1]
    n = mid.shape[0]
    edge_sum = vertical + pltpu.roll(mid, 1, 0) + pltpu.roll(mid, n - 1, 0)
    corners = pltpu.roll(vertical, 1, 0) + pltpu.roll(vertical, n - 1, 0)
    return gain * mid - (4.0 * edge_sum + corners) * (1.0 / 6.0)


def _total(ref, row):
    value = ref[row : row + 1, :]
    return value + pltpu.roll(value, value.shape[1] // 2, 1)


def _ratio(num_ref, num_row, den_ref, den_row):
    return _total(num_ref, num_row) / _total(den_ref, den_row)


def _row_sum(value, keep):
    return jnp.sum(jnp.where(keep, value, 0.0), axis=0, keepdims=True)


class _Plan:
    def __init__(self, slab_rows, first_inner, inner_rows, half):
        self.half = half
        self.slab_rows = slab_rows
        self.first_inner = first_inner
        self.inner_rows = inner_rows

    def span(self, halo):
        return self.first_inner - halo, self.first_inner + self.inner_rows + halo

    def inner_row(self, r):
        return (r >= self.first_inner) & (r < self.first_inner + self.inner_rows)


def _zero_edges(ref):
    ref[0] = jnp.zeros(ref.shape[1:], ref.dtype)
    ref[ref.shape[0] - 1] = jnp.zeros(ref.shape[1:], ref.dtype)


def _apply_q(plan, reach, source, gain_ref, weight_ref, inside_ref, row_ref, inner_ref, stiff_ref,
             applied_ref, dot_source, ahead=None):

    def first_pass(r, carry):
        if ahead is not None:
            ahead(r + 1, 0)
        stiff_ref[r] = weight_ref[r] * _stiffen_row(source, r, gain_ref[r])
        return carry

    lax.fori_loop(*plan.span(reach + 1), first_pass, 0)

    def second_pass(r, totals):
        applied = _stiffen_row(stiff_ref, r, gain_ref[r])
        keep = (inside_ref[...] > 0.5) & (row_ref[r] > 0.5)
        applied = jnp.where(keep, applied, 0.0)
        applied_ref[r] = applied
        inner = (inner_ref[...] > 0.5) & plan.inner_row(r)
        return totals + _row_sum(dot_source[r] * applied, inner)

    return lax.fori_loop(*plan.span(reach), second_pass, jnp.zeros((1, source.shape[2]), jnp.float32))


def _spread(value, lane):
    return jnp.broadcast_to(value[:, lane : lane + 1], value.shape)


def _plane_row(value, diagonal):
    return jnp.sum(jnp.where(diagonal, value, 0.0), axis=0, keepdims=True)


def _first_kernel(plan, ext_ref, inside_ref, row_ref, inner_ref, diagonal_ref,
                  z_out, gain_out, weight_out, stiff_out, applied_out, dots_out, stiff_obs_out,
                  observed_scr, scratch):
    sublanes = z_out.shape[1]
    lanes = z_out.shape[2]
    probes = lanes // 2

    def relayout(r, carry):
        cells = ext_ref[r]
        left = cells[0:sublanes]
        right = cells[plan.half : plan.half + sublanes]
        low = lax.broadcasted_iota(jnp.int32, (sublanes, lanes), 1) < probes
        z_out[r] = jnp.where(low, left, pltpu.roll(right, probes, 1))
        observed_scr[r] = jnp.where(low, _spread(left, probes), _spread(right, probes))
        gain_out[r] = jnp.where(low, _spread(left, probes + 1), _spread(right, probes + 1)) + 20.0 / 6.0
        weight_out[r] = jnp.where(low, _spread(left, probes + 2), _spread(right, probes + 2))
        return carry

    reach = 2 * (ITERS - 1)
    start, stop = plan.span(reach + 1)
    assert start >= 1 and stop == plan.slab_rows - 1
    lax.fori_loop(0, start + 1, relayout, 0)

    def probe_pass(r, totals):
        relayout(r + 1, 0)
        stiffness = _stiffen_row(z_out, r, gain_out[r])
        stiff_out[r] = stiffness
        scratch[r] = weight_out[r] * stiffness
        z = z_out[r]
        inner = (inner_ref[...] > 0.5) & plan.inner_row(r)
        return totals + _row_sum(z * z, inner)

    zz = lax.fori_loop(*plan.span(reach + 1), probe_pass, jnp.zeros((1, lanes), jnp.float32))

    def second_pass(r, totals):
        applied = _stiffen_row(scratch, r, gain_out[r])
        keep = (inside_ref[...] > 0.5) & (row_ref[r] > 0.5)
        applied = jnp.where(keep, applied, 0.0)
        applied_out[r] = applied
        inner = (inner_ref[...] > 0.5) & plan.inner_row(r)
        return totals + _row_sum(z_out[r] * applied, inner)

    za = lax.fori_loop(*plan.span(reach), second_pass, jnp.zeros((1, lanes), jnp.float32))
    dots_out[0:1, :] = zz
    dots_out[1:2, :] = za

    def observed_pass(r, carry):
        stiff_obs = _stiffen_row(observed_scr, plan.first_inner + r, gain_out[plan.first_inner + r])
        stiff_obs_out[pl.ds(r, 1), :] = _plane_row(stiff_obs, diagonal_ref[...] > 0.5)
        return carry

    lax.fori_loop(0, plan.inner_rows, observed_pass, 0)


def _start_kernel(plan, first_ref, z_ref, applied_ref, inner_ref, residual_out, rr_out):
    step = _ratio(first_ref, 0, first_ref, 1)

    def body(r, totals):
        residual = z_ref[r] - step * applied_ref[r]
        residual_out[r] = residual
        inner = (inner_ref[...] > 0.5) & plan.inner_row(r)
        return totals + _row_sum(residual * residual, inner)

    rr_out[...] = lax.fori_loop(
        *plan.span(2 * (ITERS - 1)), body, jnp.zeros((1, z_ref.shape[2]), jnp.float32)
    )


def _update_kernel(plan, reach, norm_ref, curvature_ref, residual_ref, applied_ref, inner_ref,
                   residual_out, rr_out):
    step = _ratio(norm_ref, 0, curvature_ref, 0)

    def body(r, totals):
        residual = residual_ref[r] - step * applied_ref[r]
        residual_out[r] = residual
        inner = (inner_ref[...] > 0.5) & plan.inner_row(r)
        return totals + _row_sum(residual * residual, inner)

    rr_out[...] = lax.fori_loop(
        *plan.span(reach), body, jnp.zeros((1, residual_ref.shape[2]), jnp.float32)
    )


def _direction_kernel(plan, reach, next_ref, now_ref, residual_ref, direction_ref, gain_ref,
                      weight_ref, inside_ref, row_ref, inner_ref, direction_out, applied_out, pa_out,
                      scratch):
    beta = _ratio(next_ref, 0, now_ref, 0)

    def new_direction(r, carry):
        direction_out[r] = residual_ref[r] + beta * direction_ref[r]
        return carry

    first, _ = plan.span(reach + 2)
    lax.fori_loop(first, first + 2, new_direction, 0)
    pa_out[...] = _apply_q(plan, reach, direction_out, gain_ref, weight_ref, inside_ref, row_ref, inner_ref,
                           scratch, applied_out, direction_out, ahead=new_direction)


def _final_kernel(plan, *refs):
    steps = ITERS
    ratio_refs = refs[: 2 * steps]
    direction_refs = refs[2 * steps : 3 * steps]
    (z_ref, stiff_ref, gain_ref, stiff_obs_ref, observed_ref, weight_ref, diagonal_ref,
     grad_kappa_out, grad_weight_out, scratch) = refs[3 * steps :]
    lanes = z_ref.shape[2]
    probes = lanes // 2
    step_lens = []
    for k in range(steps):
        num_ref, den_ref = ratio_refs[2 * k], ratio_refs[2 * k + 1]
        step_lens.append(_ratio(num_ref, 0, den_ref, 1 if k == 0 else 0))

    def new_solution(r, carry):
        solution = step_lens[0] * direction_refs[0][r]
        for k in range(1, steps):
            solution = solution + step_lens[k] * direction_refs[k][r]
        scratch[r] = solution
        return carry

    lax.fori_loop(*plan.span(1), new_solution, 0)

    def probe_sum(value, low):
        first = jnp.sum(jnp.where(low, value, 0.0), axis=1, keepdims=True)
        second = jnp.sum(jnp.where(low, 0.0, value), axis=1, keepdims=True)
        return jnp.where(low, first, second)

    def body(i, carry):
        r = plan.first_inner + i
        solution = scratch[r]
        stiff_solution = _stiffen_row(scratch, r, gain_ref[r])
        stiff_probe = stiff_ref[r]
        low = lax.broadcasted_iota(jnp.int32, solution.shape, 1) < probes
        diagonal = diagonal_ref[...] > 0.5
        weight_total = _plane_row(probe_sum(stiff_solution * stiff_probe, low), diagonal)
        kappa_total = _plane_row(
            probe_sum(solution * stiff_probe + stiff_solution * z_ref[r], low), diagonal
        )
        stiff_obs = stiff_obs_ref[pl.ds(i, 1), :]
        observed = observed_ref[pl.ds(i, 1), :]
        weight = weight_ref[pl.ds(i, 1), :]
        grad_weight_out[pl.ds(i, 1), :] = (
            0.5 * weight_total / probes - 0.5 * stiff_obs * stiff_obs
        )
        grad_kappa_out[pl.ds(i, 1), :] = (
            0.5 * weight * (kappa_total / probes) - observed * weight * stiff_obs
        )
        return carry

    lax.fori_loop(0, plan.inner_rows, body, 0)


def _vmem():
    return pl.BlockSpec(memory_space=pltpu.VMEM)


def _call(kernel, plan, inputs, out_shapes, scratch=0, smem=(), field=None):
    field = out_shapes[0] if field is None else field
    nbytes = 4 * field.shape[0] * field.shape[1] * field.shape[2]
    in_specs = [
        pl.BlockSpec(memory_space=pltpu.SMEM) if i in smem else _vmem() for i in range(len(inputs))
    ]
    return pl.pallas_call(
        lambda *refs: kernel(plan, *refs),
        out_shape=out_shapes,
        in_specs=in_specs,
        out_specs=tuple(_vmem() for _ in out_shapes),
        scratch_shapes=[pltpu.VMEM(field.shape, jnp.float32)] * scratch,
        cost_estimate=pl.CostEstimate(
            flops=40 * nbytes // 4,
            transcendentals=0,
            bytes_accessed=(len(inputs) + len(out_shapes)) * nbytes,
        ),
    )(*inputs)


def on_device(probes, observed, kappa_sq, variance_weight):
    probe_count, rows, cols = probes.shape
    half = cols // 2
    assert rows >= HALO and cols % 2 == 0 and half >= HALO and half == probe_count
    width = half + 2 * HALO
    sublanes = -(-width // 8) * 8
    slab_rows = rows + 2 * HALO
    lanes = 2 * probe_count
    stacked = jnp.concatenate(
        [probes, observed[None], kappa_sq[None], variance_weight[None]], axis=0
    )
    count = lax.axis_size("rows")
    sent = -(-HALO // 8) * 8
    assert sent <= rows
    planes = stacked.shape[0]
    fields = (probes, observed[None], kappa_sq[None], variance_weight[None])

    def edge_rows(start):
        rows_of = [lax.slice_in_dim(f, start, start + sent, axis=1) for f in fields]
        return jnp.concatenate(rows_of, axis=0).reshape(planes * sent, cols)

    below = lax.ppermute(
        edge_rows(rows - sent), "rows", [(i, i + 1) for i in range(count - 1)]
    ).reshape(planes, sent, cols)[:, sent - HALO :]
    above = lax.ppermute(
        edge_rows(0), "rows", [(i + 1, i) for i in range(count - 1)]
    ).reshape(planes, sent, cols)[:, :HALO]
    ext = jnp.concatenate(
        [jnp.transpose(piece, (1, 2, 0)) for piece in (below, stacked, above)], axis=0
    )
    ext = extended(ext, (("cols", 1),), HALO)
    ext = jnp.pad(
        ext, ((0, 0), (0, half + sublanes - ext.shape[1]), (0, lanes - ext.shape[2]))
    )

    row_at = lax.axis_index("rows") * rows - HALO + lax.iota(jnp.int32, slab_rows)
    row_in = ((row_at >= 0) & (row_at < rows * lax.axis_size("rows"))).astype(jnp.float32)
    col_in = []
    col_inner = []
    for h in range(2):
        at = lax.iota(jnp.int32, sublanes)
        col_at = lax.axis_index("cols") * cols - HALO + h * half + at
        col_in.append((col_at >= 0) & (col_at < cols * lax.axis_size("cols")) & (at < width))
        col_inner.append((at >= HALO) & (at < HALO + half))

    def on_lanes_of(columns):
        return jnp.concatenate(
            [jnp.broadcast_to(c[:, None], (sublanes, probe_count)) for c in columns], axis=1
        ).astype(jnp.float32)

    inside = on_lanes_of(col_in)
    inner = on_lanes_of(col_inner)
    lane_col = lax.iota(jnp.int32, lanes) % half + HALO
    diagonal = (lax.iota(jnp.int32, sublanes)[:, None] == lane_col[None, :]).astype(jnp.float32)
    plan = _Plan(slab_rows, HALO, rows, half)

    field = jax.ShapeDtypeStruct((slab_rows, sublanes, lanes), jnp.float32)
    lane_row = jax.ShapeDtypeStruct((1, lanes), jnp.float32)
    out_plane = jax.ShapeDtypeStruct((rows, cols), jnp.float32)

    z, gain, weight, stiff_probe, applied, first, stiff_obs = _call(
        _first_kernel, plan, (ext, inside, row_in, inner, diagonal),
        (field, field, field, field, field, jax.ShapeDtypeStruct((2, lanes), jnp.float32), out_plane),
        scratch=2, smem=(2,),
    )
    first = all_sum(first)
    residual, rr = _call(_start_kernel, plan, (first, z, applied, inner), (field, lane_row))
    directions = [z]
    ratios = [first, first]
    direction = z
    norm_now = first
    for iteration in range(1, ITERS):
        norm_next = all_sum(rr)
        reach = 2 * (ITERS - 1 - iteration)
        direction, applied, pa = _call(
            lambda plan, *refs, reach=reach: _direction_kernel(plan, reach, *refs), plan,
            (norm_next, norm_now, residual, direction, gain, weight, inside, row_in, inner),
            (field, field, lane_row), scratch=1, smem=(7,),
        )
        norm_now = norm_next
        curvature = all_sum(pa)
        directions.append(direction)
        ratios += [norm_now, curvature]
        if iteration + 1 < ITERS:
            residual, rr = _call(
                lambda plan, *refs, reach=reach: _update_kernel(plan, reach, *refs), plan, (norm_now, curvature, residual, applied, inner),
                (field, lane_row),
            )

    grad_kappa, grad_weight = _call(
        _final_kernel, plan,
        (*ratios, *directions, z, stiff_probe, gain, stiff_obs, observed, variance_weight, diagonal),
        (out_plane, out_plane), scratch=1, field=field,
    )
    return (grad_kappa, grad_weight)


def solution(mesh):
    placed = (P(None, "rows", "cols"), P("rows", "cols"), P("rows", "cols"), P("rows", "cols"))
    return jax.shard_map(
        on_device,
        mesh=mesh,
        in_specs=placed,
        out_specs=(P("rows", "cols"), P("rows", "cols")),
        check_vma=False,
    )
```
